256 devices in a mesh: dp: 4 (over x), seq: 4 (over y_hi, core), tensor: 16 (over y_lo, z).
Axes of the slice: x: 4, y: 4 (y_hi: 2, y_lo: 2; y = y_hi * 2 + y_lo), z: 8, core: 2. Of those that a mesh axis runs over, the one named last changes fastest.
Arguments:
- byte_acts: bfloat16 [4, 16384, 2048], P('dp', 'seq', 'tensor'), may hold values from -18 to 18
- conv_weight: bfloat16 [16, 1024, 128], P('tensor'), may hold values from -0.1875 to 0.1875
- conv_bias: float32 [2048], P('tensor'), may hold values from -3 to 3
- proj_weight: bfloat16 [2048, 8192], P(None, 'tensor'), may hold values from -0.125 to 0.125
- teacher: bfloat16 [4, 4096, 8192], P('dp', 'seq', 'tensor'), may hold values from -6 to 6
- span_lengths: int32 [4, 4096], P('dp'), may hold values from 1 to 16, as said below
Outputs:
- downsampled: bfloat16 [4, 4096, 2048], P('dp', 'seq', 'tensor')
- byte_grad: bfloat16 [4, 16384, 2048], P('dp', 'seq', 'tensor')
- conv_grad: float32 [16, 1024, 128], P('tensor')
- proj_grad: float32 [2048, 8192], P(None, 'tensor')
The draws below stay inside these ranges and needn't reach their ends.
Inputs may be any that keep to these rules, and one draw needn't show every extreme that they name: `span_lengths`: each document's 4096 span lengths cover its 16384 bytes in order; the longest is exactly 16.
All inputs are finite; a program needn't handle non-finite values.
Results may differ from the reference program's by a relative error of at most 0.019.
Values may be sent and summed in bfloat16 or wider, within the bound.
No kernel may reach another device: no remote copies, remote signals or barrier semaphores. Data moves between devices by JAX's collectives and lax.ppermute only.
A program may use at most 64 MiB of HBM per device.

```python
import jax
import jax.numpy as jnp
from jax import lax

D = 2048
TD = 8192
GROUPS = 16
STRIDE = 4
KERNEL = 8
MOST_SPAN = 16
GW = 128
TD_DEV = 512
DOCS = 4
SEQ_BYTES = 16384
POSITIONS = 4096
TOKENS = 4096


def draw_span_lengths(key, part):
    slot_tokens = TOKENS // 8
    key_long, key_cut, key_flip = jax.random.split(jax.random.fold_in(key, 7101), 3)
    long_len = jax.random.randint(key_long, (DOCS, 2, slot_tokens), 8, 14).astype(jnp.int32)
    long_len = long_len.at[:, 0, 0].set(MOST_SPAN).at[:, 1, 0].set(8)
    spare_bytes = 2 * MOST_SPAN - long_len[:, 0] - long_len[:, 1] - 6
    cut_points = jax.random.randint(key_cut, (DOCS, 5, slot_tokens), 0, 11).astype(jnp.int32)
    cut_points = jnp.minimum(cut_points, spare_bytes[:, None, :])
    cut_points = jnp.sort(cut_points, axis=1)
    edge_points = jnp.concatenate([jnp.zeros((DOCS, 1, slot_tokens), jnp.int32), cut_points, spare_bytes[:, None, :]], axis=1)
    short_len = 1 + edge_points[:, 1:] - edge_points[:, :-1]
    values = jnp.concatenate([long_len, short_len], axis=1)
    flip_bits = (jax.random.randint(key_flip, (), 0, 2) + jnp.arange(DOCS, dtype=jnp.int32)) % 2
    arranged = jnp.where(flip_bits[:, None, None] == 1, values[:, ::-1], values)
    return arranged.reshape(DOCS, TOKENS).astype(jnp.int32)


def draw_byte_acts(key, part):
    key_pair, key_value = jax.random.split(jax.random.fold_in(key, 5303), 2)
    pairing = jax.random.permutation(key_pair, DOCS).astype(jnp.int32)
    group_of = jnp.arange(D, dtype=jnp.int32) // GW % DOCS
    heavy = (group_of[None, :] == pairing[:, None]).astype(jnp.float32)
    factor = 1.0 + 2.0 * heavy
    base = jnp.clip(jax.random.normal(key_value, (DOCS, SEQ_BYTES, D), jnp.float32), -6.0, 6.0)
    return (base * factor[:, None, :]).astype(jnp.bfloat16)


def levels(own_key, shape, cuts, least, high):
    loudness = 1.0
    for dim, shards_of in cuts:
        heights = jax.random.uniform(jax.random.fold_in(jax.random.fold_in(own_key, 6), dim), (shards_of,), jnp.float32, least / len(cuts), high / len(cuts))
        loudness = loudness * jnp.repeat(jnp.exp(heights), shape[dim] // shards_of).reshape((-1,) + (1,) * (len(shape) - 1 - dim))
    return loudness


def scatter_about(own_key, extent, deviation, reach, cuts=(), held_as=jnp.bfloat16):
    entries = deviation * jax.random.normal(own_key, extent, jnp.float32)
    if cuts:
        entries = entries * levels(own_key, extent, cuts, -0.22, 0.18)
    return jnp.clip(entries, -reach, reach).astype(held_as)


def setup_inputs(seed: int = 0) -> dict:
    keys = jax.random.split(jax.random.key(seed), 7)
    byte_acts = draw_byte_acts(jax.random.fold_in(keys[6], 71), 0)
    conv_weight = scatter_about(keys[1], (GROUPS, KERNEL * GW, GW), (KERNEL * GW) ** -0.5, 0.1875, ((0, 16),))
    conv_bias = scatter_about(keys[2], (D,), 0.5, 3.0, ((0, 16),), jnp.float32)
    proj_weight = scatter_about(keys[3], (D, TD), D ** -0.5, 0.125, ((1, 16),))
    teacher = scatter_about(keys[4], (DOCS, TOKENS, TD), 1.0, 6.0, ((0, 4), (1, 4), (2, 16)))
    span_lengths = draw_span_lengths(jax.random.fold_in(keys[6], 71), 0)
    return dict(byte_acts=byte_acts, conv_weight=conv_weight, conv_bias=conv_bias, proj_weight=proj_weight, teacher=teacher, span_lengths=span_lengths)


def intersection_weights(span_start, span_end, span_lengths, first_position, position_count):
    byte_first = (first_position + jnp.arange(position_count, dtype=jnp.int32)) * STRIDE
    lower_edge = jnp.maximum(span_start[:, None], byte_first[None, :])
    upper_edge = jnp.minimum(span_end[:, None], byte_first[None, :] + STRIDE)
    covered = jnp.maximum(upper_edge - lower_edge, 0).astype(jnp.float32)
    return (covered / span_lengths[:, None].astype(jnp.float32)).astype(jnp.bfloat16)

def blockwise_back(err_grad, proj_weight):
    total = jnp.zeros((TOKENS, D), jnp.float32)
    for shard_index in range(TD // TD_DEV):
        err_part = err_grad[:, shard_index * TD_DEV:(shard_index + 1) * TD_DEV]
        weight_part = proj_weight[:, shard_index * TD_DEV:(shard_index + 1) * TD_DEV]
        partial_term = lax.dot_general(err_part, weight_part, (((1,), (1,)), ((), ())), preferred_element_type=jnp.float32)
        rounded = lax.optimization_barrier(partial_term.astype(jnp.bfloat16))
        total = total + rounded.astype(jnp.float32)
    return total.astype(jnp.bfloat16)

def reference(byte_acts, conv_weight, conv_bias, proj_weight, teacher, span_lengths):
    taps_weight = conv_weight.astype(jnp.float32).reshape(GROUPS, KERNEL, GW, GW)
    bias_groups = conv_bias.reshape(GROUPS, GW)
    proj_total = jnp.zeros((D, TD), jnp.float32)
    conv_total = jnp.zeros((GROUPS, KERNEL, GW, GW), jnp.float32)
    down_list = []
    grad_list = []
    for doc_index in range(DOCS):
        lengths_doc = span_lengths[doc_index].astype(jnp.int32)
        span_end = jnp.cumsum(lengths_doc).astype(jnp.int32)
        span_start = (span_end - lengths_doc).astype(jnp.int32)
        pool_weight = intersection_weights(span_start, span_end, lengths_doc, 0, POSITIONS)
        extended = jnp.concatenate([byte_acts[doc_index], jnp.zeros((STRIDE, D), byte_acts.dtype)], axis=0)
        blocks = extended.reshape(POSITIONS + 1, STRIDE, GROUPS, GW).astype(jnp.float32)
        windows = jnp.concatenate([blocks[:-1], blocks[1:]], axis=1)
        conv_out = jnp.einsum('pkgc,gkco->pgo', windows, taps_weight) + bias_groups[None]
        downsampled = conv_out.reshape(POSITIONS, D).astype(jnp.bfloat16)
        pooled = jnp.dot(pool_weight, downsampled, preferred_element_type=jnp.float32).astype(jnp.bfloat16)
        predicted = jnp.dot(pooled, proj_weight, preferred_element_type=jnp.float32)
        err_grad = (predicted - teacher[doc_index].astype(jnp.float32)).astype(jnp.bfloat16)
        proj_total = proj_total + jnp.dot(pooled.T, err_grad, preferred_element_type=jnp.float32)
        pooled_grad = blockwise_back(err_grad, proj_weight)
        down_grad = jnp.dot(pool_weight.T, pooled_grad, preferred_element_type=jnp.float32).astype(jnp.bfloat16)
        grad_groups = down_grad.astype(jnp.float32).reshape(POSITIONS, GROUPS, GW)
        conv_total = conv_total + jnp.einsum('pkgc,pgo->gkco', windows, grad_groups)
        window_grad = jnp.einsum('pgo,gkco->pkgc', grad_groups, taps_weight)
        block_grad = window_grad[:, :STRIDE]
        carried = jnp.concatenate([jnp.zeros((1, STRIDE, GROUPS, GW), jnp.float32), window_grad[:-1, STRIDE:]], axis=0)
        byte_doc = (block_grad + carried).reshape(SEQ_BYTES, D).astype(jnp.bfloat16)
        down_list.append(downsampled)
        grad_list.append(byte_doc)
    proj_grad = proj_total / jnp.sqrt(jnp.float32(DOCS * TOKENS))
    conv_grad = (conv_total / jnp.sqrt(jnp.float32(DOCS * POSITIONS))).reshape(GROUPS, KERNEL * GW, GW)
    return (jnp.stack(down_list), jnp.stack(grad_list), conv_grad, proj_grad)
```

```python
import jax
import jax.numpy as jnp
from jax import lax
from jax.sharding import PartitionSpec as P

STRIDE = 4
KERNEL = 8


def shifted(block, axis, distance):
    devices = range(lax.axis_size(axis))
    route = [(i - distance, i) for i in devices if i - distance in devices]
    return lax.ppermute(block, axis, route)


def shard_sum(block, axis):
    count = lax.axis_size(axis)
    rank = lax.axis_index(axis)
    pieces = block.reshape((count, block.shape[0] // count) + block.shape[1:])
    total = lax.dynamic_index_in_dim(pieces, rank, 0, keepdims=False).astype(jnp.float32)
    for distance in range(1, count):
        route = [(i, (i + distance) % count) for i in range(count)]
        outgoing = lax.dynamic_index_in_dim(pieces, (rank + distance) % count, 0, keepdims=False)
        total = total + lax.ppermute(outgoing, axis, route).astype(jnp.float32)
    return total


def shard_gather(piece, axis):
    count = lax.axis_size(axis)
    rank = lax.axis_index(axis)
    received = [piece]
    for distance in range(1, count):
        route = [(i, (i + distance) % count) for i in range(count)]
        received.append(lax.ppermute(piece, axis, route))
    stacked = jnp.stack(received[::-1])
    ordered = jnp.roll(stacked, rank + 1, axis=0)
    return ordered.reshape((count * piece.shape[0],) + piece.shape[1:])


def permute_psum(block, axes):
    summed = block
    for axis in axes:
        summed = shard_sum(summed, axis).astype(block.dtype)
    for axis in axes[::-1]:
        summed = shard_gather(summed, axis)
    return summed


def intersection_weights(span_start, span_end, span_lengths, first_position, position_count):
    byte_first = (first_position + jnp.arange(position_count, dtype=jnp.int32)) * STRIDE
    lower_edge = jnp.maximum(span_start[:, None], byte_first[None, :])
    upper_edge = jnp.minimum(span_end[:, None], byte_first[None, :] + STRIDE)
    covered = jnp.maximum(upper_edge - lower_edge, 0).astype(jnp.float32)
    return (covered / span_lengths[:, None].astype(jnp.float32)).astype(jnp.bfloat16)


def local(byte_acts, conv_weight, conv_bias, proj_weight, teacher, span_lengths):
    byte_rows = byte_acts[0]
    row_total, width = byte_rows.shape
    groups_here = conv_weight.shape[0]
    group_width = width // groups_here
    positions = row_total // STRIDE
    seq_count = lax.axis_size("seq")
    seq_rank = lax.axis_index("seq")
    lengths_doc = span_lengths[0]
    tokens_all = lengths_doc.shape[0]
    span_end = jnp.cumsum(lengths_doc)
    span_start = span_end - lengths_doc
    next_rows = shifted(byte_rows[:STRIDE], "seq", -1)
    extended = jnp.concatenate([byte_rows, next_rows], axis=0)
    blocks = extended.reshape(positions + 1, STRIDE, groups_here, group_width)
    windows = jnp.concatenate([blocks[:-1], blocks[1:]], axis=1)
    taps_weight = conv_weight.reshape(groups_here, KERNEL, group_width, group_width)
    conv_out = jnp.einsum(
        "pkgc,gkco->pgo", windows, taps_weight, preferred_element_type=jnp.float32
    )
    conv_out = conv_out + conv_bias.reshape(groups_here, group_width)[None]
    downsampled = conv_out.reshape(positions, width).astype(jnp.bfloat16)
    local_weight = intersection_weights(
        span_start, span_end, lengths_doc, seq_rank * positions, positions
    )
    tokens_here = tokens_all // seq_count
    own_start = lax.dynamic_slice_in_dim(span_start, seq_rank * tokens_here, tokens_here)
    own_end = lax.dynamic_slice_in_dim(span_end, seq_rank * tokens_here, tokens_here)
    own_lengths = lax.dynamic_slice_in_dim(lengths_doc, seq_rank * tokens_here, tokens_here)
    token_weight = intersection_weights(own_start, own_end, own_lengths, 0, positions * seq_count)
    down_all = lax.all_gather(downsampled, "seq", axis=0, tiled=True)
    pooled_sum = jnp.dot(token_weight, down_all, preferred_element_type=jnp.float32).astype(
        jnp.bfloat16
    )
    gathered = lax.all_gather(pooled_sum, "tensor", axis=1, tiled=True)
    predicted = jnp.dot(gathered, proj_weight, preferred_element_type=jnp.float32)
    err_grad = (predicted - teacher[0].astype(jnp.float32)).astype(jnp.bfloat16)
    proj_local = lax.dot_general(
        gathered, err_grad, (((0,), (0,)), ((), ())), preferred_element_type=jnp.float32
    )
    token_scale = 1.0 / jnp.sqrt(jnp.float32(lax.axis_size("dp") * tokens_all))
    proj_summed = permute_psum(proj_local.astype(jnp.bfloat16), ("dp", "seq")).astype(jnp.float32)
    proj_grad = proj_summed * token_scale
    weight_part = proj_weight
    pooled_grad_t = lax.psum_scatter(
        lax.dot_general(
            weight_part, err_grad, (((1,), (1,)), ((), ())), preferred_element_type=jnp.float32
        ).astype(jnp.bfloat16),
        "tensor",
        scatter_dimension=0,
        tiled=True,
    )
    weight_part = local_weight
    down_sum = lax.dot_general(
        weight_part,
        lax.all_gather(pooled_grad_t, "seq", axis=1, tiled=True),
        (((0,), (1,)), ((), ())),
        preferred_element_type=jnp.float32,
    )
    down_grad = down_sum.astype(jnp.bfloat16).reshape(positions, groups_here, group_width)
    conv_local = jnp.einsum(
        "pkgc,pgo->gkco", windows, down_grad, preferred_element_type=jnp.float32
    )
    conv_summed = lax.psum(conv_local.astype(jnp.bfloat16), ("dp", "seq")).astype(jnp.float32)
    position_scale = 1.0 / jnp.sqrt(jnp.float32(lax.axis_size("dp") * positions * seq_count))
    conv_grad = (conv_summed * position_scale).reshape(
        groups_here, KERNEL * group_width, group_width
    )
    window_grad = jnp.einsum(
        "pgo,gkco->pkgc", down_grad, taps_weight, preferred_element_type=jnp.float32
    )
    incoming = shifted(window_grad[-1, STRIDE:], "seq", 1)
    carried_grad = jnp.concatenate([incoming[None], window_grad[:-1, STRIDE:]], axis=0)
    byte_grad = (
        (window_grad[:, :STRIDE] + carried_grad).reshape(row_total, width).astype(jnp.bfloat16)
    )
    return (downsampled[None], byte_grad[None], conv_grad, proj_grad)


def solution(mesh):
    return jax.shard_map(
        local,
        mesh=mesh,
        in_specs=(
            P("dp", "seq", "tensor"),
            P("tensor", None, None),
            P("tensor"),
            P(None, "tensor"),
            P("dp", "seq", "tensor"),
            P("dp", None),
        ),
        out_specs=(
            P("dp", "seq", "tensor"),
            P("dp", "seq", "tensor"),
            P("tensor", None, None),
            P(None, "tensor"),
        ),
        check_vma=False,
    )
```

```python
import jax
import jax.numpy as jnp
from jax import lax
from jax.sharding import PartitionSpec as P

STRIDE = 4
KERNEL = 8


def shifted(block, axis, distance):
    devices = range(lax.axis_size(axis))
    route = [(i - distance, i) for i in devices if i - distance in devices]
    return lax.ppermute(block, axis, route)


def shard_sum(block, axis):
    count = lax.axis_size(axis)
    rank = lax.axis_index(axis)
    pieces = block.reshape((count, block.shape[0] // count) + block.shape[1:])
    total = lax.dynamic_index_in_dim(pieces, rank, 0, keepdims=False).astype(jnp.float32)
    for distance in range(1, count):
        route = [(i, (i + distance) % count) for i in range(count)]
        outgoing = lax.dynamic_index_in_dim(pieces, (rank + distance) % count, 0, keepdims=False)
        total = total + lax.ppermute(outgoing, axis, route).astype(jnp.float32)
    return total


def shard_gather(piece, axis):
    count = lax.axis_size(axis)
    rank = lax.axis_index(axis)
    rows = piece.shape[0]
    gathered = jnp.zeros((count * rows,) + piece.shape[1:], piece.dtype)
    gathered = lax.dynamic_update_slice_in_dim(gathered, piece, rank * rows, 0)
    for distance in range(1, count):
        route = [(i, (i + distance) % count) for i in range(count)]
        incoming = lax.ppermute(piece, axis, route)
        source = (rank + count - distance) % count
        gathered = lax.dynamic_update_slice_in_dim(gathered, incoming, source * rows, 0)
    return gathered


def permute_psum(block, axes):
    summed = block
    for axis in axes:
        summed = shard_sum(summed, axis).astype(block.dtype)
    for axis in axes[::-1]:
        summed = shard_gather(summed, axis)
    return summed


def intersection_weights(span_start, span_end, span_lengths, first_position, position_count):
    byte_first = (first_position + jnp.arange(position_count, dtype=jnp.int32)) * STRIDE
    lower_edge = jnp.maximum(span_start[:, None], byte_first[None, :])
    upper_edge = jnp.minimum(span_end[:, None], byte_first[None, :] + STRIDE)
    covered = jnp.maximum(upper_edge - lower_edge, 0).astype(jnp.float32)
    return (covered / span_lengths[:, None].astype(jnp.float32)).astype(jnp.bfloat16)


def local(byte_acts, conv_weight, conv_bias, proj_weight, teacher, span_lengths):
    byte_rows = byte_acts[0]
    row_total, width = byte_rows.shape
    groups_here = conv_weight.shape[0]
    group_width = width // groups_here
    positions = row_total // STRIDE
    seq_count = lax.axis_size("seq")
    seq_rank = lax.axis_index("seq")
    lengths_doc = span_lengths[0]
    tokens_all = lengths_doc.shape[0]
    span_end = jnp.cumsum(lengths_doc)
    span_start = span_end - lengths_doc
    next_rows = shifted(byte_rows[:STRIDE], "seq", -1)
    extended = jnp.concatenate([byte_rows, next_rows], axis=0)
    blocks = extended.reshape(positions + 1, STRIDE, groups_here, group_width)
    windows = jnp.concatenate([blocks[:-1], blocks[1:]], axis=1)
    taps_weight = conv_weight.reshape(groups_here, KERNEL, group_width, group_width)
    conv_out = jnp.einsum(
        "pkgc,gkco->pgo", windows, taps_weight, preferred_element_type=jnp.float32
    )
    conv_out = conv_out + conv_bias.reshape(groups_here, group_width)[None]
    downsampled = conv_out.reshape(positions, width).astype(jnp.bfloat16)
    local_weight = intersection_weights(
        span_start, span_end, lengths_doc, seq_rank * positions, positions
    )
    tokens_here = tokens_all // seq_count
    own_start = lax.dynamic_slice_in_dim(span_start, seq_rank * tokens_here, tokens_here)
    own_end = lax.dynamic_slice_in_dim(span_end, seq_rank * tokens_here, tokens_here)
    own_lengths = lax.dynamic_slice_in_dim(lengths_doc, seq_rank * tokens_here, tokens_here)
    token_weight = intersection_weights(own_start, own_end, own_lengths, 0, positions * seq_count)
    down_all = lax.all_gather(downsampled, "seq", axis=0, tiled=True)
    pooled_sum = jnp.dot(token_weight, down_all, preferred_element_type=jnp.float32).astype(
        jnp.bfloat16
    )
    gathered = lax.all_gather(pooled_sum, "tensor", axis=1, tiled=True)
    predicted = jnp.dot(gathered, proj_weight, preferred_element_type=jnp.float32)
    err_grad = (predicted - teacher[0].astype(jnp.float32)).astype(jnp.bfloat16)
    proj_local = lax.dot_general(
        gathered, err_grad, (((0,), (0,)), ((), ())), preferred_element_type=jnp.float32
    )
    token_scale = 1.0 / jnp.sqrt(jnp.float32(lax.axis_size("dp") * tokens_all))
    proj_summed = permute_psum(proj_local.astype(jnp.bfloat16), ("dp", "seq")).astype(jnp.float32)
    proj_grad = proj_summed * token_scale
    weight_part = proj_weight
    pooled_grad_t = lax.psum_scatter(
        lax.dot_general(
            weight_part, err_grad, (((1,), (1,)), ((), ())), preferred_element_type=jnp.float32
        ).astype(jnp.bfloat16),
        "tensor",
        scatter_dimension=0,
        tiled=True,
    )
    weight_part = local_weight
    down_sum = lax.dot_general(
        weight_part,
        lax.all_gather(pooled_grad_t, "seq", axis=1, tiled=True),
        (((0,), (1,)), ((), ())),
        preferred_element_type=jnp.float32,
    )
    down_grad = down_sum.astype(jnp.bfloat16).reshape(positions, groups_here, group_width)
    conv_local = jnp.einsum(
        "pkgc,pgo->gkco", windows, down_grad, preferred_element_type=jnp.float32
    )
    conv_flat = conv_local.astype(jnp.bfloat16).reshape(KERNEL * groups_here * group_width, group_width)
    conv_summed = (
        permute_psum(conv_flat, ("dp", "seq"))
        .reshape(conv_local.shape)
        .astype(jnp.float32)
    )
    position_scale = 1.0 / jnp.sqrt(jnp.float32(lax.axis_size("dp") * positions * seq_count))
    conv_grad = (conv_summed * position_scale).reshape(
        groups_here, KERNEL * group_width, group_width
    )
    window_grad = jnp.einsum(
        "pgo,gkco->pkgc", down_grad, taps_weight, preferred_element_type=jnp.float32
    )
    incoming = shifted(window_grad[-1, STRIDE:], "seq", 1)
    carried_grad = jnp.concatenate([incoming[None], window_grad[:-1, STRIDE:]], axis=0)
    byte_grad = (
        (window_grad[:, :STRIDE] + carried_grad).reshape(row_total, width).astype(jnp.bfloat16)
    )
    return (downsampled[None], byte_grad[None], conv_grad, proj_grad)


def solution(mesh):
    return jax.shard_map(
        local,
        mesh=mesh,
        in_specs=(
            P("dp", "seq", "tensor"),
            P("tensor", None, None),
            P("tensor"),
            P(None, "tensor"),
            P("dp", "seq", "tensor"),
            P("dp", None),
        ),
        out_specs=(
            P("dp", "seq", "tensor"),
            P("dp", "seq", "tensor"),
            P("tensor", None, None),
            P(None, "tensor"),
        ),
        check_vma=False,
    )
```

```python
import jax
import jax.numpy as jnp
from jax import lax
from jax.sharding import PartitionSpec as P

STRIDE = 4
KERNEL = 8
TENSOR_RING = 8


def shifted(block, axis, distance):
    devices = range(lax.axis_size(axis))
    route = [(i - distance, i) for i in devices if i - distance in devices]
    return lax.ppermute(block, axis, route)


def shard_sum(block, axis):
    count = lax.axis_size(axis)
    rank = lax.axis_index(axis)
    pieces = block.reshape((count, block.shape[0] // count) + block.shape[1:])
    total = lax.dynamic_index_in_dim(pieces, rank, 0, keepdims=False).astype(jnp.float32)
    for distance in range(1, count):
        route = [(i, (i + distance) % count) for i in range(count)]
        outgoing = lax.dynamic_index_in_dim(pieces, (rank + distance) % count, 0, keepdims=False)
        total = total + lax.ppermute(outgoing, axis, route).astype(jnp.float32)
    return total


def shard_gather(piece, axis):
    count = lax.axis_size(axis)
    rank = lax.axis_index(axis)
    rows = piece.shape[0]
    gathered = jnp.zeros((count * rows,) + piece.shape[1:], piece.dtype)
    gathered = lax.dynamic_update_slice_in_dim(gathered, piece, rank * rows, 0)
    for distance in range(1, count):
        route = [(i, (i + distance) % count) for i in range(count)]
        incoming = lax.ppermute(piece, axis, route)
        source = (rank + count - distance) % count
        gathered = lax.dynamic_update_slice_in_dim(gathered, incoming, source * rows, 0)
    return gathered


def permute_psum(block, axes):
    summed = block
    for axis in axes:
        summed = shard_sum(summed, axis).astype(block.dtype)
    for axis in axes[::-1]:
        summed = shard_gather(summed, axis)
    return summed


def ring_routes(count, ring):
    def device(pair, place):
        return pair * ring + place % ring
    pairs = count // ring
    plus = [(device(a, b), device(a, b + 1)) for a in range(pairs) for b in range(ring)]
    minus = [(device(a, b), device(a, b - 1)) for a in range(pairs) for b in range(ring)]
    across = [(i, (i + ring) % count) for i in range(count)]
    return plus, minus, across


def tensor_gather(piece, axis, ring):
    count = lax.axis_size(axis)
    rank = lax.axis_index(axis)
    pair_index = rank // ring
    place = rank % ring
    plus, minus, across = ring_routes(count, ring)
    other = lax.ppermute(piece, axis, across)
    pair = jnp.where(pair_index == 0, jnp.stack([piece, other]), jnp.stack([other, piece]))
    slots = jnp.zeros((ring,) + pair.shape, pair.dtype)
    slots = lax.dynamic_update_index_in_dim(slots, pair, place, 0)
    forward = pair
    backward = pair
    plus_steps = ring // 2
    minus_steps = ring - 1 - plus_steps
    for step in range(1, plus_steps + 1):
        forward = lax.ppermute(forward, axis, plus)
        slots = lax.dynamic_update_index_in_dim(slots, forward, (place + ring - step) % ring, 0)
        if step <= minus_steps:
            backward = lax.ppermute(backward, axis, minus)
            slots = lax.dynamic_update_index_in_dim(slots, backward, (place + step) % ring, 0)
    rows, width = piece.shape
    return slots.transpose(2, 1, 0, 3).reshape(rows, count * width)


def tensor_scatter(block, axis, ring):
    count = lax.axis_size(axis)
    rank = lax.axis_index(axis)
    pair_index = rank // ring
    place = rank % ring
    plus, minus, across = ring_routes(count, ring)
    view = block.reshape((count // ring, ring, block.shape[0] // count) + block.shape[1:])

    def own(target):
        return lax.dynamic_index_in_dim(view, target % ring, 1, keepdims=False).astype(jnp.float32)

    plus_steps = ring // 2
    minus_steps = ring - 1 - plus_steps
    total = own(place)
    outgoing = own(place + plus_steps).astype(block.dtype)
    for step in range(1, plus_steps + 1):
        incoming = lax.ppermute(outgoing, axis, plus).astype(jnp.float32)
        if step < plus_steps:
            outgoing = (incoming + own(place + plus_steps - step)).astype(block.dtype)
        else:
            total = total + incoming
    outgoing = own(place + ring - minus_steps).astype(block.dtype)
    for step in range(1, minus_steps + 1):
        incoming = lax.ppermute(outgoing, axis, minus).astype(jnp.float32)
        if step < minus_steps:
            outgoing = (incoming + own(place + ring - minus_steps + step)).astype(block.dtype)
        else:
            total = total + incoming
    sent = lax.dynamic_index_in_dim(total, 1 - pair_index, 0, keepdims=False)
    kept = lax.dynamic_index_in_dim(total, pair_index, 0, keepdims=False)
    return kept + lax.ppermute(sent.astype(block.dtype), axis, across).astype(jnp.float32)


def intersection_weights(span_start, span_end, span_lengths, first_position, position_count):
    byte_first = (first_position + jnp.arange(position_count, dtype=jnp.int32)) * STRIDE
    lower_edge = jnp.maximum(span_start[:, None], byte_first[None, :])
    upper_edge = jnp.minimum(span_end[:, None], byte_first[None, :] + STRIDE)
    covered = jnp.maximum(upper_edge - lower_edge, 0).astype(jnp.float32)
    return (covered / span_lengths[:, None].astype(jnp.float32)).astype(jnp.bfloat16)


def local(byte_acts, conv_weight, conv_bias, proj_weight, teacher, span_lengths):
    byte_rows = byte_acts[0]
    row_total, width = byte_rows.shape
    groups_here = conv_weight.shape[0]
    group_width = width // groups_here
    positions = row_total // STRIDE
    seq_count = lax.axis_size("seq")
    seq_rank = lax.axis_index("seq")
    lengths_doc = span_lengths[0]
    tokens_all = lengths_doc.shape[0]
    span_end = jnp.cumsum(lengths_doc)
    span_start = span_end - lengths_doc
    next_rows = shifted(byte_rows[:STRIDE], "seq", -1)
    extended = jnp.concatenate([byte_rows, next_rows], axis=0)
    blocks = extended.reshape(positions + 1, STRIDE, groups_here, group_width)
    windows = jnp.concatenate([blocks[:-1], blocks[1:]], axis=1)
    taps_weight = conv_weight.reshape(groups_here, KERNEL, group_width, group_width)
    conv_out = jnp.einsum(
        "pkgc,gkco->pgo", windows, taps_weight, preferred_element_type=jnp.float32
    )
    conv_out = conv_out + conv_bias.reshape(groups_here, group_width)[None]
    downsampled = conv_out.reshape(positions, width).astype(jnp.bfloat16)
    local_weight = intersection_weights(
        span_start, span_end, lengths_doc, seq_rank * positions, positions
    )
    tokens_here = tokens_all // seq_count
    own_start = lax.dynamic_slice_in_dim(span_start, seq_rank * tokens_here, tokens_here)
    own_end = lax.dynamic_slice_in_dim(span_end, seq_rank * tokens_here, tokens_here)
    own_lengths = lax.dynamic_slice_in_dim(lengths_doc, seq_rank * tokens_here, tokens_here)
    token_weight = intersection_weights(own_start, own_end, own_lengths, 0, positions * seq_count)
    down_all = lax.all_gather(downsampled, "seq", axis=0, tiled=True)
    pooled_sum = jnp.dot(token_weight, down_all, preferred_element_type=jnp.float32).astype(
        jnp.bfloat16
    )
    ring = TENSOR_RING
    split = tokens_here // 2
    gathered_parts = [
        lax.all_gather(pooled_sum[:split], "tensor", axis=1, tiled=True),
        tensor_gather(pooled_sum[split:], "tensor", ring),
    ]
    teacher_rows = teacher[0]
    err_parts = []
    proj_local = None
    for part, (gathered, lo, hi) in enumerate(
        zip(gathered_parts, (0, split), (split, tokens_here))
    ):
        predicted = jnp.dot(gathered, proj_weight, preferred_element_type=jnp.float32)
        err_part = (predicted - teacher_rows[lo:hi].astype(jnp.float32)).astype(jnp.bfloat16)
        err_parts.append(err_part)
        term = lax.dot_general(
            gathered, err_part, (((0,), (0,)), ((), ())), preferred_element_type=jnp.float32
        )
        proj_local = term if proj_local is None else proj_local + term
    token_scale = 1.0 / jnp.sqrt(jnp.float32(lax.axis_size("dp") * tokens_all))
    proj_summed = permute_psum(proj_local.astype(jnp.bfloat16), ("dp", "seq")).astype(jnp.float32)
    proj_grad = proj_summed * token_scale
    grad_blocks = [
        lax.dot_general(
            proj_weight, err_part, (((1,), (1,)), ((), ())), preferred_element_type=jnp.float32
        ).astype(jnp.bfloat16)
        for err_part in err_parts
    ]
    pooled_grad_t = jnp.concatenate(
        [
            lax.psum_scatter(grad_blocks[0], "tensor", scatter_dimension=0, tiled=True),
            tensor_scatter(grad_blocks[1], "tensor", ring).astype(jnp.bfloat16),
        ],
        axis=1,
    )
    weight_part = local_weight
    down_sum = lax.dot_general(
        weight_part,
        lax.all_gather(pooled_grad_t, "seq", axis=1, tiled=True),
        (((0,), (1,)), ((), ())),
        preferred_element_type=jnp.float32,
    )
    down_grad = down_sum.astype(jnp.bfloat16).reshape(positions, groups_here, group_width)
    conv_local = jnp.einsum(
        "pkgc,pgo->gkco", windows, down_grad, preferred_element_type=jnp.float32
    )
    conv_flat = conv_local.astype(jnp.bfloat16).reshape(KERNEL * groups_here * group_width, group_width)
    conv_summed = (
        permute_psum(conv_flat, ("dp", "seq"))
        .reshape(conv_local.shape)
        .astype(jnp.float32)
    )
    position_scale = 1.0 / jnp.sqrt(jnp.float32(lax.axis_size("dp") * positions * seq_count))
    conv_grad = (conv_summed * position_scale).reshape(
        groups_here, KERNEL * group_width, group_width
    )
    window_grad = jnp.einsum(
        "pgo,gkco->pkgc", down_grad, taps_weight, preferred_element_type=jnp.float32
    )
    incoming = shifted(window_grad[-1, STRIDE:], "seq", 1)
    carried_grad = jnp.concatenate([incoming[None], window_grad[:-1, STRIDE:]], axis=0)
    byte_grad = (
        (window_grad[:, :STRIDE] + carried_grad).reshape(row_total, width).astype(jnp.bfloat16)
    )
    return (downsampled[None], byte_grad[None], conv_grad, proj_grad)


def solution(mesh):
    return jax.shard_map(
        local,
        mesh=mesh,
        in_specs=(
            P("dp", "seq", "tensor"),
            P("tensor", None, None),
            P("tensor"),
            P(None, "tensor"),
            P("dp", "seq", "tensor"),
            P("dp", None),
        ),
        out_specs=(
            P("dp", "seq", "tensor"),
            P("dp", "seq", "tensor"),
            P("tensor", None, None),
            P(None, "tensor"),
        ),
        check_vma=False,
    )
```

```python
import jax
import jax.numpy as jnp
from jax import lax
from jax.sharding import PartitionSpec as P

STRIDE = 4
KERNEL = 8
TENSOR_RING = 8


def shifted(block, axis, distance):
    devices = range(lax.axis_size(axis))
    route = [(i - distance, i) for i in devices if i - distance in devices]
    return lax.ppermute(block, axis, route)


def shard_sum(block, axis):
    count = lax.axis_size(axis)
    rank = lax.axis_index(axis)
    pieces = block.reshape((count, block.shape[0] // count) + block.shape[1:])
    total = lax.dynamic_index_in_dim(pieces, rank, 0, keepdims=False).astype(jnp.float32)
    for distance in range(1, count):
        route = [(i, (i + distance) % count) for i in range(count)]
        outgoing = lax.dynamic_index_in_dim(pieces, (rank + distance) % count, 0, keepdims=False)
        total = total + lax.ppermute(outgoing, axis, route).astype(jnp.float32)
    return total


def shard_gather(piece, axis):
    count = lax.axis_size(axis)
    rank = lax.axis_index(axis)
    rows = piece.shape[0]
    gathered = jnp.zeros((count * rows,) + piece.shape[1:], piece.dtype)
    gathered = lax.dynamic_update_slice_in_dim(gathered, piece, rank * rows, 0)
    for distance in range(1, count):
        route = [(i, (i + distance) % count) for i in range(count)]
        incoming = lax.ppermute(piece, axis, route)
        source = (rank + count - distance) % count
        gathered = lax.dynamic_update_slice_in_dim(gathered, incoming, source * rows, 0)
    return gathered


def exchange_psum(block, axes):
    summed = block
    for axis in axes:
        count = lax.axis_size(axis)
        rank = lax.axis_index(axis)
        slots = jnp.zeros((count,) + block.shape, block.dtype)
        slots = lax.dynamic_update_index_in_dim(slots, summed, rank, 0)
        for distance in range(1, count):
            route = [(i, (i + distance) % count) for i in range(count)]
            incoming = lax.ppermute(summed, axis, route)
            slots = lax.dynamic_update_index_in_dim(slots, incoming, (rank + count - distance) % count, 0)
        summed = jnp.sum(slots.astype(jnp.float32), axis=0).astype(block.dtype)
    return summed


def permute_psum(block, axes):
    summed = block
    for axis in axes:
        summed = shard_sum(summed, axis).astype(block.dtype)
    for axis in axes[::-1]:
        summed = shard_gather(summed, axis)
    return summed


def ring_routes(count, ring):
    def device(pair, place):
        return pair * ring + place % ring
    pairs = count // ring
    plus = [(device(a, b), device(a, b + 1)) for a in range(pairs) for b in range(ring)]
    minus = [(device(a, b), device(a, b - 1)) for a in range(pairs) for b in range(ring)]
    across = [(i, (i + ring) % count) for i in range(count)]
    return plus, minus, across


def tensor_gather(piece, axis, ring):
    count = lax.axis_size(axis)
    rank = lax.axis_index(axis)
    pair_index = rank // ring
    place = rank % ring
    plus, minus, across = ring_routes(count, ring)
    other = lax.ppermute(piece, axis, across)
    pair = jnp.where(pair_index == 0, jnp.stack([piece, other]), jnp.stack([other, piece]))
    slots = jnp.zeros((ring,) + pair.shape, pair.dtype)
    slots = lax.dynamic_update_index_in_dim(slots, pair, place, 0)
    forward = pair
    backward = pair
    plus_steps = ring // 2
    minus_steps = ring - 1 - plus_steps
    for step in range(1, plus_steps + 1):
        forward = lax.ppermute(forward, axis, plus)
        slots = lax.dynamic_update_index_in_dim(slots, forward, (place + ring - step) % ring, 0)
        if step <= minus_steps:
            backward = lax.ppermute(backward, axis, minus)
            slots = lax.dynamic_update_index_in_dim(slots, backward, (place + step) % ring, 0)
    rows, width = piece.shape
    return slots.transpose(2, 1, 0, 3).reshape(rows, count * width)


def tensor_scatter(block, axis, ring):
    count = lax.axis_size(axis)
    rank = lax.axis_index(axis)
    pair_index = rank // ring
    place = rank % ring
    plus, minus, across = ring_routes(count, ring)
    view = block.reshape((count // ring, ring, block.shape[0] // count) + block.shape[1:])

    def own(target):
        return lax.dynamic_index_in_dim(view, target % ring, 1, keepdims=False).astype(jnp.float32)

    plus_steps = ring // 2
    minus_steps = ring - 1 - plus_steps
    total = own(place)
    outgoing = own(place + plus_steps).astype(block.dtype)
    for step in range(1, plus_steps + 1):
        incoming = lax.ppermute(outgoing, axis, plus).astype(jnp.float32)
        if step < plus_steps:
            outgoing = (incoming + own(place + plus_steps - step)).astype(block.dtype)
        else:
            total = total + incoming
    outgoing = own(place + ring - minus_steps).astype(block.dtype)
    for step in range(1, minus_steps + 1):
        incoming = lax.ppermute(outgoing, axis, minus).astype(jnp.float32)
        if step < minus_steps:
            outgoing = (incoming + own(place + ring - minus_steps + step)).astype(block.dtype)
        else:
            total = total + incoming
    sent = lax.dynamic_index_in_dim(total, 1 - pair_index, 0, keepdims=False)
    kept = lax.dynamic_index_in_dim(total, pair_index, 0, keepdims=False)
    return kept + lax.ppermute(sent.astype(block.dtype), axis, across).astype(jnp.float32)


def intersection_weights(span_start, span_end, span_lengths, first_position, position_count):
    byte_first = (first_position + jnp.arange(position_count, dtype=jnp.int32)) * STRIDE
    lower_edge = jnp.maximum(span_start[:, None], byte_first[None, :])
    upper_edge = jnp.minimum(span_end[:, None], byte_first[None, :] + STRIDE)
    covered = jnp.maximum(upper_edge - lower_edge, 0).astype(jnp.float32)
    return (covered / span_lengths[:, None].astype(jnp.float32)).astype(jnp.bfloat16)


def local(byte_acts, conv_weight, conv_bias, proj_weight, teacher, span_lengths):
    byte_rows = byte_acts[0]
    row_total, width = byte_rows.shape
    groups_here = conv_weight.shape[0]
    group_width = width // groups_here
    positions = row_total // STRIDE
    seq_count = lax.axis_size("seq")
    seq_rank = lax.axis_index("seq")
    lengths_doc = span_lengths[0]
    tokens_all = lengths_doc.shape[0]
    span_end = jnp.cumsum(lengths_doc)
    span_start = span_end - lengths_doc
    next_rows = shifted(byte_rows[:STRIDE], "seq", -1)
    extended = jnp.concatenate([byte_rows, next_rows], axis=0)
    blocks = extended.reshape(positions + 1, STRIDE, groups_here, group_width)
    windows = jnp.concatenate([blocks[:-1], blocks[1:]], axis=1)
    taps_weight = conv_weight.reshape(groups_here, KERNEL, group_width, group_width)
    conv_out = jnp.einsum(
        "pkgc,gkco->pgo", windows, taps_weight, preferred_element_type=jnp.float32
    )
    conv_out = conv_out + conv_bias.reshape(groups_here, group_width)[None]
    downsampled = conv_out.reshape(positions, width).astype(jnp.bfloat16)
    local_weight = intersection_weights(
        span_start, span_end, lengths_doc, seq_rank * positions, positions
    )
    tokens_here = tokens_all // seq_count
    own_start = lax.dynamic_slice_in_dim(span_start, seq_rank * tokens_here, tokens_here)
    own_end = lax.dynamic_slice_in_dim(span_end, seq_rank * tokens_here, tokens_here)
    own_lengths = lax.dynamic_slice_in_dim(lengths_doc, seq_rank * tokens_here, tokens_here)
    token_weight = intersection_weights(own_start, own_end, own_lengths, 0, positions * seq_count)
    down_all = shard_gather(downsampled, "seq")
    pooled_sum = jnp.dot(token_weight, down_all, preferred_element_type=jnp.float32).astype(
        jnp.bfloat16
    )
    ring = TENSOR_RING
    split = tokens_here // 2
    gathered_parts = [
        lax.all_gather(pooled_sum[:split], "tensor", axis=1, tiled=True),
        tensor_gather(pooled_sum[split:], "tensor", ring),
    ]
    teacher_rows = teacher[0]
    err_parts = []
    proj_local = None
    for part, (gathered, lo, hi) in enumerate(
        zip(gathered_parts, (0, split), (split, tokens_here))
    ):
        predicted = jnp.dot(gathered, proj_weight, preferred_element_type=jnp.float32)
        err_part = (predicted - teacher_rows[lo:hi].astype(jnp.float32)).astype(jnp.bfloat16)
        err_parts.append(err_part)
        term = lax.dot_general(
            gathered, err_part, (((0,), (0,)), ((), ())), preferred_element_type=jnp.float32
        )
        proj_local = term if proj_local is None else proj_local + term
    token_scale = 1.0 / jnp.sqrt(jnp.float32(lax.axis_size("dp") * tokens_all))
    proj_summed = permute_psum(proj_local.astype(jnp.bfloat16), ("dp", "seq")).astype(jnp.float32)
    proj_grad = proj_summed * token_scale
    grad_blocks = [
        lax.dot_general(
            proj_weight, err_part, (((1,), (1,)), ((), ())), preferred_element_type=jnp.float32
        ).astype(jnp.bfloat16)
        for err_part in err_parts
    ]
    pooled_grad_t = jnp.concatenate(
        [
            lax.psum_scatter(grad_blocks[0], "tensor", scatter_dimension=0, tiled=True),
            tensor_scatter(grad_blocks[1], "tensor", ring).astype(jnp.bfloat16),
        ],
        axis=1,
    )
    weight_part = local_weight
    down_sum = lax.dot_general(
        weight_part,
        lax.all_gather(pooled_grad_t, "seq", axis=1, tiled=True),
        (((0,), (1,)), ((), ())),
        preferred_element_type=jnp.float32,
    )
    down_grad = down_sum.astype(jnp.bfloat16).reshape(positions, groups_here, group_width)
    conv_local = jnp.einsum(
        "pkgc,pgo->gkco", windows, down_grad, preferred_element_type=jnp.float32
    )
    conv_flat = conv_local.astype(jnp.bfloat16).reshape(KERNEL * groups_here * group_width, group_width)
    conv_summed = (
        exchange_psum(conv_flat, ("dp", "seq"))
        .reshape(conv_local.shape)
        .astype(jnp.float32)
    )
    position_scale = 1.0 / jnp.sqrt(jnp.float32(lax.axis_size("dp") * positions * seq_count))
    conv_grad = (conv_summed * position_scale).reshape(
        groups_here, KERNEL * group_width, group_width
    )
    window_grad = jnp.einsum(
        "pgo,gkco->pkgc", down_grad, taps_weight, preferred_element_type=jnp.float32
    )
    incoming = shifted(window_grad[-1, STRIDE:], "seq", 1)
    carried_grad = jnp.concatenate([incoming[None], window_grad[:-1, STRIDE:]], axis=0)
    byte_grad = (
        (window_grad[:, :STRIDE] + carried_grad).reshape(row_total, width).astype(jnp.bfloat16)
    )
    return (downsampled[None], byte_grad[None], conv_grad, proj_grad)


def solution(mesh):
    return jax.shard_map(
        local,
        mesh=mesh,
        in_specs=(
            P("dp", "seq", "tensor"),
            P("tensor", None, None),
            P("tensor"),
            P(None, "tensor"),
            P("dp", "seq", "tensor"),
            P("dp", None),
        ),
        out_specs=(
            P("dp", "seq", "tensor"),
            P("dp", "seq", "tensor"),
            P("tensor", None, None),
            P(None, "tensor"),
        ),
        check_vma=False,
    )
```

```python
import jax
import jax.numpy as jnp
from jax import lax
from jax.sharding import PartitionSpec as P

STRIDE = 4
KERNEL = 8
TENSOR_RING = 8


def shifted(block, axis, distance):
    devices = range(lax.axis_size(axis))
    route = [(i - distance, i) for i in devices if i - distance in devices]
    return lax.ppermute(block, axis, route)


def shard_sum(block, axis):
    count = lax.axis_size(axis)
    received = lax.all_to_all(block, axis, 0, 0, tiled=True)
    pieces = received.reshape((count, block.shape[0] // count) + block.shape[1:])
    return jnp.sum(pieces.astype(jnp.float32), axis=0)


def shard_gather(piece, axis):
    count = lax.axis_size(axis)
    copies = jnp.broadcast_to(piece[None], (count,) + piece.shape)
    copies = copies.reshape((count * piece.shape[0],) + piece.shape[1:])
    return lax.all_to_all(copies, axis, 0, 0, tiled=True)


def exchange_psum(block, axes):
    summed = block
    for axis in axes:
        count = lax.axis_size(axis)
        gathered = shard_gather(summed, axis).reshape((count,) + block.shape)
        summed = jnp.sum(gathered.astype(jnp.float32), axis=0).astype(block.dtype)
    return summed


def permute_psum(block, axes):
    summed = block
    for axis in axes:
        summed = shard_sum(summed, axis).astype(block.dtype)
    for axis in axes[::-1]:
        summed = shard_gather(summed, axis)
    return summed


def ring_routes(count, ring):
    def device(pair, place):
        return pair * ring + place % ring
    pairs = count // ring
    plus = [(device(a, b), device(a, b + 1)) for a in range(pairs) for b in range(ring)]
    minus = [(device(a, b), device(a, b - 1)) for a in range(pairs) for b in range(ring)]
    across = [(i, (i + ring) % count) for i in range(count)]
    return plus, minus, across


def tensor_gather(piece, axis, ring):
    count = lax.axis_size(axis)
    rank = lax.axis_index(axis)
    pair_index = rank // ring
    place = rank % ring
    plus, minus, across = ring_routes(count, ring)
    other = lax.ppermute(piece, axis, across)
    pair = jnp.where(pair_index == 0, jnp.stack([piece, other]), jnp.stack([other, piece]))
    slots = jnp.zeros((ring,) + pair.shape, pair.dtype)
    slots = lax.dynamic_update_index_in_dim(slots, pair, place, 0)
    forward = pair
    backward = pair
    plus_steps = ring // 2
    minus_steps = ring - 1 - plus_steps
    for step in range(1, plus_steps + 1):
        forward = lax.ppermute(forward, axis, plus)
        slots = lax.dynamic_update_index_in_dim(slots, forward, (place + ring - step) % ring, 0)
        if step <= minus_steps:
            backward = lax.ppermute(backward, axis, minus)
            slots = lax.dynamic_update_index_in_dim(slots, backward, (place + step) % ring, 0)
    rows, width = piece.shape
    return slots.transpose(2, 1, 0, 3).reshape(rows, count * width)


def tensor_scatter(block, axis, ring):
    count = lax.axis_size(axis)
    rank = lax.axis_index(axis)
    pair_index = rank // ring
    place = rank % ring
    plus, minus, across = ring_routes(count, ring)
    view = block.reshape((count // ring, ring, block.shape[0] // count) + block.shape[1:])

    def own(target):
        return lax.dynamic_index_in_dim(view, target % ring, 1, keepdims=False).astype(jnp.float32)

    plus_steps = ring // 2
    minus_steps = ring - 1 - plus_steps
    total = own(place)
    outgoing = own(place + plus_steps).astype(block.dtype)
    for step in range(1, plus_steps + 1):
        incoming = lax.ppermute(outgoing, axis, plus).astype(jnp.float32)
        if step < plus_steps:
            outgoing = (incoming + own(place + plus_steps - step)).astype(block.dtype)
        else:
            total = total + incoming
    outgoing = own(place + ring - minus_steps).astype(block.dtype)
    for step in range(1, minus_steps + 1):
        incoming = lax.ppermute(outgoing, axis, minus).astype(jnp.float32)
        if step < minus_steps:
            outgoing = (incoming + own(place + ring - minus_steps + step)).astype(block.dtype)
        else:
            total = total + incoming
    sent = lax.dynamic_index_in_dim(total, 1 - pair_index, 0, keepdims=False)
    kept = lax.dynamic_index_in_dim(total, pair_index, 0, keepdims=False)
    return kept + lax.ppermute(sent.astype(block.dtype), axis, across).astype(jnp.float32)


def intersection_weights(span_start, span_end, span_lengths, first_position, position_count):
    byte_first = (first_position + jnp.arange(position_count, dtype=jnp.int32)) * STRIDE
    lower_edge = jnp.maximum(span_start[:, None], byte_first[None, :])
    upper_edge = jnp.minimum(span_end[:, None], byte_first[None, :] + STRIDE)
    covered = jnp.maximum(upper_edge - lower_edge, 0).astype(jnp.float32)
    return (covered / span_lengths[:, None].astype(jnp.float32)).astype(jnp.bfloat16)


def local(byte_acts, conv_weight, conv_bias, proj_weight, teacher, span_lengths):
    byte_rows = byte_acts[0]
    row_total, width = byte_rows.shape
    groups_here = conv_weight.shape[0]
    group_width = width // groups_here
    positions = row_total // STRIDE
    seq_count = lax.axis_size("seq")
    seq_rank = lax.axis_index("seq")
    lengths_doc = span_lengths[0]
    tokens_all = lengths_doc.shape[0]
    span_end = jnp.cumsum(lengths_doc)
    span_start = span_end - lengths_doc
    next_rows = shifted(byte_rows[:STRIDE], "seq", -1)
    extended = jnp.concatenate([byte_rows, next_rows], axis=0)
    blocks = extended.reshape(positions + 1, STRIDE, groups_here, group_width)
    windows = jnp.concatenate([blocks[:-1], blocks[1:]], axis=1)
    taps_weight = conv_weight.reshape(groups_here, KERNEL, group_width, group_width)
    conv_out = jnp.einsum(
        "pkgc,gkco->pgo", windows, taps_weight, preferred_element_type=jnp.float32
    )
    conv_out = conv_out + conv_bias.reshape(groups_here, group_width)[None]
    downsampled = conv_out.reshape(positions, width).astype(jnp.bfloat16)
    local_weight = intersection_weights(
        span_start, span_end, lengths_doc, seq_rank * positions, positions
    )
    tokens_here = tokens_all // seq_count
    own_start = lax.dynamic_slice_in_dim(span_start, seq_rank * tokens_here, tokens_here)
    own_end = lax.dynamic_slice_in_dim(span_end, seq_rank * tokens_here, tokens_here)
    own_lengths = lax.dynamic_slice_in_dim(lengths_doc, seq_rank * tokens_here, tokens_here)
    token_weight = intersection_weights(own_start, own_end, own_lengths, 0, positions * seq_count)
    down_all = shard_gather(downsampled, "seq")
    pooled_sum = jnp.dot(token_weight, down_all, preferred_element_type=jnp.float32).astype(
        jnp.bfloat16
    )
    ring = TENSOR_RING
    split = tokens_here // 2
    gathered_parts = [
        lax.all_gather(pooled_sum[:split], "tensor", axis=1, tiled=True),
        tensor_gather(pooled_sum[split:], "tensor", ring),
    ]
    teacher_rows = teacher[0]
    err_parts = []
    proj_local = None
    for part, (gathered, lo, hi) in enumerate(
        zip(gathered_parts, (0, split), (split, tokens_here))
    ):
        predicted = jnp.dot(gathered, proj_weight, preferred_element_type=jnp.float32)
        err_part = (predicted - teacher_rows[lo:hi].astype(jnp.float32)).astype(jnp.bfloat16)
        err_parts.append(err_part)
        term = lax.dot_general(
            gathered, err_part, (((0,), (0,)), ((), ())), preferred_element_type=jnp.float32
        )
        proj_local = term if proj_local is None else proj_local + term
    token_scale = 1.0 / jnp.sqrt(jnp.float32(lax.axis_size("dp") * tokens_all))
    proj_summed = permute_psum(proj_local.astype(jnp.bfloat16), ("dp", "seq")).astype(jnp.float32)
    proj_grad = proj_summed * token_scale
    grad_blocks = [
        lax.dot_general(
            proj_weight, err_part, (((1,), (1,)), ((), ())), preferred_element_type=jnp.float32
        ).astype(jnp.bfloat16)
        for err_part in err_parts
    ]
    pooled_grad_t = jnp.concatenate(
        [
            lax.psum_scatter(grad_blocks[0], "tensor", scatter_dimension=0, tiled=True),
            tensor_scatter(grad_blocks[1], "tensor", ring).astype(jnp.bfloat16),
        ],
        axis=1,
    )
    weight_part = local_weight
    down_sum = lax.dot_general(
        weight_part,
        lax.all_gather(pooled_grad_t, "seq", axis=1, tiled=True),
        (((0,), (1,)), ((), ())),
        preferred_element_type=jnp.float32,
    )
    down_grad = down_sum.astype(jnp.bfloat16).reshape(positions, groups_here, group_width)
    conv_local = jnp.einsum(
        "pkgc,pgo->gkco", windows, down_grad, preferred_element_type=jnp.float32
    )
    conv_flat = conv_local.astype(jnp.bfloat16).reshape(KERNEL * groups_here * group_width, group_width)
    conv_summed = (
        exchange_psum(conv_flat, ("dp", "seq"))
        .reshape(conv_local.shape)
        .astype(jnp.float32)
    )
    position_scale = 1.0 / jnp.sqrt(jnp.float32(lax.axis_size("dp") * positions * seq_count))
    conv_grad = (conv_summed * position_scale).reshape(
        groups_here, KERNEL * group_width, group_width
    )
    window_grad = jnp.einsum(
        "pgo,gkco->pkgc", down_grad, taps_weight, preferred_element_type=jnp.float32
    )
    incoming = shifted(window_grad[-1, STRIDE:], "seq", 1)
    carried_grad = jnp.concatenate([incoming[None], window_grad[:-1, STRIDE:]], axis=0)
    byte_grad = (
        (window_grad[:, :STRIDE] + carried_grad).reshape(row_total, width).astype(jnp.bfloat16)
    )
    return (downsampled[None], byte_grad[None], conv_grad, proj_grad)


def solution(mesh):
    return jax.shard_map(
        local,
        mesh=mesh,
        in_specs=(
            P("dp", "seq", "tensor"),
            P("tensor", None, None),
            P("tensor"),
            P(None, "tensor"),
            P("dp", "seq", "tensor"),
            P("dp", None),
        ),
        out_specs=(
            P("dp", "seq", "tensor"),
            P("dp", "seq", "tensor"),
            P("tensor", None, None),
            P(None, "tensor"),
        ),
        check_vma=False,
    )
```

```python
import jax
import jax.numpy as jnp
from jax import lax
from jax.sharding import PartitionSpec as P

STRIDE = 4
KERNEL = 8
TENSOR_RING = 8


def shifted(block, axis, distance):
    devices = range(lax.axis_size(axis))
    route = [(i - distance, i) for i in devices if i - distance in devices]
    return lax.ppermute(block, axis, route)


def shard_sum(block, axis):
    count = lax.axis_size(axis)
    rank = lax.axis_index(axis)
    pieces = block.reshape((count, block.shape[0] // count) + block.shape[1:])
    total = lax.dynamic_index_in_dim(pieces, rank, 0, keepdims=False).astype(jnp.float32)
    for distance in range(1, count):
        route = [(i, (i + distance) % count) for i in range(count)]
        outgoing = lax.dynamic_index_in_dim(pieces, (rank + distance) % count, 0, keepdims=False)
        total = total + lax.ppermute(outgoing, axis, route).astype(jnp.float32)
    return total


def shard_gather(piece, axis):
    count = lax.axis_size(axis)
    rank = lax.axis_index(axis)
    rows = piece.shape[0]
    gathered = jnp.zeros((count * rows,) + piece.shape[1:], piece.dtype)
    gathered = lax.dynamic_update_slice_in_dim(gathered, piece, rank * rows, 0)
    for distance in range(1, count):
        route = [(i, (i + distance) % count) for i in range(count)]
        incoming = lax.ppermute(piece, axis, route)
        source = (rank + count - distance) % count
        gathered = lax.dynamic_update_slice_in_dim(gathered, incoming, source * rows, 0)
    return gathered


def exchange_psum(block, axes):
    summed = block
    for axis in axes:
        count = lax.axis_size(axis)
        rank = lax.axis_index(axis)
        slots = jnp.zeros((count,) + block.shape, block.dtype)
        slots = lax.dynamic_update_index_in_dim(slots, summed, rank, 0)
        for distance in range(1, count):
            route = [(i, (i + distance) % count) for i in range(count)]
            incoming = lax.ppermute(summed, axis, route)
            slots = lax.dynamic_update_index_in_dim(slots, incoming, (rank + count - distance) % count, 0)
        summed = jnp.sum(slots.astype(jnp.float32), axis=0).astype(block.dtype)
    return summed


def permute_psum(block, axes):
    summed = block
    for axis in axes:
        summed = shard_sum(summed, axis).astype(block.dtype)
    for axis in axes[:0:-1]:
        summed = shard_gather(summed, axis)
    return summed


def ring_routes(count, ring):
    def device(pair, place):
        return pair * ring + place % ring
    pairs = count // ring
    plus = [(device(a, b), device(a, b + 1)) for a in range(pairs) for b in range(ring)]
    minus = [(device(a, b), device(a, b - 1)) for a in range(pairs) for b in range(ring)]
    across = [(i, (i + ring) % count) for i in range(count)]
    return plus, minus, across


def tensor_gather(piece, axis, ring):
    count = lax.axis_size(axis)
    rank = lax.axis_index(axis)
    pair_index = rank // ring
    place = rank % ring
    plus, minus, across = ring_routes(count, ring)
    other = lax.ppermute(piece, axis, across)
    pair = jnp.where(pair_index == 0, jnp.stack([piece, other]), jnp.stack([other, piece]))
    slots = jnp.zeros((ring,) + pair.shape, pair.dtype)
    slots = lax.dynamic_update_index_in_dim(slots, pair, place, 0)
    forward = pair
    backward = pair
    plus_steps = ring // 2
    minus_steps = ring - 1 - plus_steps
    for step in range(1, plus_steps + 1):
        forward = lax.ppermute(forward, axis, plus)
        slots = lax.dynamic_update_index_in_dim(slots, forward, (place + ring - step) % ring, 0)
        if step <= minus_steps:
            backward = lax.ppermute(backward, axis, minus)
            slots = lax.dynamic_update_index_in_dim(slots, backward, (place + step) % ring, 0)
    rows, width = piece.shape
    return slots.transpose(2, 1, 0, 3).reshape(rows, count * width)


def tensor_scatter(block, axis, ring):
    count = lax.axis_size(axis)
    rank = lax.axis_index(axis)
    pair_index = rank // ring
    place = rank % ring
    plus, minus, across = ring_routes(count, ring)
    view = block.reshape((count // ring, ring, block.shape[0] // count) + block.shape[1:])

    def own(target):
        return lax.dynamic_index_in_dim(view, target % ring, 1, keepdims=False).astype(jnp.float32)

    plus_steps = ring // 2
    minus_steps = ring - 1 - plus_steps
    total = own(place)
    outgoing = own(place + plus_steps).astype(block.dtype)
    for step in range(1, plus_steps + 1):
        incoming = lax.ppermute(outgoing, axis, plus).astype(jnp.float32)
        if step < plus_steps:
            outgoing = (incoming + own(place + plus_steps - step)).astype(block.dtype)
        else:
            total = total + incoming
    outgoing = own(place + ring - minus_steps).astype(block.dtype)
    for step in range(1, minus_steps + 1):
        incoming = lax.ppermute(outgoing, axis, minus).astype(jnp.float32)
        if step < minus_steps:
            outgoing = (incoming + own(place + ring - minus_steps + step)).astype(block.dtype)
        else:
            total = total + incoming
    sent = lax.dynamic_index_in_dim(total, 1 - pair_index, 0, keepdims=False)
    kept = lax.dynamic_index_in_dim(total, pair_index, 0, keepdims=False)
    return kept + lax.ppermute(sent.astype(block.dtype), axis, across).astype(jnp.float32)


def intersection_weights(span_start, span_end, span_lengths, first_position, position_count):
    byte_first = (first_position + jnp.arange(position_count, dtype=jnp.int32)) * STRIDE
    lower_edge = jnp.maximum(span_start[:, None], byte_first[None, :])
    upper_edge = jnp.minimum(span_end[:, None], byte_first[None, :] + STRIDE)
    covered = jnp.maximum(upper_edge - lower_edge, 0).astype(jnp.float32)
    return (covered / span_lengths[:, None].astype(jnp.float32)).astype(jnp.bfloat16)


def local(byte_acts, conv_weight, conv_bias, proj_weight, teacher, span_lengths):
    byte_rows = byte_acts[0]
    row_total, width = byte_rows.shape
    groups_here = conv_weight.shape[0]
    group_width = width // groups_here
    positions = row_total // STRIDE
    seq_count = lax.axis_size("seq")
    seq_rank = lax.axis_index("seq")
    lengths_doc = span_lengths[0]
    tokens_all = lengths_doc.shape[0]
    span_end = jnp.cumsum(lengths_doc)
    span_start = span_end - lengths_doc
    next_rows = shifted(byte_rows[:STRIDE], "seq", -1)
    extended = jnp.concatenate([byte_rows, next_rows], axis=0)
    blocks = extended.reshape(positions + 1, STRIDE, groups_here, group_width)
    windows = jnp.concatenate([blocks[:-1], blocks[1:]], axis=1)
    taps_weight = conv_weight.reshape(groups_here, KERNEL, group_width, group_width)
    conv_out = jnp.einsum(
        "pkgc,gkco->pgo", windows, taps_weight, preferred_element_type=jnp.float32
    )
    conv_out = conv_out + conv_bias.reshape(groups_here, group_width)[None]
    downsampled = conv_out.reshape(positions, width).astype(jnp.bfloat16)
    local_weight = intersection_weights(
        span_start, span_end, lengths_doc, seq_rank * positions, positions
    )
    tokens_here = tokens_all // seq_count
    own_start = lax.dynamic_slice_in_dim(span_start, seq_rank * tokens_here, tokens_here)
    own_end = lax.dynamic_slice_in_dim(span_end, seq_rank * tokens_here, tokens_here)
    own_lengths = lax.dynamic_slice_in_dim(lengths_doc, seq_rank * tokens_here, tokens_here)
    token_weight = intersection_weights(own_start, own_end, own_lengths, 0, positions * seq_count)
    down_all = shard_gather(downsampled, "seq")
    pooled_sum = jnp.dot(token_weight, down_all, preferred_element_type=jnp.float32).astype(
        jnp.bfloat16
    )
    ring = TENSOR_RING
    split = tokens_here * 3 // 8
    gathered_parts = [
        lax.all_gather(pooled_sum[:split], "tensor", axis=1, tiled=True),
        tensor_gather(pooled_sum[split:], "tensor", ring),
    ]
    teacher_rows = teacher[0]
    err_parts = []
    proj_local = None
    for part, (gathered, lo, hi) in enumerate(
        zip(gathered_parts, (0, split), (split, tokens_here))
    ):
        predicted = jnp.dot(gathered, proj_weight, preferred_element_type=jnp.float32)
        err_part = (predicted - teacher_rows[lo:hi].astype(jnp.float32)).astype(jnp.bfloat16)
        err_parts.append(err_part)
        term = lax.dot_general(
            gathered, err_part, (((0,), (0,)), ((), ())), preferred_element_type=jnp.float32
        )
        proj_local = term if proj_local is None else proj_local + term
    token_scale = 1.0 / jnp.sqrt(jnp.float32(lax.axis_size("dp") * tokens_all))
    proj_partial = permute_psum(proj_local.astype(jnp.bfloat16), ("dp", "seq"))
    err_grad = jnp.concatenate(err_parts, axis=0)
    half = tokens_here // 2
    grad_blocks = [
        lax.dot_general(
            proj_weight, err_part, (((1,), (1,)), ((), ())), preferred_element_type=jnp.float32
        ).astype(jnp.bfloat16)
        for err_part in (err_grad[:half], err_grad[half:])
    ]
    pooled_grad_t = jnp.concatenate(
        [
            lax.psum_scatter(grad_blocks[0], "tensor", scatter_dimension=0, tiled=True),
            tensor_scatter(grad_blocks[1], "tensor", ring).astype(jnp.bfloat16),
        ],
        axis=1,
    )
    weight_part = local_weight
    pooled_grad_all = lax.all_gather(pooled_grad_t, "seq", axis=1, tiled=True)
    pooled_grad_all, proj_partial = lax.optimization_barrier((pooled_grad_all, proj_partial))
    proj_summed = lax.all_gather(proj_partial, "dp", axis=0, tiled=True).astype(jnp.float32)
    proj_grad = proj_summed * token_scale
    down_sum = lax.dot_general(
        weight_part,
        pooled_grad_all,
        (((0,), (1,)), ((), ())),
        preferred_element_type=jnp.float32,
    )
    down_grad = down_sum.astype(jnp.bfloat16).reshape(positions, groups_here, group_width)
    conv_local = jnp.einsum(
        "pkgc,pgo->gkco", windows, down_grad, preferred_element_type=jnp.float32
    )
    conv_flat = conv_local.astype(jnp.bfloat16).reshape(KERNEL * groups_here * group_width, group_width)
    conv_summed = (
        exchange_psum(conv_flat, ("dp", "seq"))
        .reshape(conv_local.shape)
        .astype(jnp.float32)
    )
    position_scale = 1.0 / jnp.sqrt(jnp.float32(lax.axis_size("dp") * positions * seq_count))
    conv_grad = (conv_summed * position_scale).reshape(
        groups_here, KERNEL * group_width, group_width
    )
    window_grad = jnp.einsum(
        "pgo,gkco->pkgc", down_grad, taps_weight, preferred_element_type=jnp.float32
    )
    incoming = shifted(window_grad[-1, STRIDE:], "seq", 1)
    carried_grad = jnp.concatenate([incoming[None], window_grad[:-1, STRIDE:]], axis=0)
    byte_grad = (
        (window_grad[:, :STRIDE] + carried_grad).reshape(row_total, width).astype(jnp.bfloat16)
    )
    return (downsampled[None], byte_grad[None], conv_grad, proj_grad)


def solution(mesh):
    return jax.shard_map(
        local,
        mesh=mesh,
        in_specs=(
            P("dp", "seq", "tensor"),
            P("tensor", None, None),
            P("tensor"),
            P(None, "tensor"),
            P("dp", "seq", "tensor"),
            P("dp", None),
        ),
        out_specs=(
            P("dp", "seq", "tensor"),
            P("dp", "seq", "tensor"),
            P("tensor", None, None),
            P(None, "tensor"),
        ),
        check_vma=False,
    )
```

```python
import jax
import jax.numpy as jnp
from jax import lax
from jax.sharding import PartitionSpec as P

STRIDE = 4
KERNEL = 8
TENSOR_RING = 8


def shifted(block, axis, distance):
    devices = range(lax.axis_size(axis))
    route = [(i - distance, i) for i in devices if i - distance in devices]
    return lax.ppermute(block, axis, route)


def shard_sum(block, axis):
    count = lax.axis_size(axis)
    rank = lax.axis_index(axis)
    pieces = block.reshape((count, block.shape[0] // count) + block.shape[1:])
    total = lax.dynamic_index_in_dim(pieces, rank, 0, keepdims=False).astype(jnp.float32)
    for distance in range(1, count):
        route = [(i, (i + distance) % count) for i in range(count)]
        outgoing = lax.dynamic_index_in_dim(pieces, (rank + distance) % count, 0, keepdims=False)
        total = total + lax.ppermute(outgoing, axis, route).astype(jnp.float32)
    return total


def shard_gather(piece, axis):
    count = lax.axis_size(axis)
    rank = lax.axis_index(axis)
    rows = piece.shape[0]
    gathered = jnp.zeros((count * rows,) + piece.shape[1:], piece.dtype)
    gathered = lax.dynamic_update_slice_in_dim(gathered, piece, rank * rows, 0)
    for distance in range(1, count):
        route = [(i, (i + distance) % count) for i in range(count)]
        incoming = lax.ppermute(piece, axis, route)
        source = (rank + count - distance) % count
        gathered = lax.dynamic_update_slice_in_dim(gathered, incoming, source * rows, 0)
    return gathered


def exchange_psum(block, axes):
    summed = block
    for axis in axes:
        count = lax.axis_size(axis)
        rank = lax.axis_index(axis)
        slots = jnp.zeros((count,) + block.shape, block.dtype)
        slots = lax.dynamic_update_index_in_dim(slots, summed, rank, 0)
        for distance in range(1, count):
            route = [(i, (i + distance) % count) for i in range(count)]
            incoming = lax.ppermute(summed, axis, route)
            slots = lax.dynamic_update_index_in_dim(slots, incoming, (rank + count - distance) % count, 0)
        summed = jnp.sum(slots.astype(jnp.float32), axis=0).astype(block.dtype)
    return summed


def permute_psum(block, axes):
    summed = block
    for axis in axes:
        summed = shard_sum(summed, axis).astype(block.dtype)
    for axis in axes[::-1]:
        summed = shard_gather(summed, axis)
    return summed


def ring_routes(count, ring):
    def device(pair, place):
        return pair * ring + place % ring
    pairs = count // ring
    plus = [(device(a, b), device(a, b + 1)) for a in range(pairs) for b in range(ring)]
    minus = [(device(a, b), device(a, b - 1)) for a in range(pairs) for b in range(ring)]
    across = [(i, (i + ring) % count) for i in range(count)]
    return plus, minus, across


def tensor_gather(piece, axis, ring):
    count = lax.axis_size(axis)
    rank = lax.axis_index(axis)
    pair_index = rank // ring
    place = rank % ring
    plus, minus, across = ring_routes(count, ring)
    other = lax.ppermute(piece, axis, across)
    pair = jnp.where(pair_index == 0, jnp.stack([piece, other]), jnp.stack([other, piece]))
    slots = jnp.zeros((ring,) + pair.shape, pair.dtype)
    slots = lax.dynamic_update_index_in_dim(slots, pair, place, 0)
    forward = pair
    backward = pair
    plus_steps = ring // 2
    minus_steps = ring - 1 - plus_steps
    for step in range(1, plus_steps + 1):
        forward = lax.ppermute(forward, axis, plus)
        slots = lax.dynamic_update_index_in_dim(slots, forward, (place + ring - step) % ring, 0)
        if step <= minus_steps:
            backward = lax.ppermute(backward, axis, minus)
            slots = lax.dynamic_update_index_in_dim(slots, backward, (place + step) % ring, 0)
    rows, width = piece.shape
    return slots.transpose(2, 1, 0, 3).reshape(rows, count * width)


def tensor_scatter(block, axis, ring):
    count = lax.axis_size(axis)
    rank = lax.axis_index(axis)
    pair_index = rank // ring
    place = rank % ring
    plus, minus, across = ring_routes(count, ring)
    view = block.reshape((count // ring, ring, block.shape[0] // count) + block.shape[1:])

    def own(target):
        return lax.dynamic_index_in_dim(view, target % ring, 1, keepdims=False).astype(jnp.float32)

    plus_steps = ring // 2
    minus_steps = ring - 1 - plus_steps
    total = own(place)
    outgoing = own(place + plus_steps).astype(block.dtype)
    for step in range(1, plus_steps + 1):
        incoming = lax.ppermute(outgoing, axis, plus).astype(jnp.float32)
        if step < plus_steps:
            outgoing = (incoming + own(place + plus_steps - step)).astype(block.dtype)
        else:
            total = total + incoming
    outgoing = own(place + ring - minus_steps).astype(block.dtype)
    for step in range(1, minus_steps + 1):
        incoming = lax.ppermute(outgoing, axis, minus).astype(jnp.float32)
        if step < minus_steps:
            outgoing = (incoming + own(place + ring - minus_steps + step)).astype(block.dtype)
        else:
            total = total + incoming
    sent = lax.dynamic_index_in_dim(total, 1 - pair_index, 0, keepdims=False)
    kept = lax.dynamic_index_in_dim(total, pair_index, 0, keepdims=False)
    return kept + lax.ppermute(sent.astype(block.dtype), axis, across).astype(jnp.float32)


def intersection_weights(span_start, span_end, span_lengths, first_position, position_count):
    byte_first = (first_position + jnp.arange(position_count, dtype=jnp.int32)) * STRIDE
    lower_edge = jnp.maximum(span_start[:, None], byte_first[None, :])
    upper_edge = jnp.minimum(span_end[:, None], byte_first[None, :] + STRIDE)
    covered = jnp.maximum(upper_edge - lower_edge, 0).astype(jnp.float32)
    return (covered / span_lengths[:, None].astype(jnp.float32)).astype(jnp.bfloat16)


def local(byte_acts, conv_weight, conv_bias, proj_weight, teacher, span_lengths):
    byte_rows = byte_acts[0]
    row_total, width = byte_rows.shape
    groups_here = conv_weight.shape[0]
    group_width = width // groups_here
    positions = row_total // STRIDE
    seq_count = lax.axis_size("seq")
    seq_rank = lax.axis_index("seq")
    lengths_doc = span_lengths[0]
    tokens_all = lengths_doc.shape[0]
    span_end = jnp.cumsum(lengths_doc)
    span_start = span_end - lengths_doc
    next_rows = shifted(byte_rows[:STRIDE], "seq", -1)
    extended = jnp.concatenate([byte_rows, next_rows], axis=0)
    blocks = extended.reshape(positions + 1, STRIDE, groups_here, group_width)
    windows = jnp.concatenate([blocks[:-1], blocks[1:]], axis=1)
    taps_weight = conv_weight.reshape(groups_here, KERNEL, group_width, group_width)
    conv_out = jnp.einsum(
        "pkgc,gkco->pgo", windows, taps_weight, preferred_element_type=jnp.float32
    )
    conv_out = conv_out + conv_bias.reshape(groups_here, group_width)[None]
    downsampled = conv_out.reshape(positions, width).astype(jnp.bfloat16)
    local_weight = intersection_weights(
        span_start, span_end, lengths_doc, seq_rank * positions, positions
    )
    tokens_here = tokens_all // seq_count
    own_start = lax.dynamic_slice_in_dim(span_start, seq_rank * tokens_here, tokens_here)
    own_end = lax.dynamic_slice_in_dim(span_end, seq_rank * tokens_here, tokens_here)
    own_lengths = lax.dynamic_slice_in_dim(lengths_doc, seq_rank * tokens_here, tokens_here)
    token_weight = intersection_weights(own_start, own_end, own_lengths, 0, positions * seq_count)
    down_all = shard_gather(downsampled, "seq")
    pooled_sum = jnp.dot(token_weight, down_all, preferred_element_type=jnp.float32).astype(
        jnp.bfloat16
    )
    ring = TENSOR_RING
    gathered = tensor_gather(pooled_sum, "tensor", ring)
    predicted = jnp.dot(gathered, proj_weight, preferred_element_type=jnp.float32)
    err_grad = (predicted - teacher[0].astype(jnp.float32)).astype(jnp.bfloat16)
    proj_local = lax.dot_general(
        gathered, err_grad, (((0,), (0,)), ((), ())), preferred_element_type=jnp.float32
    )
    token_scale = 1.0 / jnp.sqrt(jnp.float32(lax.axis_size("dp") * tokens_all))
    proj_summed = permute_psum(proj_local.astype(jnp.bfloat16), ("dp", "seq")).astype(jnp.float32)
    proj_grad = proj_summed * token_scale
    grad_block = lax.dot_general(
        proj_weight, err_grad, (((1,), (1,)), ((), ())), preferred_element_type=jnp.float32
    ).astype(jnp.bfloat16)
    pooled_grad_t = tensor_scatter(grad_block, "tensor", ring).astype(jnp.bfloat16)
    weight_part = local_weight
    down_sum = lax.dot_general(
        weight_part,
        lax.all_gather(pooled_grad_t, "seq", axis=1, tiled=True),
        (((0,), (1,)), ((), ())),
        preferred_element_type=jnp.float32,
    )
    down_grad = down_sum.astype(jnp.bfloat16).reshape(positions, groups_here, group_width)
    conv_local = jnp.einsum(
        "pkgc,pgo->gkco", windows, down_grad, preferred_element_type=jnp.float32
    )
    conv_flat = conv_local.astype(jnp.bfloat16).reshape(KERNEL * groups_here * group_width, group_width)
    conv_summed = (
        exchange_psum(conv_flat, ("dp", "seq"))
        .reshape(conv_local.shape)
        .astype(jnp.float32)
    )
    position_scale = 1.0 / jnp.sqrt(jnp.float32(lax.axis_size("dp") * positions * seq_count))
    conv_grad = (conv_summed * position_scale).reshape(
        groups_here, KERNEL * group_width, group_width
    )
    window_grad = jnp.einsum(
        "pgo,gkco->pkgc", down_grad, taps_weight, preferred_element_type=jnp.float32
    )
    incoming = shifted(window_grad[-1, STRIDE:], "seq", 1)
    carried_grad = jnp.concatenate([incoming[None], window_grad[:-1, STRIDE:]], axis=0)
    byte_grad = (
        (window_grad[:, :STRIDE] + carried_grad).reshape(row_total, width).astype(jnp.bfloat16)
    )
    return (downsampled[None], byte_grad[None], conv_grad, proj_grad)


def solution(mesh):
    return jax.shard_map(
        local,
        mesh=mesh,
        in_specs=(
            P("dp", "seq", "tensor"),
            P("tensor", None, None),
            P("tensor"),
            P(None, "tensor"),
            P("dp", "seq", "tensor"),
            P("dp", None),
        ),
        out_specs=(
            P("dp", "seq", "tensor"),
            P("dp", "seq", "tensor"),
            P("tensor", None, None),
            P(None, "tensor"),
        ),
        check_vma=False,
    )
```

```python
import jax
import jax.numpy as jnp
from jax import lax
from jax.sharding import PartitionSpec as P

STRIDE = 4
KERNEL = 8
TENSOR_RING = 8


def shifted(block, axis, distance):
    devices = range(lax.axis_size(axis))
    route = [(i - distance, i) for i in devices if i - distance in devices]
    return lax.ppermute(block, axis, route)


def shard_sum(block, axis):
    count = lax.axis_size(axis)
    rank = lax.axis_index(axis)
    pieces = block.reshape((count, block.shape[0] // count) + block.shape[1:])
    total = lax.dynamic_index_in_dim(pieces, rank, 0, keepdims=False).astype(jnp.float32)
    for distance in range(1, count):
        route = [(i, (i + distance) % count) for i in range(count)]
        outgoing = lax.dynamic_index_in_dim(pieces, (rank + distance) % count, 0, keepdims=False)
        total = total + lax.ppermute(outgoing, axis, route).astype(jnp.float32)
    return total


def shard_gather(piece, axis):
    count = lax.axis_size(axis)
    rank = lax.axis_index(axis)
    rows = piece.shape[0]
    gathered = jnp.zeros((count * rows,) + piece.shape[1:], piece.dtype)
    gathered = lax.dynamic_update_slice_in_dim(gathered, piece, rank * rows, 0)
    for distance in range(1, count):
        route = [(i, (i + distance) % count) for i in range(count)]
        incoming = lax.ppermute(piece, axis, route)
        source = (rank + count - distance) % count
        gathered = lax.dynamic_update_slice_in_dim(gathered, incoming, source * rows, 0)
    return gathered


def exchange_psum(block, axes):
    summed = block
    for axis in axes:
        count = lax.axis_size(axis)
        rank = lax.axis_index(axis)
        slots = jnp.zeros((count,) + block.shape, block.dtype)
        slots = lax.dynamic_update_index_in_dim(slots, summed, rank, 0)
        for distance in range(1, count):
            route = [(i, (i + distance) % count) for i in range(count)]
            incoming = lax.ppermute(summed, axis, route)
            slots = lax.dynamic_update_index_in_dim(slots, incoming, (rank + count - distance) % count, 0)
        summed = jnp.sum(slots.astype(jnp.float32), axis=0).astype(block.dtype)
    return summed


def permute_psum(block, axes):
    summed = block
    for axis in axes:
        summed = shard_sum(summed, axis).astype(block.dtype)
    for axis in axes[::-1]:
        summed = shard_gather(summed, axis)
    return summed


def ring_routes(count, ring):
    def device(pair, place):
        return pair * ring + place % ring
    pairs = count // ring
    plus = [(device(a, b), device(a, b + 1)) for a in range(pairs) for b in range(ring)]
    minus = [(device(a, b), device(a, b - 1)) for a in range(pairs) for b in range(ring)]
    across = [(i, (i + ring) % count) for i in range(count)]
    return plus, minus, across


def tensor_gather(piece, axis, ring):
    count = lax.axis_size(axis)
    rank = lax.axis_index(axis)
    pair_index = rank // ring
    place = rank % ring
    plus, minus, across = ring_routes(count, ring)
    other = lax.ppermute(piece, axis, across)
    pair = jnp.where(pair_index == 0, jnp.stack([piece, other]), jnp.stack([other, piece]))
    slots = jnp.zeros((ring,) + pair.shape, pair.dtype)
    slots = lax.dynamic_update_index_in_dim(slots, pair, place, 0)
    forward = pair
    backward = pair
    plus_steps = ring // 2
    minus_steps = ring - 1 - plus_steps
    for step in range(1, plus_steps + 1):
        forward = lax.ppermute(forward, axis, plus)
        slots = lax.dynamic_update_index_in_dim(slots, forward, (place + ring - step) % ring, 0)
        if step <= minus_steps:
            backward = lax.ppermute(backward, axis, minus)
            slots = lax.dynamic_update_index_in_dim(slots, backward, (place + step) % ring, 0)
    rows, width = piece.shape
    return slots.transpose(2, 1, 0, 3).reshape(rows, count * width)


def tensor_scatter(block, axis, ring):
    count = lax.axis_size(axis)
    rank = lax.axis_index(axis)
    pair_index = rank // ring
    place = rank % ring
    plus, minus, across = ring_routes(count, ring)
    view = block.reshape((count // ring, ring, block.shape[0] // count) + block.shape[1:])

    def own(target):
        return lax.dynamic_index_in_dim(view, target % ring, 1, keepdims=False).astype(jnp.float32)

    plus_steps = ring // 2
    minus_steps = ring - 1 - plus_steps
    total = own(place)
    outgoing = own(place + plus_steps).astype(block.dtype)
    for step in range(1, plus_steps + 1):
        incoming = lax.ppermute(outgoing, axis, plus).astype(jnp.float32)
        if step < plus_steps:
            outgoing = (incoming + own(place + plus_steps - step)).astype(block.dtype)
        else:
            total = total + incoming
    outgoing = own(place + ring - minus_steps).astype(block.dtype)
    for step in range(1, minus_steps + 1):
        incoming = lax.ppermute(outgoing, axis, minus).astype(jnp.float32)
        if step < minus_steps:
            outgoing = (incoming + own(place + ring - minus_steps + step)).astype(block.dtype)
        else:
            total = total + incoming
    sent = lax.dynamic_index_in_dim(total, 1 - pair_index, 0, keepdims=False)
    kept = lax.dynamic_index_in_dim(total, pair_index, 0, keepdims=False)
    return kept + lax.ppermute(sent.astype(block.dtype), axis, across).astype(jnp.float32)


def intersection_weights(span_start, span_end, span_lengths, first_position, position_count):
    byte_first = (first_position + jnp.arange(position_count, dtype=jnp.int32)) * STRIDE
    lower_edge = jnp.maximum(span_start[:, None], byte_first[None, :])
    upper_edge = jnp.minimum(span_end[:, None], byte_first[None, :] + STRIDE)
    covered = jnp.maximum(upper_edge - lower_edge, 0).astype(jnp.float32)
    return (covered / span_lengths[:, None].astype(jnp.float32)).astype(jnp.bfloat16)


def local(byte_acts, conv_weight, conv_bias, proj_weight, teacher, span_lengths):
    byte_rows = byte_acts[0]
    row_total, width = byte_rows.shape
    groups_here = conv_weight.shape[0]
    group_width = width // groups_here
    positions = row_total // STRIDE
    seq_count = lax.axis_size("seq")
    seq_rank = lax.axis_index("seq")
    lengths_doc = span_lengths[0]
    tokens_all = lengths_doc.shape[0]
    span_end = jnp.cumsum(lengths_doc)
    span_start = span_end - lengths_doc
    next_rows = shifted(byte_rows[:STRIDE], "seq", -1)
    extended = jnp.concatenate([byte_rows, next_rows], axis=0)
    blocks = extended.reshape(positions + 1, STRIDE, groups_here, group_width)
    windows = jnp.concatenate([blocks[:-1], blocks[1:]], axis=1)
    taps_weight = conv_weight.reshape(groups_here, KERNEL, group_width, group_width)
    conv_out = jnp.einsum(
        "pkgc,gkco->pgo", windows, taps_weight, preferred_element_type=jnp.float32
    )
    conv_out = conv_out + conv_bias.reshape(groups_here, group_width)[None]
    downsampled = conv_out.reshape(positions, width).astype(jnp.bfloat16)
    local_weight = intersection_weights(
        span_start, span_end, lengths_doc, seq_rank * positions, positions
    )
    tokens_here = tokens_all // seq_count
    own_start = lax.dynamic_slice_in_dim(span_start, seq_rank * tokens_here, tokens_here)
    own_end = lax.dynamic_slice_in_dim(span_end, seq_rank * tokens_here, tokens_here)
    own_lengths = lax.dynamic_slice_in_dim(lengths_doc, seq_rank * tokens_here, tokens_here)
    token_weight = intersection_weights(own_start, own_end, own_lengths, 0, positions * seq_count)
    down_all = shard_gather(downsampled, "seq")
    pooled_sum = jnp.dot(token_weight, down_all, preferred_element_type=jnp.float32).astype(
        jnp.bfloat16
    )
    ring = TENSOR_RING
    gathered = tensor_gather(pooled_sum, "tensor", ring)
    predicted = jnp.dot(gathered, proj_weight, preferred_element_type=jnp.float32)
    err_grad = (predicted - teacher[0].astype(jnp.float32)).astype(jnp.bfloat16)
    proj_local = lax.dot_general(
        gathered, err_grad, (((0,), (0,)), ((), ())), preferred_element_type=jnp.float32
    )
    token_scale = 1.0 / jnp.sqrt(jnp.float32(lax.axis_size("dp") * tokens_all))
    proj_summed = permute_psum(proj_local.astype(jnp.bfloat16), ("dp", "seq")).astype(jnp.float32)
    proj_grad = proj_summed * token_scale
    half = tokens_here // 2
    grad_blocks = [
        lax.dot_general(
            proj_weight, err_part, (((1,), (1,)), ((), ())), preferred_element_type=jnp.float32
        ).astype(jnp.bfloat16)
        for err_part in (err_grad[:half], err_grad[half:])
    ]
    pooled_grad_t = jnp.concatenate(
        [
            lax.psum_scatter(grad_blocks[0], "tensor", scatter_dimension=0, tiled=True),
            tensor_scatter(grad_blocks[1], "tensor", ring).astype(jnp.bfloat16),
        ],
        axis=1,
    )
    weight_part = local_weight
    down_sum = lax.dot_general(
        weight_part,
        lax.all_gather(pooled_grad_t, "seq", axis=1, tiled=True),
        (((0,), (1,)), ((), ())),
        preferred_element_type=jnp.float32,
    )
    down_grad = down_sum.astype(jnp.bfloat16).reshape(positions, groups_here, group_width)
    conv_local = jnp.einsum(
        "pkgc,pgo->gkco", windows, down_grad, preferred_element_type=jnp.float32
    )
    conv_flat = conv_local.astype(jnp.bfloat16).reshape(KERNEL * groups_here * group_width, group_width)
    conv_summed = (
        exchange_psum(conv_flat, ("dp", "seq"))
        .reshape(conv_local.shape)
        .astype(jnp.float32)
    )
    position_scale = 1.0 / jnp.sqrt(jnp.float32(lax.axis_size("dp") * positions * seq_count))
    conv_grad = (conv_summed * position_scale).reshape(
        groups_here, KERNEL * group_width, group_width
    )
    window_grad = jnp.einsum(
        "pgo,gkco->pkgc", down_grad, taps_weight, preferred_element_type=jnp.float32
    )
    incoming = shifted(window_grad[-1, STRIDE:], "seq", 1)
    carried_grad = jnp.concatenate([incoming[None], window_grad[:-1, STRIDE:]], axis=0)
    byte_grad = (
        (window_grad[:, :STRIDE] + carried_grad).reshape(row_total, width).astype(jnp.bfloat16)
    )
    return (downsampled[None], byte_grad[None], conv_grad, proj_grad)


def solution(mesh):
    return jax.shard_map(
        local,
        mesh=mesh,
        in_specs=(
            P("dp", "seq", "tensor"),
            P("tensor", None, None),
            P("tensor"),
            P(None, "tensor"),
            P("dp", "seq", "tensor"),
            P("dp", None),
        ),
        out_specs=(
            P("dp", "seq", "tensor"),
            P("dp", "seq", "tensor"),
            P("tensor", None, None),
            P(None, "tensor"),
        ),
        check_vma=False,
    )
```

```python
import jax
import jax.numpy as jnp
from jax import lax
from jax.sharding import PartitionSpec as P

STRIDE = 4
KERNEL = 8
TENSOR_RING = 8


def shifted(block, axis, distance):
    devices = range(lax.axis_size(axis))
    route = [(i - distance, i) for i in devices if i - distance in devices]
    return lax.ppermute(block, axis, route)


def shard_sum(block, axis):
    count = lax.axis_size(axis)
    rank = lax.axis_index(axis)
    pieces = block.reshape((count, block.shape[0] // count) + block.shape[1:])
    total = lax.dynamic_index_in_dim(pieces, rank, 0, keepdims=False).astype(jnp.float32)
    for distance in range(1, count):
        route = [(i, (i + distance) % count) for i in range(count)]
        outgoing = lax.dynamic_index_in_dim(pieces, (rank + distance) % count, 0, keepdims=False)
        total = total + lax.ppermute(outgoing, axis, route).astype(jnp.float32)
    return total


def shard_gather(piece, axis):
    count = lax.axis_size(axis)
    rank = lax.axis_index(axis)
    rows = piece.shape[0]
    gathered = jnp.zeros((count * rows,) + piece.shape[1:], piece.dtype)
    gathered = lax.dynamic_update_slice_in_dim(gathered, piece, rank * rows, 0)
    for distance in range(1, count):
        route = [(i, (i + distance) % count) for i in range(count)]
        incoming = lax.ppermute(piece, axis, route)
        source = (rank + count - distance) % count
        gathered = lax.dynamic_update_slice_in_dim(gathered, incoming, source * rows, 0)
    return gathered


def exchange_psum(block, axes):
    summed = block
    for axis in axes:
        count = lax.axis_size(axis)
        rank = lax.axis_index(axis)
        slots = jnp.zeros((count,) + block.shape, block.dtype)
        slots = lax.dynamic_update_index_in_dim(slots, summed, rank, 0)
        for distance in range(1, count):
            route = [(i, (i + distance) % count) for i in range(count)]
            incoming = lax.ppermute(summed, axis, route)
            slots = lax.dynamic_update_index_in_dim(slots, incoming, (rank + count - distance) % count, 0)
        summed = jnp.sum(slots.astype(jnp.float32), axis=0).astype(block.dtype)
    return summed


def permute_psum(block, axes):
    summed = block
    for axis in axes:
        summed = shard_sum(summed, axis).astype(block.dtype)
    for axis in axes[:0:-1]:
        summed = shard_gather(summed, axis)
    return summed


def ring_routes(count, ring):
    def device(pair, place):
        return pair * ring + place % ring
    pairs = count // ring
    plus = [(device(a, b), device(a, b + 1)) for a in range(pairs) for b in range(ring)]
    minus = [(device(a, b), device(a, b - 1)) for a in range(pairs) for b in range(ring)]
    across = [(i, (i + ring) % count) for i in range(count)]
    return plus, minus, across


def tensor_gather(piece, axis, ring):
    count = lax.axis_size(axis)
    rank = lax.axis_index(axis)
    pair_index = rank // ring
    place = rank % ring
    plus, minus, across = ring_routes(count, ring)
    other = lax.ppermute(piece, axis, across)
    pair = jnp.where(pair_index == 0, jnp.stack([piece, other]), jnp.stack([other, piece]))
    slots = jnp.zeros((ring,) + pair.shape, pair.dtype)
    slots = lax.dynamic_update_index_in_dim(slots, pair, place, 0)
    forward = pair
    backward = pair
    plus_steps = ring // 2
    minus_steps = ring - 1 - plus_steps
    for step in range(1, plus_steps + 1):
        forward = lax.ppermute(forward, axis, plus)
        slots = lax.dynamic_update_index_in_dim(slots, forward, (place + ring - step) % ring, 0)
        if step <= minus_steps:
            backward = lax.ppermute(backward, axis, minus)
            slots = lax.dynamic_update_index_in_dim(slots, backward, (place + step) % ring, 0)
    rows, width = piece.shape
    return slots.transpose(2, 1, 0, 3).reshape(rows, count * width)


def tensor_scatter(block, axis, ring):
    count = lax.axis_size(axis)
    rank = lax.axis_index(axis)
    pair_index = rank // ring
    place = rank % ring
    plus, minus, across = ring_routes(count, ring)
    view = block.reshape((count // ring, ring, block.shape[0] // count) + block.shape[1:])

    def own(target):
        return lax.dynamic_index_in_dim(view, target % ring, 1, keepdims=False).astype(jnp.float32)

    plus_steps = ring // 2
    minus_steps = ring - 1 - plus_steps
    total = own(place)
    outgoing = own(place + plus_steps).astype(block.dtype)
    for step in range(1, plus_steps + 1):
        incoming = lax.ppermute(outgoing, axis, plus).astype(jnp.float32)
        if step < plus_steps:
            outgoing = (incoming + own(place + plus_steps - step)).astype(block.dtype)
        else:
            total = total + incoming
    outgoing = own(place + ring - minus_steps).astype(block.dtype)
    for step in range(1, minus_steps + 1):
        incoming = lax.ppermute(outgoing, axis, minus).astype(jnp.float32)
        if step < minus_steps:
            outgoing = (incoming + own(place + ring - minus_steps + step)).astype(block.dtype)
        else:
            total = total + incoming
    sent = lax.dynamic_index_in_dim(total, 1 - pair_index, 0, keepdims=False)
    kept = lax.dynamic_index_in_dim(total, pair_index, 0, keepdims=False)
    return kept + lax.ppermute(sent.astype(block.dtype), axis, across).astype(jnp.float32)


def intersection_weights(span_start, span_end, span_lengths, first_position, position_count):
    byte_first = (first_position + jnp.arange(position_count, dtype=jnp.int32)) * STRIDE
    lower_edge = jnp.maximum(span_start[:, None], byte_first[None, :])
    upper_edge = jnp.minimum(span_end[:, None], byte_first[None, :] + STRIDE)
    covered = jnp.maximum(upper_edge - lower_edge, 0).astype(jnp.float32)
    return (covered / span_lengths[:, None].astype(jnp.float32)).astype(jnp.bfloat16)


def local(byte_acts, conv_weight, conv_bias, proj_weight, teacher, span_lengths):
    byte_rows = byte_acts[0]
    row_total, width = byte_rows.shape
    groups_here = conv_weight.shape[0]
    group_width = width // groups_here
    positions = row_total // STRIDE
    seq_count = lax.axis_size("seq")
    seq_rank = lax.axis_index("seq")
    lengths_doc = span_lengths[0]
    tokens_all = lengths_doc.shape[0]
    span_end = jnp.cumsum(lengths_doc)
    span_start = span_end - lengths_doc
    next_rows = shifted(byte_rows[:STRIDE], "seq", -1)
    extended = jnp.concatenate([byte_rows, next_rows], axis=0)
    blocks = extended.reshape(positions + 1, STRIDE, groups_here, group_width)
    windows = jnp.concatenate([blocks[:-1], blocks[1:]], axis=1)
    taps_weight = conv_weight.reshape(groups_here, KERNEL, group_width, group_width)
    conv_out = jnp.einsum(
        "pkgc,gkco->pgo", windows, taps_weight, preferred_element_type=jnp.float32
    )
    conv_out = conv_out + conv_bias.reshape(groups_here, group_width)[None]
    downsampled = conv_out.reshape(positions, width).astype(jnp.bfloat16)
    local_weight = intersection_weights(
        span_start, span_end, lengths_doc, seq_rank * positions, positions
    )
    tokens_here = tokens_all // seq_count
    own_start = lax.dynamic_slice_in_dim(span_start, seq_rank * tokens_here, tokens_here)
    own_end = lax.dynamic_slice_in_dim(span_end, seq_rank * tokens_here, tokens_here)
    own_lengths = lax.dynamic_slice_in_dim(lengths_doc, seq_rank * tokens_here, tokens_here)
    token_weight = intersection_weights(own_start, own_end, own_lengths, 0, positions * seq_count)
    down_all = shard_gather(downsampled, "seq")
    pooled_sum = jnp.dot(token_weight, down_all, preferred_element_type=jnp.float32).astype(
        jnp.bfloat16
    )
    ring = TENSOR_RING
    gathered = tensor_gather(pooled_sum, "tensor", ring)
    predicted = jnp.dot(gathered, proj_weight, preferred_element_type=jnp.float32)
    err_grad = (predicted - teacher[0].astype(jnp.float32)).astype(jnp.bfloat16)
    proj_local = lax.dot_general(
        gathered, err_grad, (((0,), (0,)), ((), ())), preferred_element_type=jnp.float32
    )
    token_scale = 1.0 / jnp.sqrt(jnp.float32(lax.axis_size("dp") * tokens_all))
    proj_partial = permute_psum(proj_local.astype(jnp.bfloat16), ("dp", "seq"))
    half = tokens_here // 2
    grad_blocks = [
        lax.dot_general(
            proj_weight, err_part, (((1,), (1,)), ((), ())), preferred_element_type=jnp.float32
        ).astype(jnp.bfloat16)
        for err_part in (err_grad[:half], err_grad[half:])
    ]
    pooled_grad_t = jnp.concatenate(
        [
            lax.psum_scatter(grad_blocks[0], "tensor", scatter_dimension=0, tiled=True),
            tensor_scatter(grad_blocks[1], "tensor", ring).astype(jnp.bfloat16),
        ],
        axis=1,
    )
    weight_part = local_weight
    down_sum = lax.dot_general(
        weight_part,
        lax.all_gather(pooled_grad_t, "seq", axis=1, tiled=True),
        (((0,), (1,)), ((), ())),
        preferred_element_type=jnp.float32,
    )
    down_sum, proj_partial = lax.optimization_barrier((down_sum, proj_partial))
    proj_summed = shard_gather(proj_partial, "dp").astype(jnp.float32)
    proj_grad = proj_summed * token_scale
    down_grad = down_sum.astype(jnp.bfloat16).reshape(positions, groups_here, group_width)
    conv_local = jnp.einsum(
        "pkgc,pgo->gkco", windows, down_grad, preferred_element_type=jnp.float32
    )
    conv_flat = conv_local.astype(jnp.bfloat16).reshape(KERNEL * groups_here * group_width, group_width)
    conv_summed = (
        exchange_psum(conv_flat, ("dp", "seq"))
        .reshape(conv_local.shape)
        .astype(jnp.float32)
    )
    position_scale = 1.0 / jnp.sqrt(jnp.float32(lax.axis_size("dp") * positions * seq_count))
    conv_grad = (conv_summed * position_scale).reshape(
        groups_here, KERNEL * group_width, group_width
    )
    window_grad = jnp.einsum(
        "pgo,gkco->pkgc", down_grad, taps_weight, preferred_element_type=jnp.float32
    )
    incoming = shifted(window_grad[-1, STRIDE:], "seq", 1)
    carried_grad = jnp.concatenate([incoming[None], window_grad[:-1, STRIDE:]], axis=0)
    byte_grad = (
        (window_grad[:, :STRIDE] + carried_grad).reshape(row_total, width).astype(jnp.bfloat16)
    )
    return (downsampled[None], byte_grad[None], conv_grad, proj_grad)


def solution(mesh):
    return jax.shard_map(
        local,
        mesh=mesh,
        in_specs=(
            P("dp", "seq", "tensor"),
            P("tensor", None, None),
            P("tensor"),
            P(None, "tensor"),
            P("dp", "seq", "tensor"),
            P("dp", None),
        ),
        out_specs=(
            P("dp", "seq", "tensor"),
            P("dp", "seq", "tensor"),
            P("tensor", None, None),
            P(None, "tensor"),
        ),
        check_vma=False,
    )
```

```python
import jax
import jax.numpy as jnp
from jax import lax
from jax.sharding import PartitionSpec as P

STRIDE = 4
KERNEL = 8
TENSOR_RING = 8


def shifted(block, axis, distance):
    devices = range(lax.axis_size(axis))
    route = [(i - distance, i) for i in devices if i - distance in devices]
    return lax.ppermute(block, axis, route)


def shard_sum(block, axis):
    count = lax.axis_size(axis)
    rank = lax.axis_index(axis)
    pieces = block.reshape((count, block.shape[0] // count) + block.shape[1:])
    total = lax.dynamic_index_in_dim(pieces, rank, 0, keepdims=False).astype(jnp.float32)
    for distance in range(1, count):
        route = [(i, (i + distance) % count) for i in range(count)]
        outgoing = lax.dynamic_index_in_dim(pieces, (rank + distance) % count, 0, keepdims=False)
        total = total + lax.ppermute(outgoing, axis, route).astype(jnp.float32)
    return total


def shard_gather(piece, axis):
    count = lax.axis_size(axis)
    rank = lax.axis_index(axis)
    rows = piece.shape[0]
    gathered = jnp.zeros((count * rows,) + piece.shape[1:], piece.dtype)
    gathered = lax.dynamic_update_slice_in_dim(gathered, piece, rank * rows, 0)
    for distance in range(1, count):
        route = [(i, (i + distance) % count) for i in range(count)]
        incoming = lax.ppermute(piece, axis, route)
        source = (rank + count - distance) % count
        gathered = lax.dynamic_update_slice_in_dim(gathered, incoming, source * rows, 0)
    return gathered


def exchange_psum(block, axes):
    summed = block
    for axis in axes:
        count = lax.axis_size(axis)
        rank = lax.axis_index(axis)
        slots = jnp.zeros((count,) + block.shape, block.dtype)
        slots = lax.dynamic_update_index_in_dim(slots, summed, rank, 0)
        for distance in range(1, count):
            route = [(i, (i + distance) % count) for i in range(count)]
            incoming = lax.ppermute(summed, axis, route)
            slots = lax.dynamic_update_index_in_dim(slots, incoming, (rank + count - distance) % count, 0)
        summed = jnp.sum(slots.astype(jnp.float32), axis=0).astype(block.dtype)
    return summed


def permute_psum(block, axes):
    summed = block
    for axis in axes:
        summed = shard_sum(summed, axis).astype(block.dtype)
    for axis in axes[::-1]:
        summed = shard_gather(summed, axis)
    return summed


def ring_routes(count, ring):
    def device(pair, place):
        return pair * ring + place % ring
    pairs = count // ring
    plus = [(device(a, b), device(a, b + 1)) for a in range(pairs) for b in range(ring)]
    minus = [(device(a, b), device(a, b - 1)) for a in range(pairs) for b in range(ring)]
    across = [(i, (i + ring) % count) for i in range(count)]
    return plus, minus, across


def tensor_gather(piece, axis, ring):
    count = lax.axis_size(axis)
    rank = lax.axis_index(axis)
    pair_index = rank // ring
    place = rank % ring
    plus, minus, across = ring_routes(count, ring)
    other = lax.ppermute(piece, axis, across)
    pair = jnp.where(pair_index == 0, jnp.stack([piece, other]), jnp.stack([other, piece]))
    slots = jnp.zeros((ring,) + pair.shape, pair.dtype)
    slots = lax.dynamic_update_index_in_dim(slots, pair, place, 0)
    forward = pair
    backward = pair
    full_steps = (ring - 1) // 2
    for step in range(1, full_steps + 1):
        forward = lax.ppermute(forward, axis, plus)
        slots = lax.dynamic_update_index_in_dim(slots, forward, (place + ring - step) % ring, 0)
        backward = lax.ppermute(backward, axis, minus)
        slots = lax.dynamic_update_index_in_dim(slots, backward, (place + step) % ring, 0)
    if ring % 2 == 0:
        rows_half = pair.shape[1] // 2
        far = (place + ring // 2) % ring
        front = lax.ppermute(forward[:, :rows_half], axis, plus)
        back = lax.ppermute(backward[:, rows_half:], axis, minus)
        slots = lax.dynamic_update_index_in_dim(
            slots, jnp.concatenate([front, back], axis=1), far, 0
        )
    rows, width = piece.shape
    return slots.transpose(2, 1, 0, 3).reshape(rows, count * width)


def tensor_scatter(block, axis, ring):
    count = lax.axis_size(axis)
    rank = lax.axis_index(axis)
    pair_index = rank // ring
    place = rank % ring
    plus, minus, across = ring_routes(count, ring)
    view = block.reshape((count // ring, ring, block.shape[0] // count) + block.shape[1:])

    def own(target):
        return lax.dynamic_index_in_dim(view, target % ring, 1, keepdims=False).astype(jnp.float32)

    plus_steps = ring // 2
    minus_steps = ring - 1 - plus_steps
    total = own(place)
    outgoing = own(place + plus_steps).astype(block.dtype)
    for step in range(1, plus_steps + 1):
        incoming = lax.ppermute(outgoing, axis, plus).astype(jnp.float32)
        if step < plus_steps:
            outgoing = (incoming + own(place + plus_steps - step)).astype(block.dtype)
        else:
            total = total + incoming
    outgoing = own(place + ring - minus_steps).astype(block.dtype)
    for step in range(1, minus_steps + 1):
        incoming = lax.ppermute(outgoing, axis, minus).astype(jnp.float32)
        if step < minus_steps:
            outgoing = (incoming + own(place + ring - minus_steps + step)).astype(block.dtype)
        else:
            total = total + incoming
    sent = lax.dynamic_index_in_dim(total, 1 - pair_index, 0, keepdims=False)
    kept = lax.dynamic_index_in_dim(total, pair_index, 0, keepdims=False)
    return kept + lax.ppermute(sent.astype(block.dtype), axis, across).astype(jnp.float32)


def intersection_weights(span_start, span_end, span_lengths, first_position, position_count):
    byte_first = (first_position + jnp.arange(position_count, dtype=jnp.int32)) * STRIDE
    lower_edge = jnp.maximum(span_start[:, None], byte_first[None, :])
    upper_edge = jnp.minimum(span_end[:, None], byte_first[None, :] + STRIDE)
    covered = jnp.maximum(upper_edge - lower_edge, 0).astype(jnp.float32)
    return (covered / span_lengths[:, None].astype(jnp.float32)).astype(jnp.bfloat16)


def local(byte_acts, conv_weight, conv_bias, proj_weight, teacher, span_lengths):
    byte_rows = byte_acts[0]
    row_total, width = byte_rows.shape
    groups_here = conv_weight.shape[0]
    group_width = width // groups_here
    positions = row_total // STRIDE
    seq_count = lax.axis_size("seq")
    seq_rank = lax.axis_index("seq")
    lengths_doc = span_lengths[0]
    tokens_all = lengths_doc.shape[0]
    span_end = jnp.cumsum(lengths_doc)
    span_start = span_end - lengths_doc
    next_rows = shifted(byte_rows[:STRIDE], "seq", -1)
    extended = jnp.concatenate([byte_rows, next_rows], axis=0)
    blocks = extended.reshape(positions + 1, STRIDE, groups_here, group_width)
    windows = jnp.concatenate([blocks[:-1], blocks[1:]], axis=1)
    taps_weight = conv_weight.reshape(groups_here, KERNEL, group_width, group_width)
    conv_out = jnp.einsum(
        "pkgc,gkco->pgo", windows, taps_weight, preferred_element_type=jnp.float32
    )
    conv_out = conv_out + conv_bias.reshape(groups_here, group_width)[None]
    downsampled = conv_out.reshape(positions, width).astype(jnp.bfloat16)
    local_weight = intersection_weights(
        span_start, span_end, lengths_doc, seq_rank * positions, positions
    )
    tokens_here = tokens_all // seq_count
    own_start = lax.dynamic_slice_in_dim(span_start, seq_rank * tokens_here, tokens_here)
    own_end = lax.dynamic_slice_in_dim(span_end, seq_rank * tokens_here, tokens_here)
    own_lengths = lax.dynamic_slice_in_dim(lengths_doc, seq_rank * tokens_here, tokens_here)
    token_weight = intersection_weights(own_start, own_end, own_lengths, 0, positions * seq_count)
    down_all = shard_gather(downsampled, "seq")
    pooled_sum = jnp.dot(token_weight, down_all, preferred_element_type=jnp.float32).astype(
        jnp.bfloat16
    )
    ring = TENSOR_RING
    gathered = tensor_gather(pooled_sum, "tensor", ring)
    predicted = jnp.dot(gathered, proj_weight, preferred_element_type=jnp.float32)
    err_grad = (predicted - teacher[0].astype(jnp.float32)).astype(jnp.bfloat16)
    proj_local = lax.dot_general(
        gathered, err_grad, (((0,), (0,)), ((), ())), preferred_element_type=jnp.float32
    )
    token_scale = 1.0 / jnp.sqrt(jnp.float32(lax.axis_size("dp") * tokens_all))
    proj_summed = permute_psum(proj_local.astype(jnp.bfloat16), ("dp", "seq")).astype(jnp.float32)
    proj_grad = proj_summed * token_scale
    half = tokens_here // 2
    grad_blocks = [
        lax.dot_general(
            proj_weight, err_part, (((1,), (1,)), ((), ())), preferred_element_type=jnp.float32
        ).astype(jnp.bfloat16)
        for err_part in (err_grad[:half], err_grad[half:])
    ]
    pooled_grad_t = jnp.concatenate(
        [
            lax.psum_scatter(grad_blocks[0], "tensor", scatter_dimension=0, tiled=True),
            tensor_scatter(grad_blocks[1], "tensor", ring).astype(jnp.bfloat16),
        ],
        axis=1,
    )
    weight_part = local_weight
    down_sum = lax.dot_general(
        weight_part,
        lax.all_gather(pooled_grad_t, "seq", axis=1, tiled=True),
        (((0,), (1,)), ((), ())),
        preferred_element_type=jnp.float32,
    )
    down_grad = down_sum.astype(jnp.bfloat16).reshape(positions, groups_here, group_width)
    conv_local = jnp.einsum(
        "pkgc,pgo->gkco", windows, down_grad, preferred_element_type=jnp.float32
    )
    conv_flat = conv_local.astype(jnp.bfloat16).reshape(KERNEL * groups_here * group_width, group_width)
    conv_summed = (
        exchange_psum(conv_flat, ("dp", "seq"))
        .reshape(conv_local.shape)
        .astype(jnp.float32)
    )
    position_scale = 1.0 / jnp.sqrt(jnp.float32(lax.axis_size("dp") * positions * seq_count))
    conv_grad = (conv_summed * position_scale).reshape(
        groups_here, KERNEL * group_width, group_width
    )
    window_grad = jnp.einsum(
        "pgo,gkco->pkgc", down_grad, taps_weight, preferred_element_type=jnp.float32
    )
    incoming = shifted(window_grad[-1, STRIDE:], "seq", 1)
    carried_grad = jnp.concatenate([incoming[None], window_grad[:-1, STRIDE:]], axis=0)
    byte_grad = (
        (window_grad[:, :STRIDE] + carried_grad).reshape(row_total, width).astype(jnp.bfloat16)
    )
    return (downsampled[None], byte_grad[None], conv_grad, proj_grad)


def solution(mesh):
    return jax.shard_map(
        local,
        mesh=mesh,
        in_specs=(
            P("dp", "seq", "tensor"),
            P("tensor", None, None),
            P("tensor"),
            P(None, "tensor"),
            P("dp", "seq", "tensor"),
            P("dp", None),
        ),
        out_specs=(
            P("dp", "seq", "tensor"),
            P("dp", "seq", "tensor"),
            P("tensor", None, None),
            P(None, "tensor"),
        ),
        check_vma=False,
    )
```

```python
import jax
import jax.numpy as jnp
from jax import lax
from jax.sharding import PartitionSpec as P

STRIDE = 4
KERNEL = 8
TENSOR_RING = 8


def shifted(block, axis, distance):
    devices = range(lax.axis_size(axis))
    route = [(i - distance, i) for i in devices if i - distance in devices]
    return lax.ppermute(block, axis, route)


def shard_sum(block, axis):
    count = lax.axis_size(axis)
    rank = lax.axis_index(axis)
    pieces = block.reshape((count, block.shape[0] // count) + block.shape[1:])
    total = lax.dynamic_index_in_dim(pieces, rank, 0, keepdims=False).astype(jnp.float32)
    for distance in range(1, count):
        route = [(i, (i + distance) % count) for i in range(count)]
        outgoing = lax.dynamic_index_in_dim(pieces, (rank + distance) % count, 0, keepdims=False)
        total = total + lax.ppermute(outgoing, axis, route).astype(jnp.float32)
    return total


def shard_gather(piece, axis):
    count = lax.axis_size(axis)
    rank = lax.axis_index(axis)
    rows = piece.shape[0]
    gathered = jnp.zeros((count * rows,) + piece.shape[1:], piece.dtype)
    gathered = lax.dynamic_update_slice_in_dim(gathered, piece, rank * rows, 0)
    for distance in range(1, count):
        route = [(i, (i + distance) % count) for i in range(count)]
        incoming = lax.ppermute(piece, axis, route)
        source = (rank + count - distance) % count
        gathered = lax.dynamic_update_slice_in_dim(gathered, incoming, source * rows, 0)
    return gathered


def exchange_psum(block, axes):
    summed = block
    for axis in axes:
        count = lax.axis_size(axis)
        rank = lax.axis_index(axis)
        slots = jnp.zeros((count,) + block.shape, block.dtype)
        slots = lax.dynamic_update_index_in_dim(slots, summed, rank, 0)
        for distance in range(1, count):
            route = [(i, (i + distance) % count) for i in range(count)]
            incoming = lax.ppermute(summed, axis, route)
            slots = lax.dynamic_update_index_in_dim(slots, incoming, (rank + count - distance) % count, 0)
        summed = jnp.sum(slots.astype(jnp.float32), axis=0).astype(block.dtype)
    return summed


def permute_psum(block, axes):
    summed = block
    for axis in axes:
        summed = shard_sum(summed, axis).astype(block.dtype)
    for axis in axes[::-1]:
        summed = shard_gather(summed, axis)
    return summed


def ring_routes(count, ring):
    def device(pair, place):
        return pair * ring + place % ring
    pairs = count // ring
    plus = [(device(a, b), device(a, b + 1)) for a in range(pairs) for b in range(ring)]
    minus = [(device(a, b), device(a, b - 1)) for a in range(pairs) for b in range(ring)]
    across = [(i, (i + ring) % count) for i in range(count)]
    return plus, minus, across


def tensor_gather(piece, axis, ring):
    count = lax.axis_size(axis)
    rank = lax.axis_index(axis)
    pair_index = rank // ring
    place = rank % ring
    plus, minus, across = ring_routes(count, ring)
    other = lax.ppermute(piece, axis, across)
    pair = jnp.where(pair_index == 0, jnp.stack([piece, other]), jnp.stack([other, piece]))
    slots = jnp.zeros((ring,) + pair.shape, pair.dtype)
    slots = lax.dynamic_update_index_in_dim(slots, pair, place, 0)
    forward = pair
    backward = pair
    full_steps = (ring - 1) // 2
    for step in range(1, full_steps + 1):
        forward = lax.ppermute(forward, axis, plus)
        slots = lax.dynamic_update_index_in_dim(slots, forward, (place + ring - step) % ring, 0)
        backward = lax.ppermute(backward, axis, minus)
        slots = lax.dynamic_update_index_in_dim(slots, backward, (place + step) % ring, 0)
    if ring % 2 == 0:
        rows_half = pair.shape[1] // 2
        far = (place + ring // 2) % ring
        front = lax.ppermute(forward[:, :rows_half], axis, plus)
        back = lax.ppermute(backward[:, rows_half:], axis, minus)
        slots = lax.dynamic_update_index_in_dim(
            slots, jnp.concatenate([front, back], axis=1), far, 0
        )
    rows, width = piece.shape
    return slots.transpose(2, 1, 0, 3).reshape(rows, count * width)


def tensor_scatter(block, axis, ring):
    count = lax.axis_size(axis)
    rank = lax.axis_index(axis)
    pair_index = rank // ring
    place = rank % ring
    plus, minus, across = ring_routes(count, ring)
    view = block.reshape((count // ring, ring, block.shape[0] // count) + block.shape[1:])

    def own(target):
        return lax.dynamic_index_in_dim(view, target % ring, 1, keepdims=False).astype(jnp.float32)

    plus_steps = ring // 2
    minus_steps = ring - 1 - plus_steps
    total = own(place)
    outgoing = own(place + plus_steps).astype(block.dtype)
    for step in range(1, plus_steps + 1):
        incoming = lax.ppermute(outgoing, axis, plus).astype(jnp.float32)
        if step < plus_steps:
            outgoing = (incoming + own(place + plus_steps - step)).astype(block.dtype)
        else:
            total = total + incoming
    outgoing = own(place + ring - minus_steps).astype(block.dtype)
    for step in range(1, minus_steps + 1):
        incoming = lax.ppermute(outgoing, axis, minus).astype(jnp.float32)
        if step < minus_steps:
            outgoing = (incoming + own(place + ring - minus_steps + step)).astype(block.dtype)
        else:
            total = total + incoming
    sent = lax.dynamic_index_in_dim(total, 1 - pair_index, 0, keepdims=False)
    kept = lax.dynamic_index_in_dim(total, pair_index, 0, keepdims=False)
    return kept + lax.ppermute(sent.astype(block.dtype), axis, across).astype(jnp.float32)


def intersection_weights(span_start, span_end, span_lengths, first_position, position_count):
    byte_first = (first_position + jnp.arange(position_count, dtype=jnp.int32)) * STRIDE
    lower_edge = jnp.maximum(span_start[:, None], byte_first[None, :])
    upper_edge = jnp.minimum(span_end[:, None], byte_first[None, :] + STRIDE)
    covered = jnp.maximum(upper_edge - lower_edge, 0).astype(jnp.float32)
    inverse_length = 1.0 / span_lengths.astype(jnp.float32)
    return (covered * inverse_length[:, None]).astype(jnp.bfloat16)


def local(byte_acts, conv_weight, conv_bias, proj_weight, teacher, span_lengths):
    byte_rows = byte_acts[0]
    row_total, width = byte_rows.shape
    groups_here = conv_weight.shape[0]
    group_width = width // groups_here
    positions = row_total // STRIDE
    seq_count = lax.axis_size("seq")
    seq_rank = lax.axis_index("seq")
    lengths_doc = span_lengths[0]
    tokens_all = lengths_doc.shape[0]
    span_end = jnp.cumsum(lengths_doc)
    span_start = span_end - lengths_doc
    next_rows = shifted(byte_rows[:STRIDE], "seq", -1)
    extended = jnp.concatenate([byte_rows, next_rows], axis=0)
    blocks = extended.reshape(positions + 1, STRIDE, groups_here, group_width)
    windows = jnp.concatenate([blocks[:-1], blocks[1:]], axis=1)
    taps_weight = conv_weight.reshape(groups_here, KERNEL, group_width, group_width)
    conv_out = jnp.einsum(
        "pkgc,gkco->pgo", windows, taps_weight, preferred_element_type=jnp.float32
    )
    conv_out = conv_out + conv_bias.reshape(groups_here, group_width)[None]
    downsampled = conv_out.reshape(positions, width).astype(jnp.bfloat16)
    local_weight = intersection_weights(
        span_start, span_end, lengths_doc, seq_rank * positions, positions
    )
    tokens_here = tokens_all // seq_count
    own_start = lax.dynamic_slice_in_dim(span_start, seq_rank * tokens_here, tokens_here)
    own_end = lax.dynamic_slice_in_dim(span_end, seq_rank * tokens_here, tokens_here)
    own_lengths = lax.dynamic_slice_in_dim(lengths_doc, seq_rank * tokens_here, tokens_here)
    token_weight = intersection_weights(own_start, own_end, own_lengths, 0, positions * seq_count)
    down_all = shard_gather(downsampled, "seq")
    pooled_sum = jnp.dot(token_weight, down_all, preferred_element_type=jnp.float32).astype(
        jnp.bfloat16
    )
    ring = TENSOR_RING
    gathered = tensor_gather(pooled_sum, "tensor", ring)
    predicted = jnp.dot(gathered, proj_weight, preferred_element_type=jnp.float32)
    err_grad = (predicted - teacher[0].astype(jnp.float32)).astype(jnp.bfloat16)
    proj_local = lax.dot_general(
        gathered, err_grad, (((0,), (0,)), ((), ())), preferred_element_type=jnp.float32
    )
    token_scale = 1.0 / jnp.sqrt(jnp.float32(lax.axis_size("dp") * tokens_all))
    proj_summed = permute_psum(proj_local.astype(jnp.bfloat16), ("dp", "seq")).astype(jnp.float32)
    proj_grad = proj_summed * token_scale
    half = tokens_here // 2
    grad_blocks = [
        lax.dot_general(
            proj_weight, err_part, (((1,), (1,)), ((), ())), preferred_element_type=jnp.float32
        ).astype(jnp.bfloat16)
        for err_part in (err_grad[:half], err_grad[half:])
    ]
    pooled_grad_t = jnp.concatenate(
        [
            lax.psum_scatter(grad_blocks[0], "tensor", scatter_dimension=0, tiled=True),
            tensor_scatter(grad_blocks[1], "tensor", ring).astype(jnp.bfloat16),
        ],
        axis=1,
    )
    weight_part = local_weight
    down_sum = lax.dot_general(
        weight_part,
        lax.all_gather(pooled_grad_t, "seq", axis=1, tiled=True),
        (((0,), (1,)), ((), ())),
        preferred_element_type=jnp.float32,
    )
    down_grad = down_sum.astype(jnp.bfloat16).reshape(positions, groups_here, group_width)
    conv_local = jnp.einsum(
        "pkgc,pgo->gkco", windows, down_grad, preferred_element_type=jnp.float32
    )
    conv_flat = conv_local.astype(jnp.bfloat16).reshape(KERNEL * groups_here * group_width, group_width)
    conv_summed = (
        exchange_psum(conv_flat, ("dp", "seq"))
        .reshape(conv_local.shape)
        .astype(jnp.float32)
    )
    position_scale = 1.0 / jnp.sqrt(jnp.float32(lax.axis_size("dp") * positions * seq_count))
    conv_grad = (conv_summed * position_scale).reshape(
        groups_here, KERNEL * group_width, group_width
    )
    window_grad = jnp.einsum(
        "pgo,gkco->pkgc", down_grad, taps_weight, preferred_element_type=jnp.float32
    )
    incoming = shifted(window_grad[-1, STRIDE:], "seq", 1)
    carried_grad = jnp.concatenate([incoming[None], window_grad[:-1, STRIDE:]], axis=0)
    byte_grad = (
        (window_grad[:, :STRIDE] + carried_grad).reshape(row_total, width).astype(jnp.bfloat16)
    )
    return (downsampled[None], byte_grad[None], conv_grad, proj_grad)


def solution(mesh):
    return jax.shard_map(
        local,
        mesh=mesh,
        in_specs=(
            P("dp", "seq", "tensor"),
            P("tensor", None, None),
            P("tensor"),
            P(None, "tensor"),
            P("dp", "seq", "tensor"),
            P("dp", None),
        ),
        out_specs=(
            P("dp", "seq", "tensor"),
            P("dp", "seq", "tensor"),
            P("tensor", None, None),
            P(None, "tensor"),
        ),
        check_vma=False,
    )
```

```python
import jax
import jax.numpy as jnp
from jax import lax
from jax.sharding import PartitionSpec as P

STRIDE = 4
KERNEL = 8
TENSOR_RING = 8


def shifted(block, axis, distance):
    devices = range(lax.axis_size(axis))
    route = [(i - distance, i) for i in devices if i - distance in devices]
    return lax.ppermute(block, axis, route)


def shard_sum(block, axis):
    count = lax.axis_size(axis)
    rank = lax.axis_index(axis)
    pieces = block.reshape((count, block.shape[0] // count) + block.shape[1:])
    total = lax.dynamic_index_in_dim(pieces, rank, 0, keepdims=False).astype(jnp.float32)
    for distance in range(1, count):
        route = [(i, (i + distance) % count) for i in range(count)]
        outgoing = lax.dynamic_index_in_dim(pieces, (rank + distance) % count, 0, keepdims=False)
        total = total + lax.ppermute(outgoing, axis, route).astype(jnp.float32)
    return total


def shard_gather(piece, axis):
    count = lax.axis_size(axis)
    rank = lax.axis_index(axis)
    rows = piece.shape[0]
    gathered = jnp.zeros((count * rows,) + piece.shape[1:], piece.dtype)
    gathered = lax.dynamic_update_slice_in_dim(gathered, piece, rank * rows, 0)
    for distance in range(1, count):
        route = [(i, (i + distance) % count) for i in range(count)]
        incoming = lax.ppermute(piece, axis, route)
        source = (rank + count - distance) % count
        gathered = lax.dynamic_update_slice_in_dim(gathered, incoming, source * rows, 0)
    return gathered


def exchange_psum(block, axes):
    summed = block
    for axis in axes:
        count = lax.axis_size(axis)
        rank = lax.axis_index(axis)
        slots = jnp.zeros((count,) + block.shape, block.dtype)
        slots = lax.dynamic_update_index_in_dim(slots, summed, rank, 0)
        for distance in range(1, count):
            route = [(i, (i + distance) % count) for i in range(count)]
            incoming = lax.ppermute(summed, axis, route)
            slots = lax.dynamic_update_index_in_dim(slots, incoming, (rank + count - distance) % count, 0)
        summed = jnp.sum(slots.astype(jnp.float32), axis=0).astype(block.dtype)
    return summed


def permute_psum(block, axes):
    summed = block
    for axis in axes:
        summed = shard_sum(summed, axis).astype(block.dtype)
    for axis in axes[::-1]:
        summed = shard_gather(summed, axis)
    return summed


def ring_routes(count, ring):
    def device(pair, place):
        return pair * ring + place % ring
    pairs = count // ring
    plus = [(device(a, b), device(a, b + 1)) for a in range(pairs) for b in range(ring)]
    minus = [(device(a, b), device(a, b - 1)) for a in range(pairs) for b in range(ring)]
    across = [(i, (i + ring) % count) for i in range(count)]
    return plus, minus, across


def tensor_gather(piece, axis, ring):
    count = lax.axis_size(axis)
    rank = lax.axis_index(axis)
    pair_index = rank // ring
    place = rank % ring
    plus, minus, across = ring_routes(count, ring)
    other = lax.ppermute(piece, axis, across)
    pair = jnp.where(pair_index == 0, jnp.stack([piece, other]), jnp.stack([other, piece]))
    slots = jnp.zeros((ring,) + pair.shape, pair.dtype)
    slots = lax.dynamic_update_index_in_dim(slots, pair, place, 0)
    forward = pair
    backward = pair
    full_steps = (ring - 1) // 2
    for step in range(1, full_steps + 1):
        forward = lax.ppermute(forward, axis, plus)
        slots = lax.dynamic_update_index_in_dim(slots, forward, (place + ring - step) % ring, 0)
        backward = lax.ppermute(backward, axis, minus)
        slots = lax.dynamic_update_index_in_dim(slots, backward, (place + step) % ring, 0)
    if ring % 2 == 0:
        rows_half = pair.shape[1] // 2
        far = (place + ring // 2) % ring
        front = lax.ppermute(forward[:, :rows_half], axis, plus)
        back = lax.ppermute(backward[:, rows_half:], axis, minus)
        slots = lax.dynamic_update_index_in_dim(
            slots, jnp.concatenate([front, back], axis=1), far, 0
        )
    rows, width = piece.shape
    return slots.transpose(2, 1, 0, 3).reshape(rows, count * width)


def tensor_gather_late_pair(piece, axis, ring):
    count = lax.axis_size(axis)
    rank = lax.axis_index(axis)
    pair_index = rank // ring
    place = rank % ring
    plus, minus, across = ring_routes(count, ring)
    slots = jnp.zeros((ring,) + piece.shape, piece.dtype)
    slots = lax.dynamic_update_index_in_dim(slots, piece, place, 0)
    forward = piece
    backward = piece
    for step in range(1, (ring - 1) // 2 + 1):
        forward = lax.ppermute(forward, axis, plus)
        slots = lax.dynamic_update_index_in_dim(slots, forward, (place + ring - step) % ring, 0)
        backward = lax.ppermute(backward, axis, minus)
        slots = lax.dynamic_update_index_in_dim(slots, backward, (place + step) % ring, 0)
    if ring % 2 == 0:
        rows_half = piece.shape[0] // 2
        front = lax.ppermute(forward[:rows_half], axis, plus)
        back = lax.ppermute(backward[rows_half:], axis, minus)
        slots = lax.dynamic_update_index_in_dim(
            slots, jnp.concatenate([front, back], axis=0), (place + ring // 2) % ring, 0
        )
    other = lax.ppermute(slots, axis, across)
    pair = jnp.where(pair_index == 0, jnp.stack([slots, other]), jnp.stack([other, slots]))
    rows, width = piece.shape
    return pair.transpose(2, 0, 1, 3).reshape(rows, count * width)


def tensor_scatter(block, axis, ring):
    count = lax.axis_size(axis)
    rank = lax.axis_index(axis)
    pair_index = rank // ring
    place = rank % ring
    plus, minus, across = ring_routes(count, ring)
    view = block.reshape((count // ring, ring, block.shape[0] // count) + block.shape[1:])

    def own(target):
        return lax.dynamic_index_in_dim(view, target % ring, 1, keepdims=False).astype(jnp.float32)

    plus_steps = ring // 2
    minus_steps = ring - 1 - plus_steps
    total = own(place)
    outgoing = own(place + plus_steps).astype(block.dtype)
    for step in range(1, plus_steps + 1):
        incoming = lax.ppermute(outgoing, axis, plus).astype(jnp.float32)
        if step < plus_steps:
            outgoing = (incoming + own(place + plus_steps - step)).astype(block.dtype)
        else:
            total = total + incoming
    outgoing = own(place + ring - minus_steps).astype(block.dtype)
    for step in range(1, minus_steps + 1):
        incoming = lax.ppermute(outgoing, axis, minus).astype(jnp.float32)
        if step < minus_steps:
            outgoing = (incoming + own(place + ring - minus_steps + step)).astype(block.dtype)
        else:
            total = total + incoming
    sent = lax.dynamic_index_in_dim(total, 1 - pair_index, 0, keepdims=False)
    kept = lax.dynamic_index_in_dim(total, pair_index, 0, keepdims=False)
    return kept + lax.ppermute(sent.astype(block.dtype), axis, across).astype(jnp.float32)


def intersection_weights(span_start, span_end, span_lengths, first_position, position_count):
    byte_first = (first_position + jnp.arange(position_count, dtype=jnp.int32)) * STRIDE
    lower_edge = jnp.maximum(span_start[:, None], byte_first[None, :])
    upper_edge = jnp.minimum(span_end[:, None], byte_first[None, :] + STRIDE)
    covered = jnp.maximum(upper_edge - lower_edge, 0).astype(jnp.float32)
    return (covered / span_lengths[:, None].astype(jnp.float32)).astype(jnp.bfloat16)


def local(byte_acts, conv_weight, conv_bias, proj_weight, teacher, span_lengths):
    byte_rows = byte_acts[0]
    row_total, width = byte_rows.shape
    groups_here = conv_weight.shape[0]
    group_width = width // groups_here
    positions = row_total // STRIDE
    seq_count = lax.axis_size("seq")
    seq_rank = lax.axis_index("seq")
    lengths_doc = span_lengths[0]
    tokens_all = lengths_doc.shape[0]
    span_end = jnp.cumsum(lengths_doc)
    span_start = span_end - lengths_doc
    next_rows = shifted(byte_rows[:STRIDE], "seq", -1)
    extended = jnp.concatenate([byte_rows, next_rows], axis=0)
    blocks = extended.reshape(positions + 1, STRIDE, groups_here, group_width)
    windows = jnp.concatenate([blocks[:-1], blocks[1:]], axis=1)
    taps_weight = conv_weight.reshape(groups_here, KERNEL, group_width, group_width)
    conv_out = jnp.einsum(
        "pkgc,gkco->pgo", windows, taps_weight, preferred_element_type=jnp.float32
    )
    conv_out = conv_out + conv_bias.reshape(groups_here, group_width)[None]
    downsampled = conv_out.reshape(positions, width).astype(jnp.bfloat16)
    local_weight = intersection_weights(
        span_start, span_end, lengths_doc, seq_rank * positions, positions
    )
    tokens_here = tokens_all // seq_count
    own_start = lax.dynamic_slice_in_dim(span_start, seq_rank * tokens_here, tokens_here)
    own_end = lax.dynamic_slice_in_dim(span_end, seq_rank * tokens_here, tokens_here)
    own_lengths = lax.dynamic_slice_in_dim(lengths_doc, seq_rank * tokens_here, tokens_here)
    token_weight = intersection_weights(own_start, own_end, own_lengths, 0, positions * seq_count)
    down_all = shard_gather(downsampled, "seq")
    pooled_sum = jnp.dot(token_weight, down_all, preferred_element_type=jnp.float32).astype(
        jnp.bfloat16
    )
    ring = TENSOR_RING
    early = tokens_here * 7 // 16
    gathered = jnp.concatenate(
        [
            tensor_gather(pooled_sum[:early], "tensor", ring),
            tensor_gather_late_pair(pooled_sum[early:], "tensor", ring),
        ],
        axis=0,
    )
    predicted = jnp.dot(gathered, proj_weight, preferred_element_type=jnp.float32)
    err_grad = (predicted - teacher[0].astype(jnp.float32)).astype(jnp.bfloat16)
    proj_local = lax.dot_general(
        gathered, err_grad, (((0,), (0,)), ((), ())), preferred_element_type=jnp.float32
    )
    token_scale = 1.0 / jnp.sqrt(jnp.float32(lax.axis_size("dp") * tokens_all))
    proj_summed = permute_psum(proj_local.astype(jnp.bfloat16), ("dp", "seq")).astype(jnp.float32)
    proj_grad = proj_summed * token_scale
    half = tokens_here // 2
    grad_blocks = [
        lax.dot_general(
            proj_weight, err_part, (((1,), (1,)), ((), ())), preferred_element_type=jnp.float32
        ).astype(jnp.bfloat16)
        for err_part in (err_grad[:half], err_grad[half:])
    ]
    pooled_grad_t = jnp.concatenate(
        [
            lax.psum_scatter(grad_blocks[0], "tensor", scatter_dimension=0, tiled=True),
            tensor_scatter(grad_blocks[1], "tensor", ring).astype(jnp.bfloat16),
        ],
        axis=1,
    )
    weight_part = local_weight
    down_sum = lax.dot_general(
        weight_part,
        lax.all_gather(pooled_grad_t, "seq", axis=1, tiled=True),
        (((0,), (1,)), ((), ())),
        preferred_element_type=jnp.float32,
    )
    down_grad = down_sum.astype(jnp.bfloat16).reshape(positions, groups_here, group_width)
    conv_local = jnp.einsum(
        "pkgc,pgo->gkco", windows, down_grad, preferred_element_type=jnp.float32
    )
    conv_flat = conv_local.astype(jnp.bfloat16).reshape(KERNEL * groups_here * group_width, group_width)
    conv_summed = (
        exchange_psum(conv_flat, ("dp", "seq"))
        .reshape(conv_local.shape)
        .astype(jnp.float32)
    )
    position_scale = 1.0 / jnp.sqrt(jnp.float32(lax.axis_size("dp") * positions * seq_count))
    conv_grad = (conv_summed * position_scale).reshape(
        groups_here, KERNEL * group_width, group_width
    )
    window_grad = jnp.einsum(
        "pgo,gkco->pkgc", down_grad, taps_weight, preferred_element_type=jnp.float32
    )
    incoming = shifted(window_grad[-1, STRIDE:], "seq", 1)
    carried_grad = jnp.concatenate([incoming[None], window_grad[:-1, STRIDE:]], axis=0)
    byte_grad = (
        (window_grad[:, :STRIDE] + carried_grad).reshape(row_total, width).astype(jnp.bfloat16)
    )
    return (downsampled[None], byte_grad[None], conv_grad, proj_grad)


def solution(mesh):
    return jax.shard_map(
        local,
        mesh=mesh,
        in_specs=(
            P("dp", "seq", "tensor"),
            P("tensor", None, None),
            P("tensor"),
            P(None, "tensor"),
            P("dp", "seq", "tensor"),
            P("dp", None),
        ),
        out_specs=(
            P("dp", "seq", "tensor"),
            P("dp", "seq", "tensor"),
            P("tensor", None, None),
            P(None, "tensor"),
        ),
        check_vma=False,
    )
```

```python
import jax
import jax.numpy as jnp
from jax import lax
from jax.sharding import PartitionSpec as P

STRIDE = 4
KERNEL = 8
TENSOR_RING = 8


def shifted(block, axis, distance):
    devices = range(lax.axis_size(axis))
    route = [(i - distance, i) for i in devices if i - distance in devices]
    return lax.ppermute(block, axis, route)


def shard_sum(block, axis):
    count = lax.axis_size(axis)
    rank = lax.axis_index(axis)
    pieces = block.reshape((count, block.shape[0] // count) + block.shape[1:])
    total = lax.dynamic_index_in_dim(pieces, rank, 0, keepdims=False).astype(jnp.float32)
    for distance in range(1, count):
        route = [(i, (i + distance) % count) for i in range(count)]
        outgoing = lax.dynamic_index_in_dim(pieces, (rank + distance) % count, 0, keepdims=False)
        total = total + lax.ppermute(outgoing, axis, route).astype(jnp.float32)
    return total


def shard_gather(piece, axis):
    count = lax.axis_size(axis)
    rank = lax.axis_index(axis)
    rows = piece.shape[0]
    gathered = jnp.zeros((count * rows,) + piece.shape[1:], piece.dtype)
    gathered = lax.dynamic_update_slice_in_dim(gathered, piece, rank * rows, 0)
    for distance in range(1, count):
        route = [(i, (i + distance) % count) for i in range(count)]
        incoming = lax.ppermute(piece, axis, route)
        source = (rank + count - distance) % count
        gathered = lax.dynamic_update_slice_in_dim(gathered, incoming, source * rows, 0)
    return gathered


def exchange_psum(block, axes):
    summed = block
    for axis in axes:
        count = lax.axis_size(axis)
        rank = lax.axis_index(axis)
        slots = jnp.zeros((count,) + block.shape, block.dtype)
        slots = lax.dynamic_update_index_in_dim(slots, summed, rank, 0)
        for distance in range(1, count):
            route = [(i, (i + distance) % count) for i in range(count)]
            incoming = lax.ppermute(summed, axis, route)
            slots = lax.dynamic_update_index_in_dim(slots, incoming, (rank + count - distance) % count, 0)
        summed = jnp.sum(slots.astype(jnp.float32), axis=0).astype(block.dtype)
    return summed


def permute_psum(block, axes):
    summed = block
    for axis in axes:
        summed = shard_sum(summed, axis).astype(block.dtype)
    for axis in axes[::-1]:
        summed = shard_gather(summed, axis)
    return summed


def ring_routes(count, ring):
    def device(pair, place):
        return pair * ring + place % ring
    pairs = count // ring
    plus = [(device(a, b), device(a, b + 1)) for a in range(pairs) for b in range(ring)]
    minus = [(device(a, b), device(a, b - 1)) for a in range(pairs) for b in range(ring)]
    across = [(i, (i + ring) % count) for i in range(count)]
    return plus, minus, across


def tensor_gather(piece, axis, ring):
    count = lax.axis_size(axis)
    rank = lax.axis_index(axis)
    pair_index = rank // ring
    place = rank % ring
    plus, minus, across = ring_routes(count, ring)
    other = lax.ppermute(piece, axis, across)
    pair = jnp.where(pair_index == 0, jnp.stack([piece, other]), jnp.stack([other, piece]))
    slots = jnp.zeros((ring,) + pair.shape, pair.dtype)
    slots = lax.dynamic_update_index_in_dim(slots, pair, place, 0)
    forward = pair
    backward = pair
    full_steps = (ring - 1) // 2
    for step in range(1, full_steps + 1):
        forward = lax.ppermute(forward, axis, plus)
        slots = lax.dynamic_update_index_in_dim(slots, forward, (place + ring - step) % ring, 0)
        backward = lax.ppermute(backward, axis, minus)
        slots = lax.dynamic_update_index_in_dim(slots, backward, (place + step) % ring, 0)
    if ring % 2 == 0:
        rows_half = pair.shape[1] // 2
        far = (place + ring // 2) % ring
        front = lax.ppermute(forward[:, :rows_half], axis, plus)
        back = lax.ppermute(backward[:, rows_half:], axis, minus)
        slots = lax.dynamic_update_index_in_dim(
            slots, jnp.concatenate([front, back], axis=1), far, 0
        )
    rows, width = piece.shape
    return slots.transpose(2, 1, 0, 3).reshape(rows, count * width)


def tensor_scatter(block, axis, ring):
    count = lax.axis_size(axis)
    rank = lax.axis_index(axis)
    pair_index = rank // ring
    place = rank % ring
    plus, minus, across = ring_routes(count, ring)
    view = block.reshape((count // ring, ring, block.shape[0] // count) + block.shape[1:])

    def own(target):
        return lax.dynamic_index_in_dim(view, target % ring, 1, keepdims=False).astype(jnp.float32)

    plus_steps = ring // 2
    minus_steps = ring - 1 - plus_steps
    total = own(place)
    outgoing = own(place + plus_steps).astype(block.dtype)
    for step in range(1, plus_steps + 1):
        incoming = lax.ppermute(outgoing, axis, plus).astype(jnp.float32)
        if step < plus_steps:
            outgoing = (incoming + own(place + plus_steps - step)).astype(block.dtype)
        else:
            total = total + incoming
    outgoing = own(place + ring - minus_steps).astype(block.dtype)
    for step in range(1, minus_steps + 1):
        incoming = lax.ppermute(outgoing, axis, minus).astype(jnp.float32)
        if step < minus_steps:
            outgoing = (incoming + own(place + ring - minus_steps + step)).astype(block.dtype)
        else:
            total = total + incoming
    sent = lax.dynamic_index_in_dim(total, 1 - pair_index, 0, keepdims=False)
    kept = lax.dynamic_index_in_dim(total, pair_index, 0, keepdims=False)
    return kept + lax.ppermute(sent.astype(block.dtype), axis, across).astype(jnp.float32)


def intersection_weights(span_start, span_end, span_lengths, first_position, position_count):
    byte_first = (first_position + jnp.arange(position_count, dtype=jnp.int32)) * STRIDE
    lower_edge = jnp.maximum(span_start[:, None], byte_first[None, :])
    upper_edge = jnp.minimum(span_end[:, None], byte_first[None, :] + STRIDE)
    covered = jnp.maximum(upper_edge - lower_edge, 0).astype(jnp.float32)
    return (covered / span_lengths[:, None].astype(jnp.float32)).astype(jnp.bfloat16)


def local(byte_acts, conv_weight, conv_bias, proj_weight, teacher, span_lengths):
    byte_rows = byte_acts[0]
    row_total, width = byte_rows.shape
    groups_here = conv_weight.shape[0]
    group_width = width // groups_here
    positions = row_total // STRIDE
    seq_count = lax.axis_size("seq")
    seq_rank = lax.axis_index("seq")
    lengths_doc = span_lengths[0]
    tokens_all = lengths_doc.shape[0]
    span_end = jnp.cumsum(lengths_doc)
    span_start = span_end - lengths_doc
    next_rows = shifted(byte_rows[:STRIDE], "seq", -1)
    extended = jnp.concatenate([byte_rows, next_rows], axis=0)
    blocks = extended.reshape(positions + 1, STRIDE, groups_here, group_width)
    windows = jnp.concatenate([blocks[:-1], blocks[1:]], axis=1)
    taps_weight = conv_weight.reshape(groups_here, KERNEL, group_width, group_width)
    conv_out = jnp.einsum(
        "pkgc,gkco->pgo", windows, taps_weight, preferred_element_type=jnp.float32
    )
    conv_out = conv_out + conv_bias.reshape(groups_here, group_width)[None]
    downsampled = conv_out.reshape(positions, width).astype(jnp.bfloat16)
    local_weight = intersection_weights(
        span_start, span_end, lengths_doc, seq_rank * positions, positions
    )
    tokens_here = tokens_all // seq_count
    own_start = lax.dynamic_slice_in_dim(span_start, seq_rank * tokens_here, tokens_here)
    own_end = lax.dynamic_slice_in_dim(span_end, seq_rank * tokens_here, tokens_here)
    own_lengths = lax.dynamic_slice_in_dim(lengths_doc, seq_rank * tokens_here, tokens_here)
    token_weight = intersection_weights(own_start, own_end, own_lengths, 0, positions * seq_count)
    down_all = shard_gather(downsampled, "seq")
    pooled_sum = jnp.dot(token_weight, down_all, preferred_element_type=jnp.float32).astype(
        jnp.bfloat16
    )
    ring = TENSOR_RING
    gathered = tensor_gather(pooled_sum, "tensor", ring)
    predicted = jnp.dot(gathered, proj_weight, preferred_element_type=jnp.float32)
    err_grad = (predicted - teacher[0].astype(jnp.float32)).astype(jnp.bfloat16)
    proj_local = lax.dot_general(
        gathered, err_grad, (((0,), (0,)), ((), ())), preferred_element_type=jnp.float32
    )
    token_scale = 1.0 / jnp.sqrt(jnp.float32(lax.axis_size("dp") * tokens_all))
    proj_summed = permute_psum(proj_local.astype(jnp.bfloat16), ("dp", "seq")).astype(jnp.float32)
    proj_grad = proj_summed * token_scale
    grad_block = lax.dot_general(
        proj_weight, err_grad, (((1,), (1,)), ((), ())), preferred_element_type=jnp.float32
    ).astype(jnp.bfloat16)
    pooled_grad_t = lax.psum_scatter(grad_block, "tensor", scatter_dimension=0, tiled=True)
    weight_part = local_weight
    down_sum = lax.dot_general(
        weight_part,
        lax.all_gather(pooled_grad_t, "seq", axis=1, tiled=True),
        (((0,), (1,)), ((), ())),
        preferred_element_type=jnp.float32,
    )
    down_grad = down_sum.astype(jnp.bfloat16).reshape(positions, groups_here, group_width)
    conv_local = jnp.einsum(
        "pkgc,pgo->gkco", windows, down_grad, preferred_element_type=jnp.float32
    )
    conv_flat = conv_local.astype(jnp.bfloat16).reshape(KERNEL * groups_here * group_width, group_width)
    conv_summed = (
        exchange_psum(conv_flat, ("dp", "seq"))
        .reshape(conv_local.shape)
        .astype(jnp.float32)
    )
    position_scale = 1.0 / jnp.sqrt(jnp.float32(lax.axis_size("dp") * positions * seq_count))
    conv_grad = (conv_summed * position_scale).reshape(
        groups_here, KERNEL * group_width, group_width
    )
    window_grad = jnp.einsum(
        "pgo,gkco->pkgc", down_grad, taps_weight, preferred_element_type=jnp.float32
    )
    incoming = shifted(window_grad[-1, STRIDE:], "seq", 1)
    carried_grad = jnp.concatenate([incoming[None], window_grad[:-1, STRIDE:]], axis=0)
    byte_grad = (
        (window_grad[:, :STRIDE] + carried_grad).reshape(row_total, width).astype(jnp.bfloat16)
    )
    return (downsampled[None], byte_grad[None], conv_grad, proj_grad)


def solution(mesh):
    return jax.shard_map(
        local,
        mesh=mesh,
        in_specs=(
            P("dp", "seq", "tensor"),
            P("tensor", None, None),
            P("tensor"),
            P(None, "tensor"),
            P("dp", "seq", "tensor"),
            P("dp", None),
        ),
        out_specs=(
            P("dp", "seq", "tensor"),
            P("dp", "seq", "tensor"),
            P("tensor", None, None),
            P(None, "tensor"),
        ),
        check_vma=False,
    )
```

```python
import jax
import jax.numpy as jnp
from jax import lax
from jax.sharding import PartitionSpec as P

STRIDE = 4
KERNEL = 8
TENSOR_RING = 8


def shifted(block, axis, distance):
    devices = range(lax.axis_size(axis))
    route = [(i - distance, i) for i in devices if i - distance in devices]
    return lax.ppermute(block, axis, route)


def shard_sum(block, axis):
    count = lax.axis_size(axis)
    rank = lax.axis_index(axis)
    pieces = block.reshape((count, block.shape[0] // count) + block.shape[1:])
    total = lax.dynamic_index_in_dim(pieces, rank, 0, keepdims=False).astype(jnp.float32)
    for distance in range(1, count):
        route = [(i, (i + distance) % count) for i in range(count)]
        outgoing = lax.dynamic_index_in_dim(pieces, (rank + distance) % count, 0, keepdims=False)
        total = total + lax.ppermute(outgoing, axis, route).astype(jnp.float32)
    return total


def shard_gather(piece, axis):
    count = lax.axis_size(axis)
    rank = lax.axis_index(axis)
    rows = piece.shape[0]
    gathered = jnp.zeros((count * rows,) + piece.shape[1:], piece.dtype)
    gathered = lax.dynamic_update_slice_in_dim(gathered, piece, rank * rows, 0)
    for distance in range(1, count):
        route = [(i, (i + distance) % count) for i in range(count)]
        incoming = lax.ppermute(piece, axis, route)
        source = (rank + count - distance) % count
        gathered = lax.dynamic_update_slice_in_dim(gathered, incoming, source * rows, 0)
    return gathered


def exchange_psum(block, axes):
    summed = block
    for axis in axes:
        count = lax.axis_size(axis)
        rank = lax.axis_index(axis)
        slots = jnp.zeros((count,) + block.shape, block.dtype)
        slots = lax.dynamic_update_index_in_dim(slots, summed, rank, 0)
        for distance in range(1, count):
            route = [(i, (i + distance) % count) for i in range(count)]
            incoming = lax.ppermute(summed, axis, route)
            slots = lax.dynamic_update_index_in_dim(slots, incoming, (rank + count - distance) % count, 0)
        summed = jnp.sum(slots.astype(jnp.float32), axis=0).astype(block.dtype)
    return summed


def permute_psum(block, axes):
    summed = block
    for axis in axes:
        summed = shard_sum(summed, axis).astype(block.dtype)
    for axis in axes[::-1]:
        summed = shard_gather(summed, axis)
    return summed


def ring_routes(count, ring):
    def device(pair, place):
        return pair * ring + place % ring
    pairs = count // ring
    plus = [(device(a, b), device(a, b + 1)) for a in range(pairs) for b in range(ring)]
    minus = [(device(a, b), device(a, b - 1)) for a in range(pairs) for b in range(ring)]
    across = [(i, (i + ring) % count) for i in range(count)]
    return plus, minus, across


def tensor_gather(piece, axis, ring):
    count = lax.axis_size(axis)
    rank = lax.axis_index(axis)
    pair_index = rank // ring
    place = rank % ring
    plus, minus, across = ring_routes(count, ring)
    other = lax.ppermute(piece, axis, across)
    pair = jnp.where(pair_index == 0, jnp.stack([piece, other]), jnp.stack([other, piece]))
    slots = jnp.zeros((ring,) + pair.shape, pair.dtype)
    slots = lax.dynamic_update_index_in_dim(slots, pair, place, 0)
    forward = pair
    backward = pair
    full_steps = (ring - 1) // 2
    for step in range(1, full_steps + 1):
        forward = lax.ppermute(forward, axis, plus)
        slots = lax.dynamic_update_index_in_dim(slots, forward, (place + ring - step) % ring, 0)
        backward = lax.ppermute(backward, axis, minus)
        slots = lax.dynamic_update_index_in_dim(slots, backward, (place + step) % ring, 0)
    if ring % 2 == 0:
        rows_half = pair.shape[1] // 2
        far = (place + ring // 2) % ring
        front = lax.ppermute(forward[:, :rows_half], axis, plus)
        back = lax.ppermute(backward[:, rows_half:], axis, minus)
        slots = lax.dynamic_update_index_in_dim(
            slots, jnp.concatenate([front, back], axis=1), far, 0
        )
    rows, width = piece.shape
    return slots.transpose(2, 1, 0, 3).reshape(rows, count * width)


def tensor_scatter(block, axis, ring):
    count = lax.axis_size(axis)
    rank = lax.axis_index(axis)
    pair_index = rank // ring
    place = rank % ring
    plus, minus, across = ring_routes(count, ring)
    view = block.reshape((count // ring, ring, block.shape[0] // count) + block.shape[1:])

    def own(target):
        return lax.dynamic_index_in_dim(view, target % ring, 1, keepdims=False).astype(jnp.float32)

    plus_steps = ring // 2
    minus_steps = ring - 1 - plus_steps
    total = own(place)
    outgoing = own(place + plus_steps).astype(block.dtype)
    for step in range(1, plus_steps + 1):
        incoming = lax.ppermute(outgoing, axis, plus).astype(jnp.float32)
        if step < plus_steps:
            outgoing = (incoming + own(place + plus_steps - step)).astype(block.dtype)
        else:
            total = total + incoming
    outgoing = own(place + ring - minus_steps).astype(block.dtype)
    for step in range(1, minus_steps + 1):
        incoming = lax.ppermute(outgoing, axis, minus).astype(jnp.float32)
        if step < minus_steps:
            outgoing = (incoming + own(place + ring - minus_steps + step)).astype(block.dtype)
        else:
            total = total + incoming
    sent = lax.dynamic_index_in_dim(total, 1 - pair_index, 0, keepdims=False)
    kept = lax.dynamic_index_in_dim(total, pair_index, 0, keepdims=False)
    return kept + lax.ppermute(sent.astype(block.dtype), axis, across).astype(jnp.float32)


def intersection_weights(span_start, span_end, span_lengths, first_position, position_count):
    byte_first = (first_position + jnp.arange(position_count, dtype=jnp.int32)) * STRIDE
    lower_edge = jnp.maximum(span_start[:, None], byte_first[None, :])
    upper_edge = jnp.minimum(span_end[:, None], byte_first[None, :] + STRIDE)
    covered = jnp.maximum(upper_edge - lower_edge, 0).astype(jnp.float32)
    return (covered / span_lengths[:, None].astype(jnp.float32)).astype(jnp.bfloat16)


def local(byte_acts, conv_weight, conv_bias, proj_weight, teacher, span_lengths):
    byte_rows = byte_acts[0]
    row_total, width = byte_rows.shape
    groups_here = conv_weight.shape[0]
    group_width = width // groups_here
    positions = row_total // STRIDE
    seq_count = lax.axis_size("seq")
    seq_rank = lax.axis_index("seq")
    lengths_doc = span_lengths[0]
    tokens_all = lengths_doc.shape[0]
    span_end = jnp.cumsum(lengths_doc)
    span_start = span_end - lengths_doc
    next_rows = shifted(byte_rows[:STRIDE], "seq", -1)
    extended = jnp.concatenate([byte_rows, next_rows], axis=0)
    blocks = extended.reshape(positions + 1, STRIDE, groups_here, group_width)
    windows = jnp.concatenate([blocks[:-1], blocks[1:]], axis=1)
    taps_weight = conv_weight.reshape(groups_here, KERNEL, group_width, group_width)
    conv_out = jnp.einsum(
        "pkgc,gkco->pgo", windows, taps_weight, preferred_element_type=jnp.float32
    )
    conv_out = conv_out + conv_bias.reshape(groups_here, group_width)[None]
    downsampled = conv_out.reshape(positions, width).astype(jnp.bfloat16)
    local_weight = intersection_weights(
        span_start, span_end, lengths_doc, seq_rank * positions, positions
    )
    tokens_here = tokens_all // seq_count
    own_start = lax.dynamic_slice_in_dim(span_start, seq_rank * tokens_here, tokens_here)
    own_end = lax.dynamic_slice_in_dim(span_end, seq_rank * tokens_here, tokens_here)
    own_lengths = lax.dynamic_slice_in_dim(lengths_doc, seq_rank * tokens_here, tokens_here)
    token_weight = intersection_weights(own_start, own_end, own_lengths, 0, positions * seq_count)
    down_all = shard_gather(downsampled, "seq")
    pooled_sum = jnp.dot(token_weight, down_all, preferred_element_type=jnp.float32).astype(
        jnp.bfloat16
    )
    ring = TENSOR_RING
    gathered = tensor_gather(pooled_sum, "tensor", ring)
    predicted = jnp.dot(gathered, proj_weight, preferred_element_type=jnp.float32)
    err_grad = (predicted - teacher[0].astype(jnp.float32)).astype(jnp.bfloat16)
    proj_local = lax.dot_general(
        gathered, err_grad, (((0,), (0,)), ((), ())), preferred_element_type=jnp.float32
    )
    token_scale = 1.0 / jnp.sqrt(jnp.float32(lax.axis_size("dp") * tokens_all))
    proj_summed = permute_psum(proj_local.astype(jnp.bfloat16), ("seq", "dp")).astype(jnp.float32)
    proj_grad = proj_summed * token_scale
    half = tokens_here // 2
    grad_blocks = [
        lax.dot_general(
            proj_weight, err_part, (((1,), (1,)), ((), ())), preferred_element_type=jnp.float32
        ).astype(jnp.bfloat16)
        for err_part in (err_grad[:half], err_grad[half:])
    ]
    pooled_grad_t = jnp.concatenate(
        [
            lax.psum_scatter(grad_blocks[0], "tensor", scatter_dimension=0, tiled=True),
            tensor_scatter(grad_blocks[1], "tensor", ring).astype(jnp.bfloat16),
        ],
        axis=1,
    )
    weight_part = local_weight
    down_sum = lax.dot_general(
        weight_part,
        lax.all_gather(pooled_grad_t, "seq", axis=1, tiled=True),
        (((0,), (1,)), ((), ())),
        preferred_element_type=jnp.float32,
    )
    down_grad = down_sum.astype(jnp.bfloat16).reshape(positions, groups_here, group_width)
    conv_local = jnp.einsum(
        "pkgc,pgo->gkco", windows, down_grad, preferred_element_type=jnp.float32
    )
    conv_flat = conv_local.astype(jnp.bfloat16).reshape(KERNEL * groups_here * group_width, group_width)
    conv_summed = (
        exchange_psum(conv_flat, ("dp", "seq"))
        .reshape(conv_local.shape)
        .astype(jnp.float32)
    )
    position_scale = 1.0 / jnp.sqrt(jnp.float32(lax.axis_size("dp") * positions * seq_count))
    conv_grad = (conv_summed * position_scale).reshape(
        groups_here, KERNEL * group_width, group_width
    )
    window_grad = jnp.einsum(
        "pgo,gkco->pkgc", down_grad, taps_weight, preferred_element_type=jnp.float32
    )
    incoming = shifted(window_grad[-1, STRIDE:], "seq", 1)
    carried_grad = jnp.concatenate([incoming[None], window_grad[:-1, STRIDE:]], axis=0)
    byte_grad = (
        (window_grad[:, :STRIDE] + carried_grad).reshape(row_total, width).astype(jnp.bfloat16)
    )
    return (downsampled[None], byte_grad[None], conv_grad, proj_grad)


def solution(mesh):
    return jax.shard_map(
        local,
        mesh=mesh,
        in_specs=(
            P("dp", "seq", "tensor"),
            P("tensor", None, None),
            P("tensor"),
            P(None, "tensor"),
            P("dp", "seq", "tensor"),
            P("dp", None),
        ),
        out_specs=(
            P("dp", "seq", "tensor"),
            P("dp", "seq", "tensor"),
            P("tensor", None, None),
            P(None, "tensor"),
        ),
        check_vma=False,
    )
```

```python
import jax
import jax.numpy as jnp
from jax import lax
from jax.sharding import PartitionSpec as P

STRIDE = 4
KERNEL = 8
TENSOR_RING = 8


def shifted(block, axis, distance):
    devices = range(lax.axis_size(axis))
    route = [(i - distance, i) for i in devices if i - distance in devices]
    return lax.ppermute(block, axis, route)


def shard_sum(block, axis):
    count = lax.axis_size(axis)
    rank = lax.axis_index(axis)
    pieces = block.reshape((count, block.shape[0] // count) + block.shape[1:])
    total = lax.dynamic_index_in_dim(pieces, rank, 0, keepdims=False).astype(jnp.float32)
    for distance in range(1, count):
        route = [(i, (i + distance) % count) for i in range(count)]
        outgoing = lax.dynamic_index_in_dim(pieces, (rank + distance) % count, 0, keepdims=False)
        total = total + lax.ppermute(outgoing, axis, route).astype(jnp.float32)
    return total


def shard_gather(piece, axis):
    count = lax.axis_size(axis)
    rank = lax.axis_index(axis)
    rows = piece.shape[0]
    gathered = jnp.zeros((count * rows,) + piece.shape[1:], piece.dtype)
    gathered = lax.dynamic_update_slice_in_dim(gathered, piece, rank * rows, 0)
    for distance in range(1, count):
        route = [(i, (i + distance) % count) for i in range(count)]
        incoming = lax.ppermute(piece, axis, route)
        source = (rank + count - distance) % count
        gathered = lax.dynamic_update_slice_in_dim(gathered, incoming, source * rows, 0)
    return gathered


def exchange_psum(block, axes):
    summed = block
    for axis in axes:
        count = lax.axis_size(axis)
        rank = lax.axis_index(axis)
        slots = jnp.zeros((count,) + block.shape, block.dtype)
        slots = lax.dynamic_update_index_in_dim(slots, summed, rank, 0)
        for distance in range(1, count):
            route = [(i, (i + distance) % count) for i in range(count)]
            incoming = lax.ppermute(summed, axis, route)
            slots = lax.dynamic_update_index_in_dim(slots, incoming, (rank + count - distance) % count, 0)
        summed = jnp.sum(slots.astype(jnp.float32), axis=0).astype(block.dtype)
    return summed


def permute_psum(block, axes):
    summed = block
    for axis in axes:
        summed = shard_sum(summed, axis).astype(block.dtype)
    for axis in axes[::-1]:
        summed = shard_gather(summed, axis)
    return summed


def ring_routes(count, ring):
    def device(pair, place):
        return pair * ring + place % ring
    pairs = count // ring
    plus = [(device(a, b), device(a, b + 1)) for a in range(pairs) for b in range(ring)]
    minus = [(device(a, b), device(a, b - 1)) for a in range(pairs) for b in range(ring)]
    across = [(i, (i + ring) % count) for i in range(count)]
    return plus, minus, across


def tensor_gather(piece, axis, ring):
    count = lax.axis_size(axis)
    rank = lax.axis_index(axis)
    pair_index = rank // ring
    place = rank % ring
    plus, minus, across = ring_routes(count, ring)
    other = lax.ppermute(piece, axis, across)
    pair = jnp.where(pair_index == 0, jnp.stack([piece, other]), jnp.stack([other, piece]))
    slots = jnp.zeros((ring,) + pair.shape, pair.dtype)
    slots = lax.dynamic_update_index_in_dim(slots, pair, place, 0)
    forward = pair
    backward = pair
    full_steps = (ring - 1) // 2
    for step in range(1, full_steps + 1):
        forward = lax.ppermute(forward, axis, plus)
        slots = lax.dynamic_update_index_in_dim(slots, forward, (place + ring - step) % ring, 0)
        backward = lax.ppermute(backward, axis, minus)
        slots = lax.dynamic_update_index_in_dim(slots, backward, (place + step) % ring, 0)
    if ring % 2 == 0:
        rows_half = pair.shape[1] // 2
        far = (place + ring // 2) % ring
        front = lax.ppermute(forward[:, :rows_half], axis, plus)
        back = lax.ppermute(backward[:, rows_half:], axis, minus)
        slots = lax.dynamic_update_index_in_dim(
            slots, jnp.concatenate([front, back], axis=1), far, 0
        )
    rows, width = piece.shape
    return slots.transpose(2, 1, 0, 3).reshape(rows, count * width)


def tensor_scatter(block, axis, ring):
    count = lax.axis_size(axis)
    rank = lax.axis_index(axis)
    pair_index = rank // ring
    place = rank % ring
    plus, minus, across = ring_routes(count, ring)
    view = block.reshape((count // ring, ring, block.shape[0] // count) + block.shape[1:])

    def own(target):
        return lax.dynamic_index_in_dim(view, target % ring, 1, keepdims=False).astype(jnp.float32)

    steps = ring // 2
    rows_half = view.shape[2] // 2
    total = own(place)
    for route, sign, rows in ((plus, 1, slice(0, rows_half)), (minus, -1, slice(rows_half, None))):
        outgoing = own(place + sign * steps)[:, rows].astype(block.dtype)
        for step in range(1, steps + 1):
            incoming = lax.ppermute(outgoing, axis, route).astype(jnp.float32)
            if step == 1:
                nearer = own(place + sign * (steps - step))
                incoming = nearer.at[:, rows].add(incoming) if steps > 1 else incoming
            if step < steps:
                base = own(place + sign * (steps - step)) if step > 1 else 0.0
                outgoing = (incoming + base).astype(block.dtype)
            else:
                total = total + incoming
    sent = lax.dynamic_index_in_dim(total, 1 - pair_index, 0, keepdims=False)
    kept = lax.dynamic_index_in_dim(total, pair_index, 0, keepdims=False)
    return kept + lax.ppermute(sent.astype(block.dtype), axis, across).astype(jnp.float32)


def intersection_weights(span_start, span_end, span_lengths, first_position, position_count):
    byte_first = (first_position + jnp.arange(position_count, dtype=jnp.int32)) * STRIDE
    lower_edge = jnp.maximum(span_start[:, None], byte_first[None, :])
    upper_edge = jnp.minimum(span_end[:, None], byte_first[None, :] + STRIDE)
    covered = jnp.maximum(upper_edge - lower_edge, 0).astype(jnp.float32)
    return (covered / span_lengths[:, None].astype(jnp.float32)).astype(jnp.bfloat16)


def local(byte_acts, conv_weight, conv_bias, proj_weight, teacher, span_lengths):
    byte_rows = byte_acts[0]
    row_total, width = byte_rows.shape
    groups_here = conv_weight.shape[0]
    group_width = width // groups_here
    positions = row_total // STRIDE
    seq_count = lax.axis_size("seq")
    seq_rank = lax.axis_index("seq")
    lengths_doc = span_lengths[0]
    tokens_all = lengths_doc.shape[0]
    span_end = jnp.cumsum(lengths_doc)
    span_start = span_end - lengths_doc
    next_rows = shifted(byte_rows[:STRIDE], "seq", -1)
    extended = jnp.concatenate([byte_rows, next_rows], axis=0)
    blocks = extended.reshape(positions + 1, STRIDE, groups_here, group_width)
    windows = jnp.concatenate([blocks[:-1], blocks[1:]], axis=1)
    taps_weight = conv_weight.reshape(groups_here, KERNEL, group_width, group_width)
    conv_out = jnp.einsum(
        "pkgc,gkco->pgo", windows, taps_weight, preferred_element_type=jnp.float32
    )
    conv_out = conv_out + conv_bias.reshape(groups_here, group_width)[None]
    downsampled = conv_out.reshape(positions, width).astype(jnp.bfloat16)
    local_weight = intersection_weights(
        span_start, span_end, lengths_doc, seq_rank * positions, positions
    )
    tokens_here = tokens_all // seq_count
    own_start = lax.dynamic_slice_in_dim(span_start, seq_rank * tokens_here, tokens_here)
    own_end = lax.dynamic_slice_in_dim(span_end, seq_rank * tokens_here, tokens_here)
    own_lengths = lax.dynamic_slice_in_dim(lengths_doc, seq_rank * tokens_here, tokens_here)
    token_weight = intersection_weights(own_start, own_end, own_lengths, 0, positions * seq_count)
    down_all = shard_gather(downsampled, "seq")
    pooled_sum = jnp.dot(token_weight, down_all, preferred_element_type=jnp.float32).astype(
        jnp.bfloat16
    )
    ring = TENSOR_RING
    gathered = tensor_gather(pooled_sum, "tensor", ring)
    predicted = jnp.dot(gathered, proj_weight, preferred_element_type=jnp.float32)
    err_grad = (predicted - teacher[0].astype(jnp.float32)).astype(jnp.bfloat16)
    proj_local = lax.dot_general(
        gathered, err_grad, (((0,), (0,)), ((), ())), preferred_element_type=jnp.float32
    )
    token_scale = 1.0 / jnp.sqrt(jnp.float32(lax.axis_size("dp") * tokens_all))
    proj_summed = permute_psum(proj_local.astype(jnp.bfloat16), ("dp", "seq")).astype(jnp.float32)
    proj_grad = proj_summed * token_scale
    half = tokens_here // 2
    grad_blocks = [
        lax.dot_general(
            proj_weight, err_part, (((1,), (1,)), ((), ())), preferred_element_type=jnp.float32
        ).astype(jnp.bfloat16)
        for err_part in (err_grad[:half], err_grad[half:])
    ]
    pooled_grad_t = jnp.concatenate(
        [
            lax.psum_scatter(grad_blocks[0], "tensor", scatter_dimension=0, tiled=True),
            tensor_scatter(grad_blocks[1], "tensor", ring).astype(jnp.bfloat16),
        ],
        axis=1,
    )
    weight_part = local_weight
    down_sum = lax.dot_general(
        weight_part,
        lax.all_gather(pooled_grad_t, "seq", axis=1, tiled=True),
        (((0,), (1,)), ((), ())),
        preferred_element_type=jnp.float32,
    )
    down_grad = down_sum.astype(jnp.bfloat16).reshape(positions, groups_here, group_width)
    conv_local = jnp.einsum(
        "pkgc,pgo->gkco", windows, down_grad, preferred_element_type=jnp.float32
    )
    conv_flat = conv_local.astype(jnp.bfloat16).reshape(KERNEL * groups_here * group_width, group_width)
    conv_summed = (
        exchange_psum(conv_flat, ("dp", "seq"))
        .reshape(conv_local.shape)
        .astype(jnp.float32)
    )
    position_scale = 1.0 / jnp.sqrt(jnp.float32(lax.axis_size("dp") * positions * seq_count))
    conv_grad = (conv_summed * position_scale).reshape(
        groups_here, KERNEL * group_width, group_width
    )
    window_grad = jnp.einsum(
        "pgo,gkco->pkgc", down_grad, taps_weight, preferred_element_type=jnp.float32
    )
    incoming = shifted(window_grad[-1, STRIDE:], "seq", 1)
    carried_grad = jnp.concatenate([incoming[None], window_grad[:-1, STRIDE:]], axis=0)
    byte_grad = (
        (window_grad[:, :STRIDE] + carried_grad).reshape(row_total, width).astype(jnp.bfloat16)
    )
    return (downsampled[None], byte_grad[None], conv_grad, proj_grad)


def solution(mesh):
    return jax.shard_map(
        local,
        mesh=mesh,
        in_specs=(
            P("dp", "seq", "tensor"),
            P("tensor", None, None),
            P("tensor"),
            P(None, "tensor"),
            P("dp", "seq", "tensor"),
            P("dp", None),
        ),
        out_specs=(
            P("dp", "seq", "tensor"),
            P("dp", "seq", "tensor"),
            P("tensor", None, None),
            P(None, "tensor"),
        ),
        check_vma=False,
    )
```

```python
import jax
import jax.numpy as jnp
from jax import lax
from jax.sharding import PartitionSpec as P

STRIDE = 4
KERNEL = 8
TENSOR_RING = 8


def shifted(block, axis, distance):
    devices = range(lax.axis_size(axis))
    route = [(i - distance, i) for i in devices if i - distance in devices]
    return lax.ppermute(block, axis, route)


def shard_sum(block, axis):
    count = lax.axis_size(axis)
    rank = lax.axis_index(axis)
    pieces = block.reshape((count, block.shape[0] // count) + block.shape[1:])
    total = lax.dynamic_index_in_dim(pieces, rank, 0, keepdims=False).astype(jnp.float32)
    for distance in range(1, count):
        route = [(i, (i + distance) % count) for i in range(count)]
        outgoing = lax.dynamic_index_in_dim(pieces, (rank + distance) % count, 0, keepdims=False)
        total = total + lax.ppermute(outgoing, axis, route).astype(jnp.float32)
    return total


def shard_gather(piece, axis):
    count = lax.axis_size(axis)
    rank = lax.axis_index(axis)
    rows = piece.shape[0]
    gathered = jnp.zeros((count * rows,) + piece.shape[1:], piece.dtype)
    gathered = lax.dynamic_update_slice_in_dim(gathered, piece, rank * rows, 0)
    for distance in range(1, count):
        route = [(i, (i + distance) % count) for i in range(count)]
        incoming = lax.ppermute(piece, axis, route)
        source = (rank + count - distance) % count
        gathered = lax.dynamic_update_slice_in_dim(gathered, incoming, source * rows, 0)
    return gathered


def exchange_psum(block, axes):
    summed = block
    for axis in axes:
        count = lax.axis_size(axis)
        rank = lax.axis_index(axis)
        slots = jnp.zeros((count,) + block.shape, block.dtype)
        slots = lax.dynamic_update_index_in_dim(slots, summed, rank, 0)
        for distance in range(1, count):
            route = [(i, (i + distance) % count) for i in range(count)]
            incoming = lax.ppermute(summed, axis, route)
            slots = lax.dynamic_update_index_in_dim(slots, incoming, (rank + count - distance) % count, 0)
        summed = jnp.sum(slots.astype(jnp.float32), axis=0).astype(block.dtype)
    return summed


def permute_psum(block, axes):
    summed = block
    for axis in axes:
        summed = shard_sum(summed, axis).astype(block.dtype)
    for axis in axes[::-1]:
        summed = shard_gather(summed, axis)
    return summed


def ring_routes(count, ring):
    def device(pair, place):
        return pair * ring + place % ring
    pairs = count // ring
    plus = [(device(a, b), device(a, b + 1)) for a in range(pairs) for b in range(ring)]
    minus = [(device(a, b), device(a, b - 1)) for a in range(pairs) for b in range(ring)]
    across = [(i, (i + ring) % count) for i in range(count)]
    return plus, minus, across


def tensor_gather(piece, axis, ring):
    count = lax.axis_size(axis)
    rank = lax.axis_index(axis)
    pair_index = rank // ring
    place = rank % ring
    plus, minus, across = ring_routes(count, ring)
    other = lax.ppermute(piece, axis, across)
    pair = jnp.where(pair_index == 0, jnp.stack([piece, other]), jnp.stack([other, piece]))
    slots = jnp.zeros((ring,) + pair.shape, pair.dtype)
    slots = lax.dynamic_update_index_in_dim(slots, pair, place, 0)
    forward = pair
    backward = pair
    full_steps = (ring - 1) // 2
    for step in range(1, full_steps + 1):
        forward = lax.ppermute(forward, axis, plus)
        slots = lax.dynamic_update_index_in_dim(slots, forward, (place + ring - step) % ring, 0)
        backward = lax.ppermute(backward, axis, minus)
        slots = lax.dynamic_update_index_in_dim(slots, backward, (place + step) % ring, 0)
    if ring % 2 == 0:
        rows_half = pair.shape[1] // 2
        far = (place + ring // 2) % ring
        front = lax.ppermute(forward[:, :rows_half], axis, plus)
        back = lax.ppermute(backward[:, rows_half:], axis, minus)
        slots = lax.dynamic_update_index_in_dim(
            slots, jnp.concatenate([front, back], axis=1), far, 0
        )
    rows, width = piece.shape
    return slots.transpose(2, 1, 0, 3).reshape(rows, count * width)


def tensor_scatter(block, axis, ring):
    count = lax.axis_size(axis)
    rank = lax.axis_index(axis)
    pair_index = rank // ring
    place = rank % ring
    plus, minus, across = ring_routes(count, ring)
    view = block.reshape((count // ring, ring, block.shape[0] // count) + block.shape[1:])

    def own(target):
        return lax.dynamic_index_in_dim(view, target % ring, 1, keepdims=False).astype(jnp.float32)

    plus_steps = ring // 2
    minus_steps = ring - 1 - plus_steps
    total = own(place)
    outgoing = own(place + plus_steps).astype(block.dtype)
    for step in range(1, plus_steps + 1):
        incoming = lax.ppermute(outgoing, axis, plus).astype(jnp.float32)
        if step < plus_steps:
            outgoing = (incoming + own(place + plus_steps - step)).astype(block.dtype)
        else:
            total = total + incoming
    outgoing = own(place + ring - minus_steps).astype(block.dtype)
    for step in range(1, minus_steps + 1):
        incoming = lax.ppermute(outgoing, axis, minus).astype(jnp.float32)
        if step < minus_steps:
            outgoing = (incoming + own(place + ring - minus_steps + step)).astype(block.dtype)
        else:
            total = total + incoming
    sent = lax.dynamic_index_in_dim(total, 1 - pair_index, 0, keepdims=False)
    kept = lax.dynamic_index_in_dim(total, pair_index, 0, keepdims=False)
    return kept + lax.ppermute(sent.astype(block.dtype), axis, across).astype(jnp.float32)


def intersection_weights(span_start, span_end, span_lengths, first_position, position_count):
    byte_first = (first_position + jnp.arange(position_count, dtype=jnp.int32)) * STRIDE
    lower_edge = jnp.maximum(span_start[:, None], byte_first[None, :])
    upper_edge = jnp.minimum(span_end[:, None], byte_first[None, :] + STRIDE)
    covered = jnp.maximum(upper_edge - lower_edge, 0).astype(jnp.float32)
    return (covered / span_lengths[:, None].astype(jnp.float32)).astype(jnp.bfloat16)


def local(byte_acts, conv_weight, conv_bias, proj_weight, teacher, span_lengths):
    byte_rows = byte_acts[0]
    row_total, width = byte_rows.shape
    groups_here = conv_weight.shape[0]
    group_width = width // groups_here
    positions = row_total // STRIDE
    seq_count = lax.axis_size("seq")
    seq_rank = lax.axis_index("seq")
    lengths_doc = span_lengths[0]
    tokens_all = lengths_doc.shape[0]
    span_end = jnp.cumsum(lengths_doc)
    span_start = span_end - lengths_doc
    next_rows = shifted(byte_rows[:STRIDE], "seq", -1)
    extended = jnp.concatenate([byte_rows, next_rows], axis=0)
    blocks = extended.reshape(positions + 1, STRIDE, groups_here, group_width)
    windows = jnp.concatenate([blocks[:-1], blocks[1:]], axis=1)
    taps_weight = conv_weight.reshape(groups_here, KERNEL, group_width, group_width)
    conv_out = jnp.einsum(
        "pkgc,gkco->pgo", windows, taps_weight, preferred_element_type=jnp.float32
    )
    conv_out = conv_out + conv_bias.reshape(groups_here, group_width)[None]
    downsampled = conv_out.reshape(positions, width).astype(jnp.bfloat16)
    local_weight = intersection_weights(
        span_start, span_end, lengths_doc, seq_rank * positions, positions
    )
    tokens_here = tokens_all // seq_count
    own_start = lax.dynamic_slice_in_dim(span_start, seq_rank * tokens_here, tokens_here)
    own_end = lax.dynamic_slice_in_dim(span_end, seq_rank * tokens_here, tokens_here)
    own_lengths = lax.dynamic_slice_in_dim(lengths_doc, seq_rank * tokens_here, tokens_here)
    token_weight = intersection_weights(own_start, own_end, own_lengths, 0, positions * seq_count)
    down_all = shard_gather(downsampled, "seq")
    pooled_sum = jnp.dot(token_weight, down_all, preferred_element_type=jnp.float32).astype(
        jnp.bfloat16
    )
    ring = TENSOR_RING
    gathered = tensor_gather(pooled_sum, "tensor", ring)
    predicted = jnp.dot(gathered, proj_weight, preferred_element_type=jnp.float32)
    err_grad = (predicted - teacher[0].astype(jnp.float32)).astype(jnp.bfloat16)
    proj_local = lax.dot_general(
        gathered, err_grad, (((0,), (0,)), ((), ())), preferred_element_type=jnp.float32
    )
    token_scale = 1.0 / jnp.sqrt(jnp.float32(lax.axis_size("dp") * tokens_all))
    proj_summed = permute_psum(proj_local.astype(jnp.bfloat16), ("dp", "seq")).astype(jnp.float32)
    proj_grad = proj_summed * token_scale
    half = tokens_here * 5 // 8
    grad_blocks = [
        lax.dot_general(
            proj_weight, err_part, (((1,), (1,)), ((), ())), preferred_element_type=jnp.float32
        ).astype(jnp.bfloat16)
        for err_part in (err_grad[:half], err_grad[half:])
    ]
    pooled_grad_t = jnp.concatenate(
        [
            lax.psum_scatter(grad_blocks[0], "tensor", scatter_dimension=0, tiled=True),
            tensor_scatter(grad_blocks[1], "tensor", ring).astype(jnp.bfloat16),
        ],
        axis=1,
    )
    weight_part = local_weight
    down_sum = lax.dot_general(
        weight_part,
        lax.all_gather(pooled_grad_t, "seq", axis=1, tiled=True),
        (((0,), (1,)), ((), ())),
        preferred_element_type=jnp.float32,
    )
    down_grad = down_sum.astype(jnp.bfloat16).reshape(positions, groups_here, group_width)
    conv_local = jnp.einsum(
        "pkgc,pgo->gkco", windows, down_grad, preferred_element_type=jnp.float32
    )
    conv_flat = conv_local.astype(jnp.bfloat16).reshape(KERNEL * groups_here * group_width, group_width)
    conv_summed = (
        exchange_psum(conv_flat, ("dp", "seq"))
        .reshape(conv_local.shape)
        .astype(jnp.float32)
    )
    position_scale = 1.0 / jnp.sqrt(jnp.float32(lax.axis_size("dp") * positions * seq_count))
    conv_grad = (conv_summed * position_scale).reshape(
        groups_here, KERNEL * group_width, group_width
    )
    window_grad = jnp.einsum(
        "pgo,gkco->pkgc", down_grad, taps_weight, preferred_element_type=jnp.float32
    )
    incoming = shifted(window_grad[-1, STRIDE:], "seq", 1)
    carried_grad = jnp.concatenate([incoming[None], window_grad[:-1, STRIDE:]], axis=0)
    byte_grad = (
        (window_grad[:, :STRIDE] + carried_grad).reshape(row_total, width).astype(jnp.bfloat16)
    )
    return (downsampled[None], byte_grad[None], conv_grad, proj_grad)


def solution(mesh):
    return jax.shard_map(
        local,
        mesh=mesh,
        in_specs=(
            P("dp", "seq", "tensor"),
            P("tensor", None, None),
            P("tensor"),
            P(None, "tensor"),
            P("dp", "seq", "tensor"),
            P("dp", None),
        ),
        out_specs=(
            P("dp", "seq", "tensor"),
            P("dp", "seq", "tensor"),
            P("tensor", None, None),
            P(None, "tensor"),
        ),
        check_vma=False,
    )
```

```python
import jax
import jax.numpy as jnp
from jax import lax
from jax.sharding import PartitionSpec as P

STRIDE = 4
KERNEL = 8
TENSOR_RING = 8


def shifted(block, axis, distance):
    devices = range(lax.axis_size(axis))
    route = [(i - distance, i) for i in devices if i - distance in devices]
    return lax.ppermute(block, axis, route)


def shard_sum(block, axis):
    count = lax.axis_size(axis)
    rank = lax.axis_index(axis)
    pieces = block.reshape((count, block.shape[0] // count) + block.shape[1:])
    total = lax.dynamic_index_in_dim(pieces, rank, 0, keepdims=False).astype(jnp.float32)
    for distance in range(1, count):
        route = [(i, (i + distance) % count) for i in range(count)]
        outgoing = lax.dynamic_index_in_dim(pieces, (rank + distance) % count, 0, keepdims=False)
        total = total + lax.ppermute(outgoing, axis, route).astype(jnp.float32)
    return total


def shard_gather(piece, axis):
    count = lax.axis_size(axis)
    rank = lax.axis_index(axis)
    rows = piece.shape[0]
    gathered = jnp.zeros((count * rows,) + piece.shape[1:], piece.dtype)
    gathered = lax.dynamic_update_slice_in_dim(gathered, piece, rank * rows, 0)
    for distance in range(1, count):
        route = [(i, (i + distance) % count) for i in range(count)]
        incoming = lax.ppermute(piece, axis, route)
        source = (rank + count - distance) % count
        gathered = lax.dynamic_update_slice_in_dim(gathered, incoming, source * rows, 0)
    return gathered


def exchange_psum(block, axes):
    summed = block
    for axis in axes:
        count = lax.axis_size(axis)
        rank = lax.axis_index(axis)
        slots = jnp.zeros((count,) + block.shape, block.dtype)
        slots = lax.dynamic_update_index_in_dim(slots, summed, rank, 0)
        for distance in range(1, count):
            route = [(i, (i + distance) % count) for i in range(count)]
            incoming = lax.ppermute(summed, axis, route)
            slots = lax.dynamic_update_index_in_dim(slots, incoming, (rank + count - distance) % count, 0)
        summed = jnp.sum(slots.astype(jnp.float32), axis=0).astype(block.dtype)
    return summed


def permute_psum(block, axes):
    summed = block
    for axis in axes:
        summed = shard_sum(summed, axis).astype(block.dtype)
    for axis in axes[::-1]:
        summed = shard_gather(summed, axis)
    return summed


def ring_routes(count, ring):
    def device(pair, place):
        return pair * ring + place % ring
    pairs = count // ring
    plus = [(device(a, b), device(a, b + 1)) for a in range(pairs) for b in range(ring)]
    minus = [(device(a, b), device(a, b - 1)) for a in range(pairs) for b in range(ring)]
    across = [(i, (i + ring) % count) for i in range(count)]
    return plus, minus, across


def tensor_gather(piece, axis, ring):
    count = lax.axis_size(axis)
    rank = lax.axis_index(axis)
    pair_index = rank // ring
    place = rank % ring
    plus, minus, across = ring_routes(count, ring)
    other = lax.ppermute(piece, axis, across)
    pair = jnp.where(pair_index == 0, jnp.stack([piece, other]), jnp.stack([other, piece]))
    slots = jnp.zeros((ring,) + pair.shape, pair.dtype)
    slots = lax.dynamic_update_index_in_dim(slots, pair, place, 0)
    forward = pair
    backward = pair
    full_steps = (ring - 1) // 2
    for step in range(1, full_steps + 1):
        forward = lax.ppermute(forward, axis, plus)
        slots = lax.dynamic_update_index_in_dim(slots, forward, (place + ring - step) % ring, 0)
        backward = lax.ppermute(backward, axis, minus)
        slots = lax.dynamic_update_index_in_dim(slots, backward, (place + step) % ring, 0)
    if ring % 2 == 0:
        rows_half = pair.shape[1] // 2
        far = (place + ring // 2) % ring
        front = lax.ppermute(forward[:, :rows_half], axis, plus)
        back = lax.ppermute(backward[:, rows_half:], axis, minus)
        slots = lax.dynamic_update_index_in_dim(
            slots, jnp.concatenate([front, back], axis=1), far, 0
        )
    rows, width = piece.shape
    return slots.transpose(2, 1, 0, 3).reshape(rows, count * width)


def tensor_scatter(block, axis, ring):
    count = lax.axis_size(axis)
    rank = lax.axis_index(axis)
    pair_index = rank // ring
    place = rank % ring
    plus, minus, across = ring_routes(count, ring)
    view = block.reshape((count // ring, ring, block.shape[0] // count) + block.shape[1:])

    def own(target):
        return lax.dynamic_index_in_dim(view, target % ring, 1, keepdims=False).astype(jnp.float32)

    plus_steps = ring // 2
    minus_steps = ring - 1 - plus_steps
    total = own(place)
    outgoing = own(place + plus_steps).astype(block.dtype)
    for step in range(1, plus_steps + 1):
        incoming = lax.ppermute(outgoing, axis, plus).astype(jnp.float32)
        if step < plus_steps:
            outgoing = (incoming + own(place + plus_steps - step)).astype(block.dtype)
        else:
            total = total + incoming
    outgoing = own(place + ring - minus_steps).astype(block.dtype)
    for step in range(1, minus_steps + 1):
        incoming = lax.ppermute(outgoing, axis, minus).astype(jnp.float32)
        if step < minus_steps:
            outgoing = (incoming + own(place + ring - minus_steps + step)).astype(block.dtype)
        else:
            total = total + incoming
    sent = lax.dynamic_index_in_dim(total, 1 - pair_index, 0, keepdims=False)
    kept = lax.dynamic_index_in_dim(total, pair_index, 0, keepdims=False)
    return kept + lax.ppermute(sent.astype(block.dtype), axis, across).astype(jnp.float32)


def intersection_weights(span_start, span_end, span_lengths, first_position, position_count):
    byte_first = (first_position + jnp.arange(position_count, dtype=jnp.int32)) * STRIDE
    lower_edge = jnp.maximum(span_start[:, None], byte_first[None, :])
    upper_edge = jnp.minimum(span_end[:, None], byte_first[None, :] + STRIDE)
    covered = jnp.maximum(upper_edge - lower_edge, 0).astype(jnp.float32)
    return (covered / span_lengths[:, None].astype(jnp.float32)).astype(jnp.bfloat16)


def local(byte_acts, conv_weight, conv_bias, proj_weight, teacher, span_lengths):
    byte_rows = byte_acts[0]
    row_total, width = byte_rows.shape
    groups_here = conv_weight.shape[0]
    group_width = width // groups_here
    positions = row_total // STRIDE
    seq_count = lax.axis_size("seq")
    seq_rank = lax.axis_index("seq")
    lengths_doc = span_lengths[0]
    tokens_all = lengths_doc.shape[0]
    span_end = jnp.cumsum(lengths_doc)
    span_start = span_end - lengths_doc
    next_rows = shifted(byte_rows[:STRIDE], "seq", -1)
    extended = jnp.concatenate([byte_rows, next_rows], axis=0)
    blocks = extended.reshape(positions + 1, STRIDE, groups_here, group_width)
    windows = jnp.concatenate([blocks[:-1], blocks[1:]], axis=1)
    taps_weight = conv_weight.reshape(groups_here, KERNEL, group_width, group_width)
    conv_out = jnp.einsum(
        "pkgc,gkco->pgo", windows, taps_weight, preferred_element_type=jnp.float32
    )
    conv_out = conv_out + conv_bias.reshape(groups_here, group_width)[None]
    downsampled = conv_out.reshape(positions, width).astype(jnp.bfloat16)
    local_weight = intersection_weights(
        span_start, span_end, lengths_doc, seq_rank * positions, positions
    )
    tokens_here = tokens_all // seq_count
    own_start = lax.dynamic_slice_in_dim(span_start, seq_rank * tokens_here, tokens_here)
    own_end = lax.dynamic_slice_in_dim(span_end, seq_rank * tokens_here, tokens_here)
    own_lengths = lax.dynamic_slice_in_dim(lengths_doc, seq_rank * tokens_here, tokens_here)
    token_weight = intersection_weights(own_start, own_end, own_lengths, 0, positions * seq_count)
    down_all = shard_gather(downsampled, "seq")
    pooled_sum = jnp.dot(token_weight, down_all, preferred_element_type=jnp.float32).astype(
        jnp.bfloat16
    )
    ring = TENSOR_RING
    gathered = tensor_gather(pooled_sum, "tensor", ring)
    predicted = jnp.dot(gathered, proj_weight, preferred_element_type=jnp.float32)
    err_grad = (predicted - teacher[0].astype(jnp.float32)).astype(jnp.bfloat16)
    proj_local = lax.dot_general(
        gathered, err_grad, (((0,), (0,)), ((), ())), preferred_element_type=jnp.float32
    )
    token_scale = 1.0 / jnp.sqrt(jnp.float32(lax.axis_size("dp") * tokens_all))
    proj_summed = permute_psum(proj_local.astype(jnp.bfloat16), ("dp", "seq")).astype(jnp.float32)
    proj_grad = proj_summed * token_scale
    half = tokens_here // 2
    grad_blocks = [
        lax.dot_general(
            proj_weight, err_part, (((1,), (1,)), ((), ())), preferred_element_type=jnp.float32
        ).astype(jnp.bfloat16)
        for err_part in (err_grad[:half], err_grad[half:])
    ]
    pooled_grad_t = jnp.concatenate(
        [
            lax.psum_scatter(grad_blocks[0], "tensor", scatter_dimension=0, tiled=True),
            tensor_scatter(grad_blocks[1], "tensor", ring).astype(jnp.bfloat16),
        ],
        axis=1,
    )
    weight_part = local_weight
    down_sum = lax.dot_general(
        weight_part,
        lax.all_gather(pooled_grad_t, "seq", axis=1, tiled=True),
        (((0,), (1,)), ((), ())),
        preferred_element_type=jnp.float32,
    )
    down_grad = down_sum.astype(jnp.bfloat16).reshape(positions, groups_here, group_width)
    conv_local = jnp.einsum(
        "pkgc,pgo->gkco", windows, down_grad, preferred_element_type=jnp.float32
    )
    conv_flat = conv_local.astype(jnp.bfloat16).reshape(KERNEL * groups_here * group_width, group_width)
    conv_summed = (
        exchange_psum(conv_flat, ("seq", "dp"))
        .reshape(conv_local.shape)
        .astype(jnp.float32)
    )
    position_scale = 1.0 / jnp.sqrt(jnp.float32(lax.axis_size("dp") * positions * seq_count))
    conv_grad = (conv_summed * position_scale).reshape(
        groups_here, KERNEL * group_width, group_width
    )
    window_grad = jnp.einsum(
        "pgo,gkco->pkgc", down_grad, taps_weight, preferred_element_type=jnp.float32
    )
    incoming = shifted(window_grad[-1, STRIDE:], "seq", 1)
    carried_grad = jnp.concatenate([incoming[None], window_grad[:-1, STRIDE:]], axis=0)
    byte_grad = (
        (window_grad[:, :STRIDE] + carried_grad).reshape(row_total, width).astype(jnp.bfloat16)
    )
    return (downsampled[None], byte_grad[None], conv_grad, proj_grad)


def solution(mesh):
    return jax.shard_map(
        local,
        mesh=mesh,
        in_specs=(
            P("dp", "seq", "tensor"),
            P("tensor", None, None),
            P("tensor"),
            P(None, "tensor"),
            P("dp", "seq", "tensor"),
            P("dp", None),
        ),
        out_specs=(
            P("dp", "seq", "tensor"),
            P("dp", "seq", "tensor"),
            P("tensor", None, None),
            P(None, "tensor"),
        ),
        check_vma=False,
    )
```

```python
import jax
import jax.numpy as jnp
from jax import lax
from jax.sharding import PartitionSpec as P

STRIDE = 4
KERNEL = 8
TENSOR_RING = 8


def shifted(block, axis, distance):
    devices = range(lax.axis_size(axis))
    route = [(i - distance, i) for i in devices if i - distance in devices]
    return lax.ppermute(block, axis, route)


def shard_sum(block, axis):
    count = lax.axis_size(axis)
    rank = lax.axis_index(axis)
    pieces = block.reshape((count, block.shape[0] // count) + block.shape[1:])
    total = lax.dynamic_index_in_dim(pieces, rank, 0, keepdims=False).astype(jnp.float32)
    for distance in range(1, count):
        route = [(i, (i + distance) % count) for i in range(count)]
        outgoing = lax.dynamic_index_in_dim(pieces, (rank + distance) % count, 0, keepdims=False)
        total = total + lax.ppermute(outgoing, axis, route).astype(jnp.float32)
    return total


def shard_gather(piece, axis):
    count = lax.axis_size(axis)
    rank = lax.axis_index(axis)
    rows = piece.shape[0]
    gathered = jnp.zeros((count * rows,) + piece.shape[1:], piece.dtype)
    gathered = lax.dynamic_update_slice_in_dim(gathered, piece, rank * rows, 0)
    for distance in range(1, count):
        route = [(i, (i + distance) % count) for i in range(count)]
        incoming = lax.ppermute(piece, axis, route)
        source = (rank + count - distance) % count
        gathered = lax.dynamic_update_slice_in_dim(gathered, incoming, source * rows, 0)
    return gathered


def exchange_psum(block, axes):
    summed = block
    for axis in axes:
        count = lax.axis_size(axis)
        rank = lax.axis_index(axis)
        slots = jnp.zeros((count,) + block.shape, block.dtype)
        slots = lax.dynamic_update_index_in_dim(slots, summed, rank, 0)
        for distance in range(1, count):
            route = [(i, (i + distance) % count) for i in range(count)]
            incoming = lax.ppermute(summed, axis, route)
            slots = lax.dynamic_update_index_in_dim(slots, incoming, (rank + count - distance) % count, 0)
        summed = jnp.sum(slots.astype(jnp.float32), axis=0).astype(block.dtype)
    return summed


def permute_psum(block, axes):
    summed = block
    for axis in axes:
        summed = shard_sum(summed, axis).astype(block.dtype)
    for axis in axes[::-1]:
        summed = shard_gather(summed, axis)
    return summed


def ring_routes(count, ring):
    def device(pair, place):
        return pair * ring + place % ring
    pairs = count // ring
    plus = [(device(a, b), device(a, b + 1)) for a in range(pairs) for b in range(ring)]
    minus = [(device(a, b), device(a, b - 1)) for a in range(pairs) for b in range(ring)]
    across = [(i, (i + ring) % count) for i in range(count)]
    return plus, minus, across


def tensor_gather(piece, axis, ring):
    count = lax.axis_size(axis)
    rank = lax.axis_index(axis)
    pair_index = rank // ring
    place = rank % ring
    plus, minus, across = ring_routes(count, ring)
    other = lax.ppermute(piece, axis, across)
    pair = jnp.where(pair_index == 0, jnp.stack([piece, other]), jnp.stack([other, piece]))
    slots = jnp.zeros((ring,) + pair.shape, pair.dtype)
    slots = lax.dynamic_update_index_in_dim(slots, pair, place, 0)
    forward = pair
    backward = pair
    full_steps = (ring - 1) // 2
    for step in range(1, full_steps + 1):
        forward = lax.ppermute(forward, axis, plus)
        slots = lax.dynamic_update_index_in_dim(slots, forward, (place + ring - step) % ring, 0)
        backward = lax.ppermute(backward, axis, minus)
        slots = lax.dynamic_update_index_in_dim(slots, backward, (place + step) % ring, 0)
    if ring % 2 == 0:
        rows_half = pair.shape[1] // 2
        far = (place + ring // 2) % ring
        front = lax.ppermute(forward[:, :rows_half], axis, plus)
        back = lax.ppermute(backward[:, rows_half:], axis, minus)
        slots = lax.dynamic_update_index_in_dim(
            slots, jnp.concatenate([front, back], axis=1), far, 0
        )
    rows, width = piece.shape
    return slots.transpose(2, 1, 0, 3).reshape(rows, count * width)


def tensor_scatter(block, axis, ring):
    count = lax.axis_size(axis)
    rank = lax.axis_index(axis)
    pair_index = rank // ring
    place = rank % ring
    plus, minus, across = ring_routes(count, ring)
    view = block.reshape((count // ring, ring, block.shape[0] // count) + block.shape[1:])

    def own(target):
        return lax.dynamic_index_in_dim(view, target % ring, 1, keepdims=False).astype(jnp.float32)

    plus_steps = ring // 2
    minus_steps = ring - 1 - plus_steps
    total = own(place)
    outgoing = own(place + plus_steps).astype(block.dtype)
    for step in range(1, plus_steps + 1):
        incoming = lax.ppermute(outgoing, axis, plus).astype(jnp.float32)
        if step < plus_steps:
            outgoing = (incoming + own(place + plus_steps - step)).astype(block.dtype)
        else:
            total = total + incoming
    outgoing = own(place + ring - minus_steps).astype(block.dtype)
    for step in range(1, minus_steps + 1):
        incoming = lax.ppermute(outgoing, axis, minus).astype(jnp.float32)
        if step < minus_steps:
            outgoing = (incoming + own(place + ring - minus_steps + step)).astype(block.dtype)
        else:
            total = total + incoming
    sent = lax.dynamic_index_in_dim(total, 1 - pair_index, 0, keepdims=False)
    kept = lax.dynamic_index_in_dim(total, pair_index, 0, keepdims=False)
    return kept + lax.ppermute(sent.astype(block.dtype), axis, across).astype(jnp.float32)


def intersection_weights(span_start, span_end, span_lengths, first_position, position_count):
    byte_first = (first_position + jnp.arange(position_count, dtype=jnp.int32)) * STRIDE
    lower_edge = jnp.maximum(span_start[:, None], byte_first[None, :])
    upper_edge = jnp.minimum(span_end[:, None], byte_first[None, :] + STRIDE)
    covered = jnp.maximum(upper_edge - lower_edge, 0).astype(jnp.float32)
    return (covered / span_lengths[:, None].astype(jnp.float32)).astype(jnp.bfloat16)


def local(byte_acts, conv_weight, conv_bias, proj_weight, teacher, span_lengths):
    byte_rows = byte_acts[0]
    row_total, width = byte_rows.shape
    groups_here = conv_weight.shape[0]
    group_width = width // groups_here
    positions = row_total // STRIDE
    seq_count = lax.axis_size("seq")
    seq_rank = lax.axis_index("seq")
    lengths_doc = span_lengths[0]
    tokens_all = lengths_doc.shape[0]
    span_end = jnp.cumsum(lengths_doc)
    span_start = span_end - lengths_doc
    next_rows = shifted(byte_rows[:STRIDE], "seq", -1)
    extended = jnp.concatenate([byte_rows, next_rows], axis=0)
    blocks = extended.reshape(positions + 1, STRIDE, groups_here, group_width)
    windows = jnp.concatenate([blocks[:-1], blocks[1:]], axis=1)
    taps_weight = conv_weight.reshape(groups_here, KERNEL, group_width, group_width)
    conv_out = jnp.einsum(
        "pkgc,gkco->pgo", windows, taps_weight, preferred_element_type=jnp.float32
    )
    conv_out = conv_out + conv_bias.reshape(groups_here, group_width)[None]
    downsampled = conv_out.reshape(positions, width).astype(jnp.bfloat16)
    local_weight = intersection_weights(
        span_start, span_end, lengths_doc, seq_rank * positions, positions
    )
    tokens_here = tokens_all // seq_count
    own_start = lax.dynamic_slice_in_dim(span_start, seq_rank * tokens_here, tokens_here)
    own_end = lax.dynamic_slice_in_dim(span_end, seq_rank * tokens_here, tokens_here)
    own_lengths = lax.dynamic_slice_in_dim(lengths_doc, seq_rank * tokens_here, tokens_here)
    token_weight = intersection_weights(own_start, own_end, own_lengths, 0, positions * seq_count)
    down_all = shard_gather(downsampled, "seq")
    pooled_sum = jnp.dot(token_weight, down_all, preferred_element_type=jnp.float32).astype(
        jnp.bfloat16
    )
    ring = TENSOR_RING
    gathered = tensor_gather(pooled_sum, "tensor", ring)
    predicted = jnp.dot(gathered, proj_weight, preferred_element_type=jnp.float32)
    err_grad = (predicted - teacher[0].astype(jnp.float32)).astype(jnp.bfloat16)
    proj_local = lax.dot_general(
        gathered, err_grad, (((0,), (0,)), ((), ())), preferred_element_type=jnp.float32
    )
    token_scale = 1.0 / jnp.sqrt(jnp.float32(lax.axis_size("dp") * tokens_all))
    proj_summed = permute_psum(proj_local.astype(jnp.bfloat16), ("dp", "seq")).astype(jnp.float32)
    proj_grad = proj_summed * token_scale
    half = tokens_here * 7 // 16
    grad_blocks = [
        lax.dot_general(
            proj_weight, err_part, (((1,), (1,)), ((), ())), preferred_element_type=jnp.float32
        ).astype(jnp.bfloat16)
        for err_part in (err_grad[:half], err_grad[half:])
    ]
    pooled_grad_t = jnp.concatenate(
        [
            lax.psum_scatter(grad_blocks[0], "tensor", scatter_dimension=0, tiled=True),
            tensor_scatter(grad_blocks[1], "tensor", ring).astype(jnp.bfloat16),
        ],
        axis=1,
    )
    weight_part = local_weight
    down_sum = lax.dot_general(
        weight_part,
        lax.all_gather(pooled_grad_t, "seq", axis=1, tiled=True),
        (((0,), (1,)), ((), ())),
        preferred_element_type=jnp.float32,
    )
    down_grad = down_sum.astype(jnp.bfloat16).reshape(positions, groups_here, group_width)
    conv_local = jnp.einsum(
        "pkgc,pgo->gkco", windows, down_grad, preferred_element_type=jnp.float32
    )
    conv_flat = conv_local.astype(jnp.bfloat16).reshape(KERNEL * groups_here * group_width, group_width)
    conv_summed = (
        exchange_psum(conv_flat, ("dp", "seq"))
        .reshape(conv_local.shape)
        .astype(jnp.float32)
    )
    position_scale = 1.0 / jnp.sqrt(jnp.float32(lax.axis_size("dp") * positions * seq_count))
    conv_grad = (conv_summed * position_scale).reshape(
        groups_here, KERNEL * group_width, group_width
    )
    window_grad = jnp.einsum(
        "pgo,gkco->pkgc", down_grad, taps_weight, preferred_element_type=jnp.float32
    )
    incoming = shifted(window_grad[-1, STRIDE:], "seq", 1)
    carried_grad = jnp.concatenate([incoming[None], window_grad[:-1, STRIDE:]], axis=0)
    byte_grad = (
        (window_grad[:, :STRIDE] + carried_grad).reshape(row_total, width).astype(jnp.bfloat16)
    )
    return (downsampled[None], byte_grad[None], conv_grad, proj_grad)


def solution(mesh):
    return jax.shard_map(
        local,
        mesh=mesh,
        in_specs=(
            P("dp", "seq", "tensor"),
            P("tensor", None, None),
            P("tensor"),
            P(None, "tensor"),
            P("dp", "seq", "tensor"),
            P("dp", None),
        ),
        out_specs=(
            P("dp", "seq", "tensor"),
            P("dp", "seq", "tensor"),
            P("tensor", None, None),
            P(None, "tensor"),
        ),
        check_vma=False,
    )
```
